256 devices in a mesh: req: 32 (over z, y), tp: 8 (over x, core).
Axes of the slice: x: 4, y: 4, z: 8, core: 2. Of those that a mesh axis runs over, the one named last changes fastest.
Arguments:
- queries: bfloat16 [16384, 7168], P('req', 'tp')
- keys_new: bfloat16 [16384, 7168], P('req', 'tp')
- values_new: bfloat16 [16384, 7168], P('req', 'tp'), may hold values from -6 to 6
- cache_keys: bfloat16 [64, 1024, 7168], P('req', None, 'tp'), may hold values from -6 to 6
- cache_values: bfloat16 [64, 1024, 7168], P('req', None, 'tp'), may hold values from -6 to 6
- out_proj: bfloat16 [7168, 3584], P('tp'), may hold values from -0.0625 to 0.0625
- req_lengths: int32 [32, 4], P('req'), may hold values from 1 to 415, as said below
- cache_owner: int32 [32, 2], P('req'), may hold values from 0 to 31, as said below
- cache_slot: int32 [32, 2], P('req'), may hold values from 0 to 1
- prior_len: int32 [32, 2], P('req'), may hold values from 1 to 1024, as said below
Outputs:
- mixed: bfloat16 [16384, 3584], P(('req', 'tp'))
- new_keys: bfloat16 [64, 192, 7168], P('req', None, 'tp')
- new_values: bfloat16 [64, 192, 7168], P('req', None, 'tp')
The draws below stay inside these ranges and needn't reach their ends.
Inputs may be any that keep to these rules, and one draw needn't show every extreme that they name: `req_lengths`: each row sums to 512; each continuing request has at most 192 new tokens, and some continuing request has exactly 192; continuing requests have at least 48 new tokens; some request has exactly 415. `cache_owner`: A continuing request's owner is the req index just before or just after its own, counted around the axis (index 0 follows index 31); the two continuing requests of one index have different owners; every cache slot of every index is used by exactly one continuing request. `prior_len`: some continuing request has exactly 1024 prior tokens.
All inputs are finite; a program needn't handle non-finite values.
Results may differ from the reference program's by a relative error of at most 0.014.
Values may be sent and summed in bfloat16 or wider, within the bound.
No kernel may reach another device: no remote copies, remote signals or barrier semaphores. Data moves between devices by JAX's collectives and lax.ppermute only.
A program may use at most 128 MiB of HBM per device.

```python
import math
import jax
import jax.numpy as jnp
from jax import lax

D = 3584
HEADS = 32
HD = 224
ATT = 7168
T_DEV = 512
SLOTS = 2
NEWCAP = 192
PMAX = 1024
TOKENS = 16384
N_REQ = 32


def shared_query_key(key):
    key_base = jax.random.normal(jax.random.fold_in(key, 11), (TOKENS, HEADS * HD), jnp.float32)
    query_out = jax.random.normal(jax.random.fold_in(key, 12), (TOKENS, HEADS * HD), jnp.float32)
    keys_out = key_base
    return (query_out, keys_out)


def draw_queries(key, part):
    return shared_query_key(key)[0].astype(jnp.bfloat16)


def draw_keys_new(key, part):
    return shared_query_key(key)[1].astype(jnp.bfloat16)


def draw_req_lengths(key, part):
    continuing = jax.random.randint(jax.random.fold_in(key, 31), (N_REQ, SLOTS), NEWCAP // 4, NEWCAP + 1)
    chosen_device = jax.random.randint(jax.random.fold_in(key, 32), (), 0, N_REQ)
    chosen_slot = jax.random.randint(jax.random.fold_in(key, 33), (), 0, SLOTS)
    longest_device = (chosen_device + 1) % N_REQ
    grid_rows = jnp.arange(N_REQ)[:, None]
    grid_cols = jnp.arange(SLOTS)[None, :]
    continuing = jnp.where((grid_rows == chosen_device) & (grid_cols == chosen_slot), NEWCAP, continuing)
    continuing = jnp.where(grid_rows == longest_device, NEWCAP // 4, continuing)
    remaining = T_DEV - jnp.sum(continuing, axis=1)
    first_part = jax.random.randint(jax.random.fold_in(key, 34), (N_REQ,), 1, remaining)
    first_part = jnp.where(jnp.arange(N_REQ) == longest_device, remaining - 1, first_part)
    second_part = remaining - first_part
    return jnp.concatenate([continuing, first_part[:, None], second_part[:, None]], axis=1).astype(jnp.int32)


def owner_and_slot(key):
    device = jnp.arange(N_REQ)
    right_first = jax.random.randint(jax.random.fold_in(key, 41), (N_REQ,), 0, 2)
    owner_bit = jax.random.randint(jax.random.fold_in(key, 43), (N_REQ,), 0, 2)
    right_owner = (device + 1) % N_REQ
    left_owner = (device + N_REQ - 1) % N_REQ
    right_slot = owner_bit[right_owner]
    left_slot = 1 - owner_bit[left_owner]
    owner_first = jnp.where(right_first == 1, right_owner, left_owner)
    owner_second = jnp.where(right_first == 1, left_owner, right_owner)
    slot_first = jnp.where(right_first == 1, right_slot, left_slot)
    slot_second = jnp.where(right_first == 1, left_slot, right_slot)
    owners = jnp.stack([owner_first, owner_second], axis=1).astype(jnp.int32)
    slot_numbers = jnp.stack([slot_first, slot_second], axis=1).astype(jnp.int32)
    return (owners, slot_numbers)


def draw_cache_owner(key, part):
    return owner_and_slot(key)[0]


def draw_cache_slot(key, part):
    return owner_and_slot(key)[1]


def draw_prior_len(key, part):
    drawn = jax.random.randint(jax.random.fold_in(key, 51), (N_REQ, SLOTS), 1, PMAX + 1)
    chosen_device = jax.random.randint(jax.random.fold_in(key, 52), (), 0, N_REQ)
    chosen_slot = jax.random.randint(jax.random.fold_in(key, 53), (), 0, SLOTS)
    grid_rows = jnp.arange(N_REQ)[:, None]
    grid_cols = jnp.arange(SLOTS)[None, :]
    return jnp.where((grid_rows == chosen_device) & (grid_cols == chosen_slot), PMAX, drawn).astype(jnp.int32)


def level_of(stream_key, shape, split, smallest, top_value):
    level, own = 1.0, jax.random.fold_in(stream_key, 6)
    for position, shards_of in split:
        heights = jnp.exp(jax.random.uniform(jax.random.fold_in(own, position), (shards_of,), jnp.float32, smallest / len(split), top_value / len(split)))
        level = level * jnp.repeat(heights, shape[position] // shards_of).reshape([-1 if axis == position else 1 for axis in range(len(shape))])
    return level


def bell_draw(own_key, dims, spread, bound, split=(), kind=jnp.bfloat16):
    values = jax.random.normal(own_key, dims, jnp.float32) * spread
    if len(split) > 0:
        values = level_of(own_key, dims, split, -0.22, 0.18) * values
    return jnp.clip(values, min=-bound, max=bound).astype(kind)


def setup_inputs(seed: int = 0) -> dict:
    arg_keys = jax.random.split(jax.random.key(seed), 11)
    queries = draw_queries(jax.random.fold_in(arg_keys[10], 71), 0)
    keys_new = draw_keys_new(jax.random.fold_in(arg_keys[10], 71), 0)
    values_new = bell_draw(arg_keys[2], (TOKENS, ATT), 1.0, 6.0, ((0, 32), (1, 8)))
    cache_keys = bell_draw(arg_keys[3], (N_REQ * SLOTS, PMAX, ATT), 1.0, 6.0, ((0, 32), (2, 8)))
    cache_values = bell_draw(arg_keys[4], (N_REQ * SLOTS, PMAX, ATT), 1.0, 6.0, ((0, 32), (2, 8)))
    out_proj = bell_draw(arg_keys[5], (ATT, D), ATT ** -0.5, 0.0625, ((0, 8),))
    req_lengths = draw_req_lengths(jax.random.fold_in(arg_keys[10], 71), 0)
    cache_owner = draw_cache_owner(jax.random.fold_in(arg_keys[10], 71), 0)
    cache_slot = draw_cache_slot(jax.random.fold_in(arg_keys[10], 71), 0)
    prior_len = draw_prior_len(jax.random.fold_in(arg_keys[10], 71), 0)
    return dict(queries=queries, keys_new=keys_new, values_new=values_new, cache_keys=cache_keys, cache_values=cache_values, out_proj=out_proj, req_lengths=req_lengths, cache_owner=cache_owner, cache_slot=cache_slot, prior_len=prior_len)


def reference(queries, keys_new, values_new, cache_keys, cache_values, out_proj, req_lengths, cache_owner, cache_slot, prior_len):
    score_scale = 1.0 / math.sqrt(HD)
    positions = jnp.arange(T_DEV, dtype=jnp.int32)
    row_marks = jnp.arange(NEWCAP, dtype=jnp.int32)
    slot_of = jnp.repeat(jnp.arange(SLOTS, dtype=jnp.int32), PMAX)
    row_in_slot = jnp.tile(jnp.arange(PMAX, dtype=jnp.int32), SLOTS)

    def one_block(b):
        req_lens = req_lengths[b]
        req_ends = jnp.cumsum(req_lens).astype(jnp.int32)
        starts = (req_ends - req_lens).astype(jnp.int32)
        segment = lax.optimization_barrier(jnp.sum((positions[:, None] >= req_ends[None, :]).astype(jnp.int32), axis=1))
        first_row = (b * T_DEV).astype(jnp.int32)
        query_block = lax.dynamic_slice_in_dim(queries, first_row, T_DEV, 0)
        key_block = lax.dynamic_slice_in_dim(keys_new, first_row, T_DEV, 0)
        value_block = lax.dynamic_slice_in_dim(values_new, first_row, T_DEV, 0)
        query_heads = query_block.astype(jnp.float32).reshape(T_DEV, HEADS, HD)
        key_heads = key_block.astype(jnp.float32).reshape(T_DEV, HEADS, HD)
        value_heads = value_block.astype(jnp.float32).reshape(T_DEV, HEADS, HD)
        slot_index = (cache_owner[b] * SLOTS + cache_slot[b]).astype(jnp.int32)
        prior_keys = cache_keys[slot_index].astype(jnp.float32).reshape(SLOTS * PMAX, HEADS, HD)
        prior_values = cache_values[slot_index].astype(jnp.float32).reshape(SLOTS * PMAX, HEADS, HD)
        own_scores = jnp.einsum('thd,shd->hts', query_heads, key_heads) * score_scale
        own_live = (segment[:, None] == segment[None, :]) & (positions[None, :] <= positions[:, None])
        prior_scores = jnp.einsum('thd,shd->hts', query_heads, prior_keys) * score_scale
        prior_limit = prior_len[b][slot_of]
        prior_live = (segment[:, None] == slot_of[None, :]) & (row_in_slot < prior_limit)[None, :]
        live_mask = jnp.concatenate([own_live, prior_live], axis=1)
        scores = jnp.concatenate([own_scores, prior_scores], axis=2)
        scores = jnp.where(live_mask[None], scores, -1e+30)
        row_top = lax.optimization_barrier(jnp.max(scores, axis=2, keepdims=True))
        weights = jnp.where(live_mask[None], jnp.exp(scores - row_top), 0.0)
        row_total = lax.optimization_barrier(jnp.sum(weights, axis=2))
        rounded = lax.optimization_barrier(weights.astype(jnp.bfloat16)).astype(jnp.float32)
        all_values = jnp.concatenate([value_heads, prior_values], axis=0)
        numerator = jnp.einsum('hts,shd->thd', rounded, all_values)
        attended = (numerator / row_total.T[:, :, None]).reshape(T_DEV, ATT).astype(jnp.bfloat16)
        mixed = jnp.dot(attended, out_proj, preferred_element_type=jnp.float32).astype(jnp.bfloat16)
        padded_keys = jnp.pad(key_block, ((0, NEWCAP), (0, 0)))
        padded_values = jnp.pad(value_block, ((0, NEWCAP), (0, 0)))
        key_rows = []
        value_rows = []
        for j in range(SLOTS):
            keep = (row_marks < req_lens[j])[:, None]
            key_rows.append(jnp.where(keep, lax.dynamic_slice_in_dim(padded_keys, starts[j], NEWCAP, 0), jnp.zeros((), jnp.bfloat16)))
            value_rows.append(jnp.where(keep, lax.dynamic_slice_in_dim(padded_values, starts[j], NEWCAP, 0), jnp.zeros((), jnp.bfloat16)))
        return (mixed, jnp.stack(key_rows), jnp.stack(value_rows), slot_index)
    mixed, key_rows, value_rows, slot_index = lax.map(one_block, jnp.arange(N_REQ, dtype=jnp.int32))
    flat_index = slot_index.reshape(-1)
    new_keys = jnp.zeros((N_REQ * SLOTS, NEWCAP, ATT), jnp.bfloat16).at[flat_index].set(key_rows.reshape(N_REQ * SLOTS, NEWCAP, ATT))
    new_values = jnp.zeros((N_REQ * SLOTS, NEWCAP, ATT), jnp.bfloat16).at[flat_index].set(value_rows.reshape(N_REQ * SLOTS, NEWCAP, ATT))
    return (mixed.reshape(TOKENS, D), new_keys, new_values)
```

```python
import math

import jax
import jax.numpy as jnp
from jax import lax
from jax.sharding import PartitionSpec as P

HD = 224
NEWCAP = 192


floor_value = -1e30


def shifted(value, axis, steps):
    count = lax.axis_size(axis)
    pairs = [(source, (source + steps) % count) for source in range(count)]
    return lax.ppermute(value, axis, pairs)


def attend_part(query_rows, key_rows, value_rows, live_mask, head_count):
    row_count = query_rows.shape[0]
    key_count = key_rows.shape[0]
    query_heads = query_rows.reshape(row_count, head_count, HD)
    key_heads = key_rows.reshape(key_count, head_count, HD)
    value_heads = value_rows.reshape(key_count, head_count, HD)
    scores = jnp.einsum(
        "thd,shd->hts", query_heads, key_heads, preferred_element_type=jnp.float32
    ) * (1.0 / math.sqrt(HD))
    scores = jnp.where(live_mask[None], scores, floor_value)
    row_top = jnp.max(scores, axis=2)
    weights = jnp.where(live_mask[None], jnp.exp(scores - row_top[:, :, None]), 0.0)
    row_total = jnp.sum(weights, axis=2)
    numerator = jnp.einsum(
        "hts,shd->thd",
        weights.astype(jnp.bfloat16),
        value_heads,
        preferred_element_type=jnp.float32,
    )
    return (numerator.reshape(row_count, head_count * HD), row_top.T, row_total.T)


def body(
    queries,
    keys_new,
    values_new,
    cache_keys,
    cache_values,
    out_proj,
    req_lengths,
    cache_owner,
    cache_slot,
    prior_len,
):
    tok_count = queries.shape[0]
    feat_width = queries.shape[1]
    head_count = feat_width // HD
    slot_count = cache_keys.shape[0]
    prior_rows = cache_keys.shape[1]
    req_lens = req_lengths[0]
    req_ends = jnp.cumsum(req_lens)
    starts = req_ends - req_lens
    positions = jnp.arange(tok_count, dtype=jnp.int32)
    row_marks = jnp.arange(NEWCAP, dtype=jnp.int32)
    prior_marks = jnp.arange(prior_rows, dtype=jnp.int32)
    req_count = lax.axis_size("req")
    req_index = lax.axis_index("req")
    raw_offset = (cache_owner[0] - req_index + req_count) % req_count
    offset = jnp.where(raw_offset == req_count - 1, -1, raw_offset)

    def request_at(distance):
        pick = offset[0] == distance
        start = jnp.where(pick, starts[0], starts[1])
        length = jnp.where(pick, req_lens[0], req_lens[1])
        slot = jnp.where(pick, cache_slot[0, 0], cache_slot[0, 1])
        prior = jnp.where(pick, prior_len[0, 0], prior_len[0, 1])
        return start, length, jnp.stack([slot, prior, length])

    def rows_of(source, start):
        return lax.dynamic_slice_in_dim(source, start, NEWCAP, 0)

    right_start, right_len, right_tag = request_at(1)
    left_start, left_len, left_tag = request_at(-1)

    from_left_q, from_left_tag = shifted(
        (rows_of(queries, right_start), right_tag), "req", 1
    )
    from_right_q, from_right_tag = shifted(
        (rows_of(queries, left_start), left_tag), "req", -1
    )

    segment = jnp.sum((positions[:, None] >= req_ends[None, :]).astype(jnp.int32), axis=1)
    own_live = (segment[:, None] == segment[None, :]) & (positions[None, :] <= positions[:, None])
    own_numer, own_top, own_total = attend_part(queries, keys_new, values_new, own_live, head_count)

    def serve(query_rows, tag):
        keys = lax.dynamic_index_in_dim(cache_keys, tag[0], 0, keepdims=False)
        values = lax.dynamic_index_in_dim(cache_values, tag[0], 0, keepdims=False)
        live_mask = jnp.broadcast_to(prior_marks[None, :] < tag[1], (NEWCAP, prior_rows))
        return attend_part(query_rows, keys, values, live_mask, head_count)

    got_right = shifted(serve(from_left_q, from_left_tag), "req", -1)
    got_left = shifted(serve(from_right_q, from_right_tag), "req", 1)

    def masked_rows(source, start, length):
        keep = (row_marks < length)[:, None]
        return jnp.where(keep, rows_of(source, start), jnp.zeros((), jnp.bfloat16))

    right_kv = (
        masked_rows(keys_new, right_start, right_len),
        masked_rows(values_new, right_start, right_len),
    )
    left_kv = (
        masked_rows(keys_new, left_start, left_len),
        masked_rows(values_new, left_start, left_len),
    )
    right_kv, left_kv, got_right, got_left = lax.optimization_barrier(
        (right_kv, left_kv, got_right, got_left)
    )
    from_left_kv = shifted(right_kv, "req", 1)
    from_right_kv = shifted(left_kv, "req", -1)

    def place(result, start, length):
        numer, top, total = result
        shift = tok_count - start
        keep = ((positions - start >= 0) & (positions - start < length))[:, None]

        def moved(x):
            padded = jnp.pad(x, ((tok_count, tok_count - NEWCAP), (0, 0)))
            return lax.dynamic_slice_in_dim(padded, shift, tok_count, 0)

        return keep, moved(numer), moved(top), moved(total)

    keep_r, numer_r, top_r, total_r = place(got_right, right_start, right_len)
    keep_l, numer_l, top_l, total_l = place(got_left, left_start, left_len)
    prior_numer = jnp.where(keep_r, numer_r, jnp.where(keep_l, numer_l, 0.0))
    prior_top = jnp.where(keep_r, top_r, jnp.where(keep_l, top_l, floor_value))
    prior_total = jnp.where(keep_r, total_r, jnp.where(keep_l, total_l, 0.0))

    both_top = jnp.maximum(own_top, prior_top)
    own_scale = jnp.exp(own_top - both_top)
    prior_scale = jnp.exp(prior_top - both_top)
    denominator = own_total * own_scale + prior_total * prior_scale
    numerator = (
        own_numer.reshape(tok_count, head_count, HD) * own_scale[:, :, None]
        + prior_numer.reshape(tok_count, head_count, HD) * prior_scale[:, :, None]
    )
    attended = (
        (numerator / denominator[:, :, None]).reshape(tok_count, feat_width).astype(jnp.bfloat16)
    )
    mixed = lax.psum_scatter(
        jnp.dot(attended, out_proj, preferred_element_type=jnp.float32).astype(jnp.bfloat16),
        "tp",
        scatter_dimension=0,
        tiled=True,
    )

    slot_ids = jnp.arange(slot_count, dtype=jnp.int32)

    def stored(from_left_rows, from_right_rows):
        at_left = (slot_ids == from_left_tag[0])[:, None, None]
        at_right = (slot_ids == from_right_tag[0])[:, None, None]
        return jnp.where(
            at_left,
            from_left_rows[None],
            jnp.where(at_right, from_right_rows[None], jnp.zeros((), jnp.bfloat16)),
        )

    new_keys = stored(from_left_kv[0], from_right_kv[0])
    new_values = stored(from_left_kv[1], from_right_kv[1])
    return (mixed, new_keys, new_values)


def solution(mesh):
    in_specs = (
        P("req", "tp"),
        P("req", "tp"),
        P("req", "tp"),
        P("req", None, "tp"),
        P("req", None, "tp"),
        P("tp", None),
        P("req", None),
        P("req", None),
        P("req", None),
        P("req", None),
    )
    out_specs = (P(("req", "tp"), None), P("req", None, "tp"), P("req", None, "tp"))
    return jax.shard_map(body, mesh=mesh, in_specs=in_specs, out_specs=out_specs, check_vma=False)
```

```python
import math

import jax
import jax.numpy as jnp
from jax import lax
from jax.sharding import PartitionSpec as P

HD = 224
NEWCAP = 192


floor_value = -1e30
TAG_ROWS = 8
RESULT_WIDTH = 1024


def shifted(value, axis, steps):
    count = lax.axis_size(axis)
    pairs = [(source, (source + steps) % count) for source in range(count)]
    return lax.ppermute(value, axis, pairs)


def attend_part(query_rows, key_rows, value_rows, live_mask, head_count):
    row_count = query_rows.shape[0]
    key_count = key_rows.shape[0]
    query_heads = query_rows.reshape(row_count, head_count, HD)
    key_heads = key_rows.reshape(key_count, head_count, HD)
    value_heads = value_rows.reshape(key_count, head_count, HD)
    scores = jnp.einsum(
        "thd,shd->hts", query_heads, key_heads, preferred_element_type=jnp.float32
    ) * (1.0 / math.sqrt(HD))
    scores = jnp.where(live_mask[None], scores, floor_value)
    row_top = jnp.max(scores, axis=2)
    weights = jnp.where(live_mask[None], jnp.exp(scores - row_top[:, :, None]), 0.0)
    row_total = jnp.sum(weights, axis=2)
    numerator = jnp.einsum(
        "hts,shd->thd",
        weights.astype(jnp.bfloat16),
        value_heads,
        preferred_element_type=jnp.float32,
    )
    return (numerator.reshape(row_count, head_count * HD), row_top.T, row_total.T)


def body(
    queries,
    keys_new,
    values_new,
    cache_keys,
    cache_values,
    out_proj,
    req_lengths,
    cache_owner,
    cache_slot,
    prior_len,
):
    tok_count = queries.shape[0]
    feat_width = queries.shape[1]
    head_count = feat_width // HD
    slot_count = cache_keys.shape[0]
    prior_rows = cache_keys.shape[1]
    req_lens = req_lengths[0]
    req_ends = jnp.cumsum(req_lens)
    starts = req_ends - req_lens
    positions = jnp.arange(tok_count, dtype=jnp.int32)
    row_marks = jnp.arange(NEWCAP, dtype=jnp.int32)
    prior_marks = jnp.arange(prior_rows, dtype=jnp.int32)
    req_count = lax.axis_size("req")
    req_index = lax.axis_index("req")
    raw_offset = (cache_owner[0] - req_index + req_count) % req_count
    offset = jnp.where(raw_offset == req_count - 1, -1, raw_offset)

    def request_at(distance):
        pick = offset[0] == distance
        start = jnp.where(pick, starts[0], starts[1])
        length = jnp.where(pick, req_lens[0], req_lens[1])
        slot = jnp.where(pick, cache_slot[0, 0], cache_slot[0, 1])
        prior = jnp.where(pick, prior_len[0, 0], prior_len[0, 1])
        return start, length, slot, prior

    def rows_of(source, start):
        return lax.dynamic_slice_in_dim(source, start, NEWCAP, 0)

    def query_bundle(start, length, slot, prior):
        tag = jnp.stack([slot, prior // 32, prior % 32, length]).astype(jnp.bfloat16)
        tag_rows = jnp.zeros((TAG_ROWS, feat_width), jnp.bfloat16).at[0, :4].set(tag)
        return jnp.concatenate([rows_of(queries, start), tag_rows], axis=0)

    def read_tag(bundle):
        tag = bundle[NEWCAP, :4].astype(jnp.float32).astype(jnp.int32)
        return tag[0], tag[1] * 32 + tag[2], tag[3]

    right_start, right_len, right_slot, right_prior = request_at(1)
    left_start, left_len, left_slot, left_prior = request_at(-1)

    from_left = shifted(query_bundle(right_start, right_len, right_slot, right_prior), "req", 1)
    from_right = shifted(query_bundle(left_start, left_len, left_slot, left_prior), "req", -1)

    segment = jnp.sum((positions[:, None] >= req_ends[None, :]).astype(jnp.int32), axis=1)
    own_live = (segment[:, None] == segment[None, :]) & (positions[None, :] <= positions[:, None])
    own_numer, own_top, own_total = attend_part(queries, keys_new, values_new, own_live, head_count)

    left_tag = read_tag(from_left)
    right_tag = read_tag(from_right)
    left_is_zero = left_tag[0] == 0
    served = []
    for s in range(slot_count):
        mine = left_is_zero if s == 0 else jnp.logical_not(left_is_zero)
        query_rows = jnp.where(mine, from_left[:NEWCAP], from_right[:NEWCAP])
        prior = jnp.where(mine, left_tag[1], right_tag[1])
        live_mask = jnp.broadcast_to(prior_marks[None, :] < prior, (NEWCAP, prior_rows))
        numer, top, total = attend_part(
            query_rows, cache_keys[s], cache_values[s], live_mask, head_count
        )
        pad = jnp.zeros((NEWCAP, RESULT_WIDTH - feat_width - 2 * head_count), jnp.float32)
        served.append(jnp.concatenate([numer, top, total, pad], axis=1))
    back_left = jnp.where(left_is_zero, served[0], served[1])
    back_right = jnp.where(left_is_zero, served[1], served[0])
    got_right = shifted(back_left, "req", -1)
    got_left = shifted(back_right, "req", 1)

    def masked_rows(source, start, length):
        keep = (row_marks < length)[:, None]
        return jnp.where(keep, rows_of(source, start), jnp.zeros((), jnp.bfloat16))

    right_kv = jnp.stack(
        [masked_rows(keys_new, right_start, right_len), masked_rows(values_new, right_start, right_len)]
    )
    left_kv = jnp.stack(
        [masked_rows(keys_new, left_start, left_len), masked_rows(values_new, left_start, left_len)]
    )
    right_kv, left_kv, got_right, got_left = lax.optimization_barrier(
        (right_kv, left_kv, got_right, got_left)
    )
    from_left_kv = shifted(right_kv, "req", 1)
    from_right_kv = shifted(left_kv, "req", -1)

    def split_result(result):
        numer = result[:, :feat_width]
        top = result[:, feat_width : feat_width + head_count]
        total = result[:, feat_width + head_count : feat_width + 2 * head_count]
        return numer, top, total

    got_right = split_result(got_right)
    got_left = split_result(got_left)

    def place(result, start, length):
        numer, top, total = result
        shift = tok_count - start
        keep = ((positions - start >= 0) & (positions - start < length))[:, None]

        def moved(x):
            padded = jnp.pad(x, ((tok_count, tok_count - NEWCAP), (0, 0)))
            return lax.dynamic_slice_in_dim(padded, shift, tok_count, 0)

        return keep, moved(numer), moved(top), moved(total)

    keep_r, numer_r, top_r, total_r = place(got_right, right_start, right_len)
    keep_l, numer_l, top_l, total_l = place(got_left, left_start, left_len)
    prior_numer = jnp.where(keep_r, numer_r, jnp.where(keep_l, numer_l, 0.0))
    prior_top = jnp.where(keep_r, top_r, jnp.where(keep_l, top_l, floor_value))
    prior_total = jnp.where(keep_r, total_r, jnp.where(keep_l, total_l, 0.0))

    both_top = jnp.maximum(own_top, prior_top)
    own_scale = jnp.exp(own_top - both_top)
    prior_scale = jnp.exp(prior_top - both_top)
    denominator = own_total * own_scale + prior_total * prior_scale
    numerator = (
        own_numer.reshape(tok_count, head_count, HD) * own_scale[:, :, None]
        + prior_numer.reshape(tok_count, head_count, HD) * prior_scale[:, :, None]
    )
    attended = (
        (numerator / denominator[:, :, None]).reshape(tok_count, feat_width).astype(jnp.bfloat16)
    )
    mixed = lax.psum_scatter(
        jnp.dot(attended, out_proj, preferred_element_type=jnp.float32).astype(jnp.bfloat16),
        "tp",
        scatter_dimension=0,
        tiled=True,
    )

    slot_ids = jnp.arange(slot_count, dtype=jnp.int32)

    def stored(from_left_rows, from_right_rows):
        at_left = (slot_ids == left_tag[0])[:, None, None]
        at_right = (slot_ids == right_tag[0])[:, None, None]
        return jnp.where(
            at_left,
            from_left_rows[None],
            jnp.where(at_right, from_right_rows[None], jnp.zeros((), jnp.bfloat16)),
        )

    new_keys = stored(from_left_kv[0], from_right_kv[0])
    new_values = stored(from_left_kv[1], from_right_kv[1])
    return (mixed, new_keys, new_values)


def solution(mesh):
    in_specs = (
        P("req", "tp"),
        P("req", "tp"),
        P("req", "tp"),
        P("req", None, "tp"),
        P("req", None, "tp"),
        P("tp", None),
        P("req", None),
        P("req", None),
        P("req", None),
        P("req", None),
    )
    out_specs = (P(("req", "tp"), None), P("req", None, "tp"), P("req", None, "tp"))
    return jax.shard_map(body, mesh=mesh, in_specs=in_specs, out_specs=out_specs, check_vma=False)
```

```python
import functools
import math

import jax
import jax.numpy as jnp
from jax import lax
from jax.experimental import pallas as pl
from jax.experimental.pallas import tpu as pltpu
from jax.sharding import PartitionSpec as P

HD = 224
NEWCAP = 192


floor_value = -1e30
TAG_ROWS = 8
RESULT_WIDTH = 1024


def shifted(value, axis, steps):
    count = lax.axis_size(axis)
    pairs = [(source, (source + steps) % count) for source in range(count)]
    return lax.ppermute(value, axis, pairs)


def attend_part(query_rows, key_rows, value_rows, live_mask, head_count):
    row_count = query_rows.shape[0]
    key_count = key_rows.shape[0]
    query_heads = query_rows.reshape(row_count, head_count, HD)
    key_heads = key_rows.reshape(key_count, head_count, HD)
    value_heads = value_rows.reshape(key_count, head_count, HD)
    scores = jnp.einsum(
        "thd,shd->hts", query_heads, key_heads, preferred_element_type=jnp.float32
    ) * (1.0 / math.sqrt(HD))
    scores = jnp.where(live_mask[None], scores, floor_value)
    row_top = jnp.max(scores, axis=2)
    weights = jnp.where(live_mask[None], jnp.exp(scores - row_top[:, :, None]), 0.0)
    row_total = jnp.sum(weights, axis=2)
    numerator = jnp.einsum(
        "hts,shd->thd",
        weights.astype(jnp.bfloat16),
        value_heads,
        preferred_element_type=jnp.float32,
    )
    return (numerator.reshape(row_count, head_count * HD), row_top.T, row_total.T)


def prior_kernel(head_count, prior_ref, query_ref, key_ref, value_ref, out_ref):
    slot = pl.program_id(0)
    prior = prior_ref[slot]
    query_rows = query_ref[...]
    key_rows = key_ref[...]
    value_rows = value_ref[...]
    row_count, feat_width = query_rows.shape
    key_count = key_rows.shape[0]
    lanes = lax.broadcasted_iota(jnp.int32, (1, feat_width), 1)
    live = lax.broadcasted_iota(jnp.int32, (1, key_count), 1) < prior
    tail_lanes = lax.broadcasted_iota(jnp.int32, (row_count, out_ref.shape[1] - feat_width), 1)
    numer = jnp.zeros((row_count, feat_width), jnp.float32)
    tail = jnp.zeros((row_count, out_ref.shape[1] - feat_width), jnp.float32)
    for h in range(head_count):
        in_head = (lanes >= h * HD) & (lanes < (h + 1) * HD)
        head_query = jnp.where(in_head, query_rows, jnp.zeros((), query_rows.dtype))
        scores = lax.dot_general(
            head_query, key_rows, (((1,), (1,)), ((), ())), preferred_element_type=jnp.float32
        ) * (1.0 / math.sqrt(HD))
        scores = jnp.where(live, scores, floor_value)
        row_top = jnp.max(scores, axis=1, keepdims=True)
        weights = jnp.where(live, jnp.exp(scores - row_top), 0.0)
        row_total = jnp.sum(weights, axis=1, keepdims=True)
        head_out = jnp.dot(
            weights.astype(jnp.bfloat16), value_rows, preferred_element_type=jnp.float32
        )
        numer = numer + jnp.where(in_head, head_out, 0.0)
        tail = jnp.where(tail_lanes == h, row_top, tail)
        tail = jnp.where(tail_lanes == head_count + h, row_total, tail)
    out_ref[:, :feat_width] = numer
    out_ref[:, feat_width:] = tail


def serve_slots(priors, query_stack, cache_keys, cache_values, head_count):
    slot_count, row_count, feat_width = query_stack.shape
    key_count = cache_keys.shape[1]
    flops = slot_count * head_count * 4 * row_count * key_count * feat_width
    moved = 2 * (query_stack.size + cache_keys.size + cache_values.size) + 4 * slot_count * row_count * RESULT_WIDTH
    return pl.pallas_call(
        functools.partial(prior_kernel, head_count),
        out_shape=jax.ShapeDtypeStruct((slot_count, row_count, RESULT_WIDTH), jnp.float32),
        grid_spec=pltpu.PrefetchScalarGridSpec(
            num_scalar_prefetch=1,
            grid=(slot_count,),
            in_specs=[
                pl.BlockSpec((None, row_count, feat_width), lambda s, pr: (s, 0, 0)),
                pl.BlockSpec((None, key_count, feat_width), lambda s, pr: (s, 0, 0)),
                pl.BlockSpec((None, key_count, feat_width), lambda s, pr: (s, 0, 0)),
            ],
            out_specs=pl.BlockSpec((None, row_count, RESULT_WIDTH), lambda s, pr: (s, 0, 0)),
        ),
        cost_estimate=pl.CostEstimate(
            flops=flops,
            transcendentals=slot_count * head_count * row_count * key_count,
            bytes_accessed=moved,
        ),
    )(priors, query_stack, cache_keys, cache_values)


def body(
    queries,
    keys_new,
    values_new,
    cache_keys,
    cache_values,
    out_proj,
    req_lengths,
    cache_owner,
    cache_slot,
    prior_len,
):
    tok_count = queries.shape[0]
    feat_width = queries.shape[1]
    head_count = feat_width // HD
    slot_count = cache_keys.shape[0]
    prior_rows = cache_keys.shape[1]
    req_lens = req_lengths[0]
    req_ends = jnp.cumsum(req_lens)
    starts = req_ends - req_lens
    positions = jnp.arange(tok_count, dtype=jnp.int32)
    row_marks = jnp.arange(NEWCAP, dtype=jnp.int32)
    prior_marks = jnp.arange(prior_rows, dtype=jnp.int32)
    req_count = lax.axis_size("req")
    req_index = lax.axis_index("req")
    raw_offset = (cache_owner[0] - req_index + req_count) % req_count
    offset = jnp.where(raw_offset == req_count - 1, -1, raw_offset)

    def request_at(distance):
        pick = offset[0] == distance
        start = jnp.where(pick, starts[0], starts[1])
        length = jnp.where(pick, req_lens[0], req_lens[1])
        slot = jnp.where(pick, cache_slot[0, 0], cache_slot[0, 1])
        prior = jnp.where(pick, prior_len[0, 0], prior_len[0, 1])
        return start, length, slot, prior

    def rows_of(source, start):
        return lax.dynamic_slice_in_dim(source, start, NEWCAP, 0)

    def query_bundle(start, length, slot, prior):
        tag = jnp.stack([slot, prior // 32, prior % 32, length]).astype(jnp.bfloat16)
        tag_rows = jnp.zeros((TAG_ROWS, feat_width), jnp.bfloat16).at[0, :4].set(tag)
        return jnp.concatenate([rows_of(queries, start), tag_rows], axis=0)

    def read_tag(bundle):
        tag = bundle[NEWCAP, :4].astype(jnp.float32).astype(jnp.int32)
        return tag[0], tag[1] * 32 + tag[2], tag[3]

    right_start, right_len, right_slot, right_prior = request_at(1)
    left_start, left_len, left_slot, left_prior = request_at(-1)

    from_left = shifted(query_bundle(right_start, right_len, right_slot, right_prior), "req", 1)
    from_right = shifted(query_bundle(left_start, left_len, left_slot, left_prior), "req", -1)

    segment = jnp.sum((positions[:, None] >= req_ends[None, :]).astype(jnp.int32), axis=1)
    own_live = (segment[:, None] == segment[None, :]) & (positions[None, :] <= positions[:, None])
    own_numer, own_top, own_total = attend_part(queries, keys_new, values_new, own_live, head_count)

    left_tag = read_tag(from_left)
    right_tag = read_tag(from_right)
    left_is_zero = left_tag[0] == 0
    left_rows = from_left[:NEWCAP]
    right_rows = from_right[:NEWCAP]
    query_stack = jnp.stack(
        [jnp.where(left_is_zero, left_rows, right_rows), jnp.where(left_is_zero, right_rows, left_rows)]
    )
    priors = jnp.stack(
        [jnp.where(left_is_zero, left_tag[1], right_tag[1]), jnp.where(left_is_zero, right_tag[1], left_tag[1])]
    )
    served = serve_slots(priors, query_stack, cache_keys, cache_values, head_count)
    back_left = jnp.where(left_is_zero, served[0], served[1])
    back_right = jnp.where(left_is_zero, served[1], served[0])
    got_right = shifted(back_left, "req", -1)
    got_left = shifted(back_right, "req", 1)

    def masked_rows(source, start, length):
        keep = (row_marks < length)[:, None]
        return jnp.where(keep, rows_of(source, start), jnp.zeros((), jnp.bfloat16))

    right_kv = jnp.stack(
        [masked_rows(keys_new, right_start, right_len), masked_rows(values_new, right_start, right_len)]
    )
    left_kv = jnp.stack(
        [masked_rows(keys_new, left_start, left_len), masked_rows(values_new, left_start, left_len)]
    )
    right_kv, left_kv, got_right, got_left = lax.optimization_barrier(
        (right_kv, left_kv, got_right, got_left)
    )
    from_left_kv = shifted(right_kv, "req", 1)
    from_right_kv = shifted(left_kv, "req", -1)

    def split_result(result):
        numer = result[:, :feat_width]
        top = result[:, feat_width : feat_width + head_count]
        total = result[:, feat_width + head_count : feat_width + 2 * head_count]
        return numer, top, total

    got_right = split_result(got_right)
    got_left = split_result(got_left)

    def place(result, start, length):
        numer, top, total = result
        shift = tok_count - start
        keep = ((positions - start >= 0) & (positions - start < length))[:, None]

        def moved(x):
            padded = jnp.pad(x, ((tok_count, tok_count - NEWCAP), (0, 0)))
            return lax.dynamic_slice_in_dim(padded, shift, tok_count, 0)

        return keep, moved(numer), moved(top), moved(total)

    keep_r, numer_r, top_r, total_r = place(got_right, right_start, right_len)
    keep_l, numer_l, top_l, total_l = place(got_left, left_start, left_len)
    prior_numer = jnp.where(keep_r, numer_r, jnp.where(keep_l, numer_l, 0.0))
    prior_top = jnp.where(keep_r, top_r, jnp.where(keep_l, top_l, floor_value))
    prior_total = jnp.where(keep_r, total_r, jnp.where(keep_l, total_l, 0.0))

    both_top = jnp.maximum(own_top, prior_top)
    own_scale = jnp.exp(own_top - both_top)
    prior_scale = jnp.exp(prior_top - both_top)
    denominator = own_total * own_scale + prior_total * prior_scale
    numerator = (
        own_numer.reshape(tok_count, head_count, HD) * own_scale[:, :, None]
        + prior_numer.reshape(tok_count, head_count, HD) * prior_scale[:, :, None]
    )
    attended = (
        (numerator / denominator[:, :, None]).reshape(tok_count, feat_width).astype(jnp.bfloat16)
    )
    mixed = lax.psum_scatter(
        jnp.dot(attended, out_proj, preferred_element_type=jnp.float32).astype(jnp.bfloat16),
        "tp",
        scatter_dimension=0,
        tiled=True,
    )

    slot_ids = jnp.arange(slot_count, dtype=jnp.int32)

    def stored(from_left_rows, from_right_rows):
        at_left = (slot_ids == left_tag[0])[:, None, None]
        at_right = (slot_ids == right_tag[0])[:, None, None]
        return jnp.where(
            at_left,
            from_left_rows[None],
            jnp.where(at_right, from_right_rows[None], jnp.zeros((), jnp.bfloat16)),
        )

    new_keys = stored(from_left_kv[0], from_right_kv[0])
    new_values = stored(from_left_kv[1], from_right_kv[1])
    return (mixed, new_keys, new_values)


def solution(mesh):
    in_specs = (
        P("req", "tp"),
        P("req", "tp"),
        P("req", "tp"),
        P("req", None, "tp"),
        P("req", None, "tp"),
        P("tp", None),
        P("req", None),
        P("req", None),
        P("req", None),
        P("req", None),
    )
    out_specs = (P(("req", "tp"), None), P("req", None, "tp"), P("req", None, "tp"))
    return jax.shard_map(body, mesh=mesh, in_specs=in_specs, out_specs=out_specs, check_vma=False)
```

```python
import functools
import math

import jax
import jax.numpy as jnp
from jax import lax
from jax.experimental import pallas as pl
from jax.experimental.pallas import tpu as pltpu
from jax.sharding import PartitionSpec as P

HD = 224
NEWCAP = 192


floor_value = -1e30
TAG_ROWS = 8
RESULT_WIDTH = 1024


def shifted(value, axis, steps):
    count = lax.axis_size(axis)
    pairs = [(source, (source + steps) % count) for source in range(count)]
    return lax.ppermute(value, axis, pairs)


def attend_part(query_rows, key_rows, value_rows, live_mask, head_count):
    row_count = query_rows.shape[0]
    key_count = key_rows.shape[0]
    query_heads = query_rows.reshape(row_count, head_count, HD)
    key_heads = key_rows.reshape(key_count, head_count, HD)
    value_heads = value_rows.reshape(key_count, head_count, HD)
    scores = jnp.einsum(
        "thd,shd->hts", query_heads, key_heads, preferred_element_type=jnp.float32
    ) * (1.0 / math.sqrt(HD))
    scores = jnp.where(live_mask[None], scores, floor_value)
    row_top = jnp.max(scores, axis=2)
    weights = jnp.where(live_mask[None], jnp.exp(scores - row_top[:, :, None]), 0.0)
    row_total = jnp.sum(weights, axis=2)
    numerator = jnp.einsum(
        "hts,shd->thd",
        weights.astype(jnp.bfloat16),
        value_heads,
        preferred_element_type=jnp.float32,
    )
    return (numerator.reshape(row_count, head_count * HD), row_top.T, row_total.T)


def prior_kernel(head_count, prior_ref, query_ref, key_ref, value_ref, out_ref):
    slot = pl.program_id(0)
    prior = prior_ref[slot]
    query_rows = query_ref[...]
    key_rows = key_ref[...]
    value_rows = value_ref[...]
    row_count, feat_width = query_rows.shape
    key_count = key_rows.shape[0]
    lanes = lax.broadcasted_iota(jnp.int32, (1, feat_width), 1)
    live = lax.broadcasted_iota(jnp.int32, (1, key_count), 1) < prior
    tail_lanes = lax.broadcasted_iota(jnp.int32, (row_count, out_ref.shape[1] - feat_width), 1)
    numer = jnp.zeros((row_count, feat_width), jnp.float32)
    tail = jnp.zeros((row_count, out_ref.shape[1] - feat_width), jnp.float32)
    for h in range(head_count):
        in_head = (lanes >= h * HD) & (lanes < (h + 1) * HD)
        head_query = jnp.where(in_head, query_rows, jnp.zeros((), query_rows.dtype))
        scores = lax.dot_general(
            head_query, key_rows, (((1,), (1,)), ((), ())), preferred_element_type=jnp.float32
        ) * (1.0 / math.sqrt(HD))
        scores = jnp.where(live, scores, floor_value)
        row_top = jnp.max(scores, axis=1, keepdims=True)
        weights = jnp.where(live, jnp.exp(scores - row_top), 0.0)
        row_total = jnp.sum(weights, axis=1, keepdims=True)
        head_out = jnp.dot(
            weights.astype(jnp.bfloat16), value_rows, preferred_element_type=jnp.float32
        )
        numer = numer + jnp.where(in_head, head_out, 0.0)
        tail = jnp.where(tail_lanes == h, row_top, tail)
        tail = jnp.where(tail_lanes == head_count + h, row_total, tail)
    out_ref[:, :feat_width] = numer
    out_ref[:, feat_width:] = tail


def serve_slots(priors, query_stack, cache_keys, cache_values, head_count):
    slot_count, row_count, feat_width = query_stack.shape
    key_count = cache_keys.shape[1]
    flops = slot_count * head_count * 4 * row_count * key_count * feat_width
    moved = 2 * (query_stack.size + cache_keys.size + cache_values.size) + 4 * slot_count * row_count * RESULT_WIDTH
    return pl.pallas_call(
        functools.partial(prior_kernel, head_count),
        out_shape=jax.ShapeDtypeStruct((slot_count, row_count, RESULT_WIDTH), jnp.float32),
        grid_spec=pltpu.PrefetchScalarGridSpec(
            num_scalar_prefetch=1,
            grid=(slot_count,),
            in_specs=[
                pl.BlockSpec((None, row_count, feat_width), lambda s, pr: (s, 0, 0)),
                pl.BlockSpec((None, key_count, feat_width), lambda s, pr: (s, 0, 0)),
                pl.BlockSpec((None, key_count, feat_width), lambda s, pr: (s, 0, 0)),
            ],
            out_specs=pl.BlockSpec((None, row_count, RESULT_WIDTH), lambda s, pr: (s, 0, 0)),
        ),
        cost_estimate=pl.CostEstimate(
            flops=flops,
            transcendentals=slot_count * head_count * row_count * key_count,
            bytes_accessed=moved,
        ),
    )(priors, query_stack, cache_keys, cache_values)


def body(
    queries,
    keys_new,
    values_new,
    cache_keys,
    cache_values,
    out_proj,
    req_lengths,
    cache_owner,
    cache_slot,
    prior_len,
):
    tok_count = queries.shape[0]
    feat_width = queries.shape[1]
    head_count = feat_width // HD
    slot_count = cache_keys.shape[0]
    prior_rows = cache_keys.shape[1]
    req_lens = req_lengths[0]
    req_ends = jnp.cumsum(req_lens)
    starts = req_ends - req_lens
    positions = jnp.arange(tok_count, dtype=jnp.int32)
    row_marks = jnp.arange(NEWCAP, dtype=jnp.int32)
    prior_marks = jnp.arange(prior_rows, dtype=jnp.int32)
    req_count = lax.axis_size("req")
    req_index = lax.axis_index("req")
    raw_offset = (cache_owner[0] - req_index + req_count) % req_count
    offset = jnp.where(raw_offset == req_count - 1, -1, raw_offset)

    def request_at(distance):
        pick = offset[0] == distance
        start = jnp.where(pick, starts[0], starts[1])
        length = jnp.where(pick, req_lens[0], req_lens[1])
        slot = jnp.where(pick, cache_slot[0, 0], cache_slot[0, 1])
        prior = jnp.where(pick, prior_len[0, 0], prior_len[0, 1])
        return start, length, slot, prior

    def rows_of(source, start):
        return lax.dynamic_slice_in_dim(source, start, NEWCAP, 0)

    def query_bundle(start, length, slot, prior):
        tag = jnp.stack([slot, prior // 32, prior % 32, length]).astype(jnp.bfloat16)
        tag_rows = jnp.zeros((TAG_ROWS, feat_width), jnp.bfloat16).at[0, :4].set(tag)
        return jnp.concatenate([rows_of(queries, start), tag_rows], axis=0)

    def read_tag(bundle):
        tag = bundle[NEWCAP, :4].astype(jnp.float32).astype(jnp.int32)
        return tag[0], tag[1] * 32 + tag[2], tag[3]

    right_start, right_len, right_slot, right_prior = request_at(1)
    left_start, left_len, left_slot, left_prior = request_at(-1)

    from_left = shifted(query_bundle(right_start, right_len, right_slot, right_prior), "req", 1)
    from_right = shifted(query_bundle(left_start, left_len, left_slot, left_prior), "req", -1)

    segment = jnp.sum((positions[:, None] >= req_ends[None, :]).astype(jnp.int32), axis=1)
    own_live = (segment[:, None] == segment[None, :]) & (positions[None, :] <= positions[:, None])
    own_numer, own_top, own_total = attend_part(queries, keys_new, values_new, own_live, head_count)

    left_tag = read_tag(from_left)
    right_tag = read_tag(from_right)
    left_is_zero = left_tag[0] == 0
    left_rows = from_left[:NEWCAP]
    right_rows = from_right[:NEWCAP]
    query_stack = jnp.stack(
        [jnp.where(left_is_zero, left_rows, right_rows), jnp.where(left_is_zero, right_rows, left_rows)]
    )
    priors = jnp.stack(
        [jnp.where(left_is_zero, left_tag[1], right_tag[1]), jnp.where(left_is_zero, right_tag[1], left_tag[1])]
    )
    served = serve_slots(priors, query_stack, cache_keys, cache_values, head_count)
    back_left = jnp.where(left_is_zero, served[0], served[1])
    back_right = jnp.where(left_is_zero, served[1], served[0])
    got_right = shifted(back_left, "req", -1)
    got_left = shifted(back_right, "req", 1)

    def masked_rows(source, start, length):
        keep = (row_marks < length)[:, None]
        return jnp.where(keep, rows_of(source, start), jnp.zeros((), jnp.bfloat16))

    right_kv = jnp.stack(
        [masked_rows(keys_new, right_start, right_len), masked_rows(values_new, right_start, right_len)]
    )
    left_kv = jnp.stack(
        [masked_rows(keys_new, left_start, left_len), masked_rows(values_new, left_start, left_len)]
    )
    right_kv, left_kv, got_right, got_left = lax.optimization_barrier(
        (right_kv, left_kv, got_right, got_left)
    )
    from_left_kv = shifted(right_kv, "req", 1)
    from_right_kv = shifted(left_kv, "req", -1)

    def split_result(result):
        numer = result[:, :feat_width]
        top = result[:, feat_width : feat_width + head_count]
        total = result[:, feat_width + head_count : feat_width + 2 * head_count]
        return numer, top, total

    got_right = split_result(got_right)
    got_left = split_result(got_left)

    def place(result, start, length):
        numer, top, total = result
        shift = tok_count - start
        keep = ((positions - start >= 0) & (positions - start < length))[:, None]

        def moved(x):
            padded = jnp.pad(x, ((tok_count, tok_count - NEWCAP), (0, 0)))
            return lax.dynamic_slice_in_dim(padded, shift, tok_count, 0)

        return keep, moved(numer), moved(top), moved(total)

    keep_r, numer_r, top_r, total_r = place(got_right, right_start, right_len)
    keep_l, numer_l, top_l, total_l = place(got_left, left_start, left_len)
    prior_numer = jnp.where(keep_r, numer_r, jnp.where(keep_l, numer_l, 0.0))
    prior_top = jnp.where(keep_r, top_r, jnp.where(keep_l, top_l, floor_value))
    prior_total = jnp.where(keep_r, total_r, jnp.where(keep_l, total_l, 0.0))

    both_top = jnp.maximum(own_top, prior_top)
    own_scale = jnp.exp(own_top - both_top)
    prior_scale = jnp.exp(prior_top - both_top)
    denominator = own_total * own_scale + prior_total * prior_scale
    numerator = (
        own_numer.reshape(tok_count, head_count, HD) * own_scale[:, :, None]
        + prior_numer.reshape(tok_count, head_count, HD) * prior_scale[:, :, None]
    )
    attended = (
        (numerator / denominator[:, :, None]).reshape(tok_count, feat_width).astype(jnp.bfloat16)
    )
    chip_count = lax.axis_size("x")
    core_count = lax.axis_size("core")
    block_rows = tok_count // (chip_count * core_count)
    reordered = (
        attended.reshape(chip_count, core_count, block_rows, feat_width)
        .transpose(1, 0, 2, 3)
        .reshape(tok_count, feat_width)
    )
    partial = jnp.dot(reordered, out_proj, preferred_element_type=jnp.float32).astype(jnp.bfloat16)
    partial = partial.reshape(core_count, chip_count * block_rows, partial.shape[1])
    partial = lax.psum_scatter(partial, "core", scatter_dimension=0, tiled=False)
    partial = partial.reshape(chip_count, block_rows, partial.shape[1])
    mixed = lax.psum_scatter(partial, "x", scatter_dimension=0, tiled=False)
    slot_ids = jnp.arange(slot_count, dtype=jnp.int32)

    def stored(from_left_rows, from_right_rows):
        at_left = (slot_ids == left_tag[0])[:, None, None]
        at_right = (slot_ids == right_tag[0])[:, None, None]
        return jnp.where(
            at_left,
            from_left_rows[None],
            jnp.where(at_right, from_right_rows[None], jnp.zeros((), jnp.bfloat16)),
        )

    new_keys = stored(from_left_kv[0], from_right_kv[0])
    new_values = stored(from_left_kv[1], from_right_kv[1])
    return (mixed, new_keys, new_values)


def solution(mesh):
    req_count, tp_count = mesh.devices.shape
    core_count = 2
    split_mesh = jax.sharding.Mesh(
        mesh.devices.reshape(req_count, tp_count // core_count, core_count), ("req", "x", "core")
    )
    tp = ("x", "core")
    in_specs = (
        P("req", tp),
        P("req", tp),
        P("req", tp),
        P("req", None, tp),
        P("req", None, tp),
        P(tp, None),
        P("req", None),
        P("req", None),
        P("req", None),
        P("req", None),
    )
    out_specs = (P(("req", "x", "core"), None), P("req", None, tp), P("req", None, tp))
    return jax.shard_map(
        body, mesh=split_mesh, in_specs=in_specs, out_specs=out_specs, check_vma=False
    )
```

```python
import functools
import math

import jax
import jax.numpy as jnp
from jax import lax
from jax.experimental import pallas as pl
from jax.experimental.pallas import tpu as pltpu
from jax.sharding import PartitionSpec as P

HD = 224
NEWCAP = 192


floor_value = -1e30
TAG_ROWS = 8
RESULT_WIDTH = 1024


def shifted(value, axis, steps):
    count = lax.axis_size(axis)
    pairs = [(source, (source + steps) % count) for source in range(count)]
    return lax.ppermute(value, axis, pairs)


def attend_part(query_rows, key_rows, value_rows, live_mask, head_count):
    row_count = query_rows.shape[0]
    key_count = key_rows.shape[0]
    query_heads = query_rows.reshape(row_count, head_count, HD)
    key_heads = key_rows.reshape(key_count, head_count, HD)
    value_heads = value_rows.reshape(key_count, head_count, HD)
    scores = jnp.einsum(
        "thd,shd->hts", query_heads, key_heads, preferred_element_type=jnp.float32
    ) * (1.0 / math.sqrt(HD))
    scores = jnp.where(live_mask[None], scores, floor_value)
    row_top = jnp.max(scores, axis=2)
    weights = jnp.where(live_mask[None], jnp.exp(scores - row_top[:, :, None]), 0.0)
    row_total = jnp.sum(weights, axis=2)
    numerator = jnp.einsum(
        "hts,shd->thd",
        weights.astype(jnp.bfloat16),
        value_heads,
        preferred_element_type=jnp.float32,
    )
    return (numerator.reshape(row_count, head_count * HD), row_top.T, row_total.T)


def prior_kernel(head_count, prior_ref, query_ref, key_ref, value_ref, out_ref):
    slot = pl.program_id(0)
    prior = prior_ref[slot]
    row_count, feat_width = query_ref.shape
    key_count = key_ref.shape[0]
    live = lax.broadcasted_iota(jnp.int32, (1, key_count), 1) < prior
    tail_lanes = lax.broadcasted_iota(jnp.int32, (row_count, out_ref.shape[1] - feat_width), 1)
    tail = jnp.zeros((row_count, out_ref.shape[1] - feat_width), jnp.float32)
    out_ref[:, :feat_width] = jnp.zeros((row_count, feat_width), jnp.float32)
    for h in range(head_count):
        low = (h * HD) // 128 * 128
        high = min(feat_width, -(-((h + 1) * HD) // 128) * 128)
        lanes = low + lax.broadcasted_iota(jnp.int32, (1, high - low), 1)
        in_head = (lanes >= h * HD) & (lanes < (h + 1) * HD)
        head_query = jnp.where(in_head, query_ref[:, low:high], jnp.zeros((), query_ref.dtype))
        scores = lax.dot_general(
            head_query, key_ref[:, low:high], (((1,), (1,)), ((), ())),
            preferred_element_type=jnp.float32,
        ) * (1.0 / math.sqrt(HD))
        scores = jnp.where(live, scores, floor_value)
        row_top = jnp.max(scores, axis=1, keepdims=True)
        weights = jnp.where(live, jnp.exp(scores - row_top), 0.0)
        row_total = jnp.sum(weights, axis=1, keepdims=True)
        head_out = jnp.dot(
            weights.astype(jnp.bfloat16), value_ref[:, low:high], preferred_element_type=jnp.float32
        )
        out_ref[:, low:high] = out_ref[:, low:high] + jnp.where(in_head, head_out, 0.0)
        tail = jnp.where(tail_lanes == h, row_top, tail)
        tail = jnp.where(tail_lanes == head_count + h, row_total, tail)
    out_ref[:, feat_width:] = tail


def serve_slots(priors, query_stack, cache_keys, cache_values, head_count):
    slot_count, row_count, feat_width = query_stack.shape
    key_count = cache_keys.shape[1]
    window_lanes = sum(
        min(feat_width, -(-((h + 1) * HD) // 128) * 128) - (h * HD) // 128 * 128
        for h in range(head_count)
    )
    flops = slot_count * 4 * row_count * key_count * window_lanes
    moved = 2 * (query_stack.size + cache_keys.size + cache_values.size) + 4 * slot_count * row_count * RESULT_WIDTH
    return pl.pallas_call(
        functools.partial(prior_kernel, head_count),
        out_shape=jax.ShapeDtypeStruct((slot_count, row_count, RESULT_WIDTH), jnp.float32),
        grid_spec=pltpu.PrefetchScalarGridSpec(
            num_scalar_prefetch=1,
            grid=(slot_count,),
            in_specs=[
                pl.BlockSpec((None, row_count, feat_width), lambda s, pr: (s, 0, 0)),
                pl.BlockSpec((None, key_count, feat_width), lambda s, pr: (s, 0, 0)),
                pl.BlockSpec((None, key_count, feat_width), lambda s, pr: (s, 0, 0)),
            ],
            out_specs=pl.BlockSpec((None, row_count, RESULT_WIDTH), lambda s, pr: (s, 0, 0)),
        ),
        cost_estimate=pl.CostEstimate(
            flops=flops,
            transcendentals=slot_count * head_count * row_count * key_count,
            bytes_accessed=moved,
        ),
    )(priors, query_stack, cache_keys, cache_values)


def body(
    queries,
    keys_new,
    values_new,
    cache_keys,
    cache_values,
    out_proj,
    req_lengths,
    cache_owner,
    cache_slot,
    prior_len,
):
    tok_count = queries.shape[0]
    feat_width = queries.shape[1]
    head_count = feat_width // HD
    slot_count = cache_keys.shape[0]
    prior_rows = cache_keys.shape[1]
    req_lens = req_lengths[0]
    req_ends = jnp.cumsum(req_lens)
    positions = jnp.arange(tok_count, dtype=jnp.int32)
    row_marks = jnp.arange(NEWCAP, dtype=jnp.int32)
    prior_marks = jnp.arange(prior_rows, dtype=jnp.int32)
    req_count = lax.axis_size("req")
    req_index = lax.axis_index("req")

    first_right = cache_owner[0, 0] == (req_index + 1) % req_count

    def request_at(distance):
        pick = first_right if distance == 1 else jnp.logical_not(first_right)
        start = jnp.where(pick, 0, req_lens[0])
        length = jnp.where(pick, req_lens[0], req_lens[1])
        slot = jnp.where(pick, cache_slot[0, 0], cache_slot[0, 1])
        prior = jnp.where(pick, prior_len[0, 0], prior_len[0, 1])
        return start, length, slot, prior

    def rows_of(source, start):
        return lax.dynamic_slice_in_dim(source, start, NEWCAP, 0)

    def query_bundle(start, length, slot, prior):
        tag = jnp.stack([slot, prior // 32, prior % 32, length]).astype(jnp.bfloat16)
        tag_rows = jnp.zeros((TAG_ROWS, feat_width), jnp.bfloat16).at[0, :4].set(tag)
        return jnp.concatenate([rows_of(queries, start), tag_rows], axis=0)

    def read_tag(bundle):
        tag = bundle[NEWCAP, :4].astype(jnp.float32).astype(jnp.int32)
        return tag[0], tag[1] * 32 + tag[2], tag[3]

    right_start, right_len, right_slot, right_prior = request_at(1)
    left_start, left_len, left_slot, left_prior = request_at(-1)

    from_left = shifted(query_bundle(right_start, right_len, right_slot, right_prior), "req", 1)
    from_right = shifted(query_bundle(left_start, left_len, left_slot, left_prior), "req", -1)

    segment = jnp.sum((positions[:, None] >= req_ends[None, :]).astype(jnp.int32), axis=1)
    own_live = (segment[:, None] == segment[None, :]) & (positions[None, :] <= positions[:, None])
    own_numer, own_top, own_total = attend_part(queries, keys_new, values_new, own_live, head_count)

    left_tag = read_tag(from_left)
    right_tag = read_tag(from_right)
    left_is_zero = left_tag[0] == 0
    left_rows = from_left[:NEWCAP]
    right_rows = from_right[:NEWCAP]
    query_stack = jnp.stack(
        [jnp.where(left_is_zero, left_rows, right_rows), jnp.where(left_is_zero, right_rows, left_rows)]
    )
    priors = jnp.stack(
        [jnp.where(left_is_zero, left_tag[1], right_tag[1]), jnp.where(left_is_zero, right_tag[1], left_tag[1])]
    )
    served = serve_slots(priors, query_stack, cache_keys, cache_values, head_count)
    back_left = jnp.where(left_is_zero, served[0], served[1])
    back_right = jnp.where(left_is_zero, served[1], served[0])
    got_right = shifted(back_left, "req", -1)
    got_left = shifted(back_right, "req", 1)

    def masked_rows(source, start, length):
        keep = (row_marks < length)[:, None]
        return jnp.where(keep, rows_of(source, start), jnp.zeros((), jnp.bfloat16))

    right_kv = jnp.stack(
        [masked_rows(keys_new, right_start, right_len), masked_rows(values_new, right_start, right_len)]
    )
    left_kv = jnp.stack(
        [masked_rows(keys_new, left_start, left_len), masked_rows(values_new, left_start, left_len)]
    )
    right_kv, left_kv, got_right, got_left = lax.optimization_barrier(
        (right_kv, left_kv, got_right, got_left)
    )
    from_left_kv = shifted(right_kv, "req", 1)
    from_right_kv = shifted(left_kv, "req", -1)

    def split_result(result):
        numer = result[:, :feat_width]
        top = result[:, feat_width : feat_width + head_count]
        total = result[:, feat_width + head_count : feat_width + 2 * head_count]
        return numer, top, total

    got_right = split_result(got_right)
    got_left = split_result(got_left)

    def place(result, start, length):
        numer, top, total = result
        shift = tok_count - start
        keep = ((positions - start >= 0) & (positions - start < length))[:, None]

        def moved(x):
            padded = jnp.pad(x, ((tok_count, tok_count - NEWCAP), (0, 0)))
            return lax.dynamic_slice_in_dim(padded, shift, tok_count, 0)

        return keep, moved(numer), moved(top), moved(total)

    keep_r, numer_r, top_r, total_r = place(got_right, right_start, right_len)
    keep_l, numer_l, top_l, total_l = place(got_left, left_start, left_len)
    prior_numer = jnp.where(keep_r, numer_r, jnp.where(keep_l, numer_l, 0.0))
    prior_top = jnp.where(keep_r, top_r, jnp.where(keep_l, top_l, floor_value))
    prior_total = jnp.where(keep_r, total_r, jnp.where(keep_l, total_l, 0.0))

    both_top = jnp.maximum(own_top, prior_top)
    own_scale = jnp.exp(own_top - both_top)
    prior_scale = jnp.exp(prior_top - both_top)
    denominator = own_total * own_scale + prior_total * prior_scale
    numerator = (
        own_numer.reshape(tok_count, head_count, HD) * own_scale[:, :, None]
        + prior_numer.reshape(tok_count, head_count, HD) * prior_scale[:, :, None]
    )
    attended = (
        (numerator / denominator[:, :, None]).reshape(tok_count, feat_width).astype(jnp.bfloat16)
    )
    mixed = lax.psum_scatter(
        jnp.dot(attended, out_proj, preferred_element_type=jnp.float32).astype(jnp.bfloat16),
        "tp",
        scatter_dimension=0,
        tiled=True,
    )

    slot_ids = jnp.arange(slot_count, dtype=jnp.int32)

    def stored(from_left_rows, from_right_rows):
        at_left = (slot_ids == left_tag[0])[:, None, None]
        at_right = (slot_ids == right_tag[0])[:, None, None]
        return jnp.where(
            at_left,
            from_left_rows[None],
            jnp.where(at_right, from_right_rows[None], jnp.zeros((), jnp.bfloat16)),
        )

    new_keys = stored(from_left_kv[0], from_right_kv[0])
    new_values = stored(from_left_kv[1], from_right_kv[1])
    return (mixed, new_keys, new_values)


def solution(mesh):
    in_specs = (
        P("req", "tp"),
        P("req", "tp"),
        P("req", "tp"),
        P("req", None, "tp"),
        P("req", None, "tp"),
        P("tp", None),
        P("req", None),
        P("req", None),
        P("req", None),
        P("req", None),
    )
    out_specs = (P(("req", "tp"), None), P("req", None, "tp"), P("req", None, "tp"))
    return jax.shard_map(body, mesh=mesh, in_specs=in_specs, out_specs=out_specs, check_vma=False)
```

```python
import functools
import math

import jax
import jax.numpy as jnp
from jax import lax
from jax.experimental import pallas as pl
from jax.experimental.pallas import tpu as pltpu
from jax.sharding import PartitionSpec as P

HD = 224
NEWCAP = 192


floor_value = -1e30
TAG_ROWS = 8
RESULT_WIDTH = 1024


def shifted(value, axis, steps):
    count = lax.axis_size(axis)
    pairs = [(source, (source + steps) % count) for source in range(count)]
    return lax.ppermute(value, axis, pairs)


def attend_part(query_rows, key_rows, value_rows, live_mask, head_count):
    row_count = query_rows.shape[0]
    key_count = key_rows.shape[0]
    query_heads = query_rows.reshape(row_count, head_count, HD)
    key_heads = key_rows.reshape(key_count, head_count, HD)
    value_heads = value_rows.reshape(key_count, head_count, HD)
    scores = jnp.einsum(
        "thd,shd->hts", query_heads, key_heads, preferred_element_type=jnp.float32
    ) * (1.0 / math.sqrt(HD))
    scores = jnp.where(live_mask[None], scores, floor_value)
    row_top = jnp.max(scores, axis=2)
    weights = jnp.where(live_mask[None], jnp.exp(scores - row_top[:, :, None]), 0.0)
    row_total = jnp.sum(weights, axis=2)
    numerator = jnp.einsum(
        "hts,shd->thd",
        weights.astype(jnp.bfloat16),
        value_heads,
        preferred_element_type=jnp.float32,
    )
    return (numerator.reshape(row_count, head_count * HD), row_top.T, row_total.T)


def prior_kernel(head_count, prior_ref, query_ref, key_ref, value_ref, out_ref, numer_ref):
    slot = pl.program_id(0)
    prior = prior_ref[slot]
    row_count, feat_width = query_ref.shape
    key_count = key_ref.shape[0]
    live = lax.broadcasted_iota(jnp.int32, (1, key_count), 1) < prior
    tail_lanes = lax.broadcasted_iota(jnp.int32, (row_count, out_ref.shape[1] - feat_width), 1)
    tail = jnp.zeros((row_count, out_ref.shape[1] - feat_width), jnp.float32)
    numer_ref[...] = jnp.zeros((row_count, feat_width), jnp.float32)
    for h in range(head_count):
        low = (h * HD) // 128 * 128
        high = min(feat_width, -(-((h + 1) * HD) // 128) * 128)
        lanes = low + lax.broadcasted_iota(jnp.int32, (1, high - low), 1)
        in_head = (lanes >= h * HD) & (lanes < (h + 1) * HD)
        head_query = jnp.where(in_head, query_ref[:, low:high], jnp.zeros((), query_ref.dtype))
        scores = lax.dot_general(
            head_query, key_ref[:, low:high], (((1,), (1,)), ((), ())),
            preferred_element_type=jnp.float32,
        ) * (1.0 / math.sqrt(HD))
        scores = jnp.where(live, scores, floor_value)
        row_top = jnp.max(scores, axis=1, keepdims=True)
        weights = jnp.where(live, jnp.exp(scores - row_top), 0.0)
        row_total = jnp.sum(weights, axis=1, keepdims=True)
        head_out = jnp.dot(
            weights.astype(jnp.bfloat16), value_ref[:, low:high], preferred_element_type=jnp.float32
        )
        numer_ref[:, low:high] = numer_ref[:, low:high] + jnp.where(in_head, head_out / row_total, 0.0)
        log_total = row_top + jnp.log(row_total)
        for part in range(3):
            piece = log_total.astype(jnp.bfloat16).astype(jnp.float32)
            tail = jnp.where(tail_lanes == part * head_count + h, piece, tail)
            log_total = log_total - piece
    out_ref[:, :feat_width] = numer_ref[...].astype(out_ref.dtype)
    out_ref[:, feat_width:] = tail.astype(out_ref.dtype)


def serve_slots(priors, query_stack, cache_keys, cache_values, head_count):
    slot_count, row_count, feat_width = query_stack.shape
    key_count = cache_keys.shape[1]
    window_lanes = sum(
        min(feat_width, -(-((h + 1) * HD) // 128) * 128) - (h * HD) // 128 * 128
        for h in range(head_count)
    )
    flops = slot_count * 4 * row_count * key_count * window_lanes
    moved = 2 * (query_stack.size + cache_keys.size + cache_values.size) + 2 * slot_count * row_count * RESULT_WIDTH
    return pl.pallas_call(
        functools.partial(prior_kernel, head_count),
        out_shape=jax.ShapeDtypeStruct((slot_count, row_count, RESULT_WIDTH), jnp.bfloat16),
        grid_spec=pltpu.PrefetchScalarGridSpec(
            num_scalar_prefetch=1,
            grid=(slot_count,),
            in_specs=[
                pl.BlockSpec((None, row_count, feat_width), lambda s, pr: (s, 0, 0)),
                pl.BlockSpec((None, key_count, feat_width), lambda s, pr: (s, 0, 0)),
                pl.BlockSpec((None, key_count, feat_width), lambda s, pr: (s, 0, 0)),
            ],
            out_specs=pl.BlockSpec((None, row_count, RESULT_WIDTH), lambda s, pr: (s, 0, 0)),
            scratch_shapes=[pltpu.VMEM((row_count, feat_width), jnp.float32)],
        ),
        cost_estimate=pl.CostEstimate(
            flops=flops,
            transcendentals=slot_count * head_count * row_count * key_count,
            bytes_accessed=moved,
        ),
    )(priors, query_stack, cache_keys, cache_values)


def body(
    queries,
    keys_new,
    values_new,
    cache_keys,
    cache_values,
    out_proj,
    req_lengths,
    cache_owner,
    cache_slot,
    prior_len,
):
    tok_count = queries.shape[0]
    feat_width = queries.shape[1]
    head_count = feat_width // HD
    slot_count = cache_keys.shape[0]
    prior_rows = cache_keys.shape[1]
    req_lens = req_lengths[0]
    req_ends = jnp.cumsum(req_lens)
    positions = jnp.arange(tok_count, dtype=jnp.int32)
    row_marks = jnp.arange(NEWCAP, dtype=jnp.int32)
    prior_marks = jnp.arange(prior_rows, dtype=jnp.int32)
    req_count = lax.axis_size("req")
    req_index = lax.axis_index("req")

    first_right = cache_owner[0, 0] == (req_index + 1) % req_count

    def request_at(distance):
        pick = first_right if distance == 1 else jnp.logical_not(first_right)
        start = jnp.where(pick, 0, req_lens[0])
        length = jnp.where(pick, req_lens[0], req_lens[1])
        slot = jnp.where(pick, cache_slot[0, 0], cache_slot[0, 1])
        prior = jnp.where(pick, prior_len[0, 0], prior_len[0, 1])
        return start, length, slot, prior

    def rows_of(source, start):
        return lax.dynamic_slice_in_dim(source, start, NEWCAP, 0)

    def query_bundle(start, length, slot, prior):
        tag = jnp.stack([slot, prior // 32, prior % 32, length]).astype(jnp.bfloat16)
        tag_rows = jnp.zeros((TAG_ROWS, feat_width), jnp.bfloat16).at[0, :4].set(tag)
        return jnp.concatenate([rows_of(queries, start), tag_rows], axis=0)

    def read_tag(bundle):
        tag = bundle[NEWCAP, :4].astype(jnp.float32).astype(jnp.int32)
        return tag[0], tag[1] * 32 + tag[2], tag[3]

    right_start, right_len, right_slot, right_prior = request_at(1)
    left_start, left_len, left_slot, left_prior = request_at(-1)

    from_left = shifted(query_bundle(right_start, right_len, right_slot, right_prior), "req", 1)
    from_right = shifted(query_bundle(left_start, left_len, left_slot, left_prior), "req", -1)

    segment = jnp.sum((positions[:, None] >= req_ends[None, :]).astype(jnp.int32), axis=1)
    own_live = (segment[:, None] == segment[None, :]) & (positions[None, :] <= positions[:, None])
    own_numer, own_top, own_total = attend_part(queries, keys_new, values_new, own_live, head_count)

    left_tag = read_tag(from_left)
    right_tag = read_tag(from_right)
    left_is_zero = left_tag[0] == 0
    left_rows = from_left[:NEWCAP]
    right_rows = from_right[:NEWCAP]
    query_stack = jnp.stack(
        [jnp.where(left_is_zero, left_rows, right_rows), jnp.where(left_is_zero, right_rows, left_rows)]
    )
    priors = jnp.stack(
        [jnp.where(left_is_zero, left_tag[1], right_tag[1]), jnp.where(left_is_zero, right_tag[1], left_tag[1])]
    )
    served = serve_slots(priors, query_stack, cache_keys, cache_values, head_count)
    back_left = jnp.where(left_is_zero, served[0], served[1])
    back_right = jnp.where(left_is_zero, served[1], served[0])
    got_right = shifted(back_left, "req", -1)
    got_left = shifted(back_right, "req", 1)

    def masked_rows(source, start, length):
        keep = (row_marks < length)[:, None]
        return jnp.where(keep, rows_of(source, start), jnp.zeros((), jnp.bfloat16))

    right_kv = jnp.stack(
        [masked_rows(keys_new, right_start, right_len), masked_rows(values_new, right_start, right_len)]
    )
    left_kv = jnp.stack(
        [masked_rows(keys_new, left_start, left_len), masked_rows(values_new, left_start, left_len)]
    )
    right_kv, left_kv, got_right, got_left = lax.optimization_barrier(
        (right_kv, left_kv, got_right, got_left)
    )
    from_left_kv = shifted(right_kv, "req", 1)
    from_right_kv = shifted(left_kv, "req", -1)

    def split_result(result):
        scaled = result[:, :feat_width]
        parts = result[:, feat_width : feat_width + 3 * head_count].astype(jnp.float32)
        log_total = (
            parts[:, :head_count]
            + parts[:, head_count : 2 * head_count]
            + parts[:, 2 * head_count : 3 * head_count]
        )
        return scaled, log_total

    got_right = split_result(got_right)
    got_left = split_result(got_left)

    def place(result, start, length):
        scaled, log_total = result
        shift = tok_count - start
        keep = ((positions - start >= 0) & (positions - start < length))[:, None]

        def moved(x):
            padded = jnp.pad(x, ((tok_count, tok_count - NEWCAP), (0, 0)))
            return lax.dynamic_slice_in_dim(padded, shift, tok_count, 0)

        return keep, moved(scaled), moved(log_total)

    keep_r, scaled_r, log_r = place(got_right, right_start, right_len)
    keep_l, scaled_l, log_l = place(got_left, left_start, left_len)
    prior_scaled = jnp.where(
        keep_r, scaled_r, jnp.where(keep_l, scaled_l, jnp.zeros((), jnp.bfloat16))
    ).astype(jnp.float32)
    prior_top = jnp.where(keep_r, log_r, jnp.where(keep_l, log_l, floor_value))
    prior_total = jnp.where(keep_r | keep_l, 1.0, 0.0)

    both_top = jnp.maximum(own_top, prior_top)
    own_scale = jnp.exp(own_top - both_top)
    prior_scale = jnp.exp(prior_top - both_top)
    denominator = own_total * own_scale + prior_total * prior_scale
    numerator = (
        own_numer.reshape(tok_count, head_count, HD) * own_scale[:, :, None]
        + prior_scaled.reshape(tok_count, head_count, HD) * prior_scale[:, :, None]
    )
    attended = (
        (numerator / denominator[:, :, None]).reshape(tok_count, feat_width).astype(jnp.bfloat16)
    )
    mixed = lax.psum_scatter(
        jnp.dot(attended, out_proj, preferred_element_type=jnp.float32).astype(jnp.bfloat16),
        "tp",
        scatter_dimension=0,
        tiled=True,
    )

    slot_ids = jnp.arange(slot_count, dtype=jnp.int32)

    def stored(from_left_rows, from_right_rows):
        at_left = (slot_ids == left_tag[0])[:, None, None]
        at_right = (slot_ids == right_tag[0])[:, None, None]
        return jnp.where(
            at_left,
            from_left_rows[None],
            jnp.where(at_right, from_right_rows[None], jnp.zeros((), jnp.bfloat16)),
        )

    new_keys = stored(from_left_kv[0], from_right_kv[0])
    new_values = stored(from_left_kv[1], from_right_kv[1])
    return (mixed, new_keys, new_values)


def solution(mesh):
    in_specs = (
        P("req", "tp"),
        P("req", "tp"),
        P("req", "tp"),
        P("req", None, "tp"),
        P("req", None, "tp"),
        P("tp", None),
        P("req", None),
        P("req", None),
        P("req", None),
        P("req", None),
    )
    out_specs = (P(("req", "tp"), None), P("req", None, "tp"), P("req", None, "tp"))
    return jax.shard_map(body, mesh=mesh, in_specs=in_specs, out_specs=out_specs, check_vma=False)
```

```python
import functools
import math

import jax
import jax.numpy as jnp
from jax import lax
from jax.experimental import pallas as pl
from jax.experimental.pallas import tpu as pltpu
from jax.sharding import PartitionSpec as P

HD = 224
NEWCAP = 192


floor_value = -1e30
TAG_ROWS = 8
RESULT_WIDTH = 1024


def shifted(value, axis, steps):
    count = lax.axis_size(axis)
    pairs = [(source, (source + steps) % count) for source in range(count)]
    return lax.ppermute(value, axis, pairs)


def attend_part(query_rows, key_rows, value_rows, live_mask, head_count):
    row_count = query_rows.shape[0]
    key_count = key_rows.shape[0]
    query_heads = query_rows.reshape(row_count, head_count, HD)
    key_heads = key_rows.reshape(key_count, head_count, HD)
    value_heads = value_rows.reshape(key_count, head_count, HD)
    scores = jnp.einsum(
        "thd,shd->hts", query_heads, key_heads, preferred_element_type=jnp.float32
    ) * (1.0 / math.sqrt(HD))
    scores = jnp.where(live_mask[None], scores, floor_value)
    row_top = jnp.max(scores, axis=2)
    weights = jnp.where(live_mask[None], jnp.exp(scores - row_top[:, :, None]), 0.0)
    row_total = jnp.sum(weights, axis=2)
    numerator = jnp.einsum(
        "hts,shd->thd",
        weights.astype(jnp.bfloat16),
        value_heads,
        preferred_element_type=jnp.float32,
    )
    return (numerator.reshape(row_count, head_count * HD), row_top.T, row_total.T)


def read_tag(bundle_ref):
    tag = bundle_ref[NEWCAP : NEWCAP + 1, :].astype(jnp.float32)
    lanes = lax.broadcasted_iota(jnp.int32, tag.shape, 1)

    def entry(i):
        return jnp.sum(jnp.where(lanes == i, tag, 0.0), axis=1, keepdims=True)

    return entry(0), entry(1) * 32 + entry(2)


def prior_kernel(head_count, left_ref, right_ref, key_ref, value_ref, out_ref, numer_ref):
    slot = pl.program_id(0)
    left_slot, left_prior = read_tag(left_ref)
    right_prior = read_tag(right_ref)[1]
    from_left = left_slot == slot.astype(jnp.float32)
    prior = jnp.where(from_left, left_prior, right_prior)
    row_count = NEWCAP
    feat_width = left_ref.shape[1]
    key_count = key_ref.shape[0]
    query_rows = jnp.where(from_left, left_ref[:NEWCAP, :], right_ref[:NEWCAP, :])
    live = lax.broadcasted_iota(jnp.int32, (1, key_count), 1).astype(jnp.float32) < prior
    tail_lanes = lax.broadcasted_iota(jnp.int32, (row_count, out_ref.shape[1] - feat_width), 1)
    tail = jnp.zeros((row_count, out_ref.shape[1] - feat_width), jnp.float32)
    numer_ref[...] = jnp.zeros((row_count, feat_width), jnp.float32)
    for h in range(head_count):
        low = (h * HD) // 128 * 128
        high = min(feat_width, -(-((h + 1) * HD) // 128) * 128)
        lanes = low + lax.broadcasted_iota(jnp.int32, (1, high - low), 1)
        in_head = (lanes >= h * HD) & (lanes < (h + 1) * HD)
        head_query = jnp.where(in_head, query_rows[:, low:high], jnp.zeros((), query_rows.dtype))
        scores = lax.dot_general(
            head_query, key_ref[:, low:high], (((1,), (1,)), ((), ())),
            preferred_element_type=jnp.float32,
        ) * (1.0 / math.sqrt(HD))
        scores = jnp.where(live, scores, floor_value)
        row_top = jnp.max(scores, axis=1, keepdims=True)
        weights = jnp.where(live, jnp.exp(scores - row_top), 0.0)
        row_total = jnp.sum(weights, axis=1, keepdims=True)
        head_out = jnp.dot(
            weights.astype(jnp.bfloat16), value_ref[:, low:high], preferred_element_type=jnp.float32
        )
        numer_ref[:, low:high] = numer_ref[:, low:high] + jnp.where(in_head, head_out / row_total, 0.0)
        log_total = row_top + jnp.log(row_total)
        for part in range(3):
            piece = log_total.astype(jnp.bfloat16).astype(jnp.float32)
            tail = jnp.where(tail_lanes == part * head_count + h, piece, tail)
            log_total = log_total - piece
    out_ref[:, :feat_width] = numer_ref[...].astype(out_ref.dtype)
    out_ref[:, feat_width:] = tail.astype(out_ref.dtype)


def serve_slots(from_left, from_right, cache_keys, cache_values, head_count):
    slot_count, key_count, feat_width = cache_keys.shape
    row_count = NEWCAP
    window_lanes = sum(
        min(feat_width, -(-((h + 1) * HD) // 128) * 128) - (h * HD) // 128 * 128
        for h in range(head_count)
    )
    flops = slot_count * 4 * row_count * key_count * window_lanes
    moved = (
        2 * (from_left.size + from_right.size + cache_keys.size + cache_values.size)
        + 2 * slot_count * row_count * RESULT_WIDTH
    )
    bundle_rows = from_left.shape[0]
    return pl.pallas_call(
        functools.partial(prior_kernel, head_count),
        out_shape=jax.ShapeDtypeStruct((slot_count, row_count, RESULT_WIDTH), jnp.bfloat16),
        grid=(slot_count,),
        in_specs=[
            pl.BlockSpec((bundle_rows, feat_width), lambda s: (0, 0)),
            pl.BlockSpec((bundle_rows, feat_width), lambda s: (0, 0)),
            pl.BlockSpec((None, key_count, feat_width), lambda s: (s, 0, 0)),
            pl.BlockSpec((None, key_count, feat_width), lambda s: (s, 0, 0)),
        ],
        out_specs=pl.BlockSpec((None, row_count, RESULT_WIDTH), lambda s: (s, 0, 0)),
        scratch_shapes=[pltpu.VMEM((row_count, feat_width), jnp.float32)],
        cost_estimate=pl.CostEstimate(
            flops=flops,
            transcendentals=slot_count * head_count * row_count * key_count,
            bytes_accessed=moved,
        ),
    )(from_left, from_right, cache_keys, cache_values)

def body(
    queries,
    keys_new,
    values_new,
    cache_keys,
    cache_values,
    out_proj,
    req_lengths,
    cache_owner,
    cache_slot,
    prior_len,
):
    tok_count = queries.shape[0]
    feat_width = queries.shape[1]
    head_count = feat_width // HD
    slot_count = cache_keys.shape[0]
    prior_rows = cache_keys.shape[1]
    req_lens = req_lengths[0]
    req_ends = jnp.cumsum(req_lens)
    positions = jnp.arange(tok_count, dtype=jnp.int32)
    row_marks = jnp.arange(NEWCAP, dtype=jnp.int32)
    prior_marks = jnp.arange(prior_rows, dtype=jnp.int32)
    req_count = lax.axis_size("req")
    req_index = lax.axis_index("req")

    first_right = cache_owner[0, 0] == (req_index + 1) % req_count

    def request_at(distance):
        pick = first_right if distance == 1 else jnp.logical_not(first_right)
        start = jnp.where(pick, 0, req_lens[0])
        length = jnp.where(pick, req_lens[0], req_lens[1])
        slot = jnp.where(pick, cache_slot[0, 0], cache_slot[0, 1])
        prior = jnp.where(pick, prior_len[0, 0], prior_len[0, 1])
        return start, length, slot, prior

    def rows_of(source, start):
        return lax.dynamic_slice_in_dim(source, start, NEWCAP, 0)

    def query_bundle(start, length, slot, prior):
        tag = jnp.stack([slot, prior // 32, prior % 32, length]).astype(jnp.bfloat16)
        tag_rows = jnp.zeros((TAG_ROWS, feat_width), jnp.bfloat16).at[0, :4].set(tag)
        return jnp.concatenate([rows_of(queries, start), tag_rows], axis=0)

    right_start, right_len, right_slot, right_prior = request_at(1)
    left_start, left_len, left_slot, left_prior = request_at(-1)

    from_left = shifted(query_bundle(right_start, right_len, right_slot, right_prior), "req", 1)
    from_right = shifted(query_bundle(left_start, left_len, left_slot, left_prior), "req", -1)

    served = serve_slots(from_left, from_right, cache_keys, cache_values, head_count)
    left_is_zero = from_left[NEWCAP, 0] == 0
    held_ends, served = lax.optimization_barrier((req_ends, served))
    segment = jnp.sum((positions[:, None] >= held_ends[None, :]).astype(jnp.int32), axis=1)
    own_live = (segment[:, None] == segment[None, :]) & (positions[None, :] <= positions[:, None])
    own_numer, own_top, own_total = attend_part(queries, keys_new, values_new, own_live, head_count)

    back_left = jnp.where(left_is_zero, served[0], served[1])
    back_right = jnp.where(left_is_zero, served[1], served[0])
    got_right = shifted(back_left, "req", -1)
    got_left = shifted(back_right, "req", 1)

    def masked_rows(source, start, length):
        keep = (row_marks < length)[:, None]
        return jnp.where(keep, rows_of(source, start), jnp.zeros((), jnp.bfloat16))

    right_kv = jnp.stack(
        [masked_rows(keys_new, right_start, right_len), masked_rows(values_new, right_start, right_len)]
    )
    left_kv = jnp.stack(
        [masked_rows(keys_new, left_start, left_len), masked_rows(values_new, left_start, left_len)]
    )
    right_kv, left_kv, got_right, got_left = lax.optimization_barrier(
        (right_kv, left_kv, got_right, got_left)
    )
    from_left_kv = shifted(right_kv, "req", 1)
    from_right_kv = shifted(left_kv, "req", -1)

    def split_result(result):
        scaled = result[:, :feat_width]
        parts = result[:, feat_width : feat_width + 3 * head_count].astype(jnp.float32)
        log_total = (
            parts[:, :head_count]
            + parts[:, head_count : 2 * head_count]
            + parts[:, 2 * head_count : 3 * head_count]
        )
        return scaled, log_total

    got_right = split_result(got_right)
    got_left = split_result(got_left)

    def place(result, start, length):
        scaled, log_total = result
        shift = tok_count - start
        keep = ((positions - start >= 0) & (positions - start < length))[:, None]

        def moved(x):
            padded = jnp.pad(x, ((tok_count, tok_count - NEWCAP), (0, 0)))
            return lax.dynamic_slice_in_dim(padded, shift, tok_count, 0)

        return keep, moved(scaled), moved(log_total)

    keep_r, scaled_r, log_r = place(got_right, right_start, right_len)
    keep_l, scaled_l, log_l = place(got_left, left_start, left_len)
    prior_scaled = jnp.where(
        keep_r, scaled_r, jnp.where(keep_l, scaled_l, jnp.zeros((), jnp.bfloat16))
    ).astype(jnp.float32)
    prior_top = jnp.where(keep_r, log_r, jnp.where(keep_l, log_l, floor_value))
    prior_total = jnp.where(keep_r | keep_l, 1.0, 0.0)

    both_top = jnp.maximum(own_top, prior_top)
    own_scale = jnp.exp(own_top - both_top)
    prior_scale = jnp.exp(prior_top - both_top)
    denominator = own_total * own_scale + prior_total * prior_scale
    numerator = (
        own_numer.reshape(tok_count, head_count, HD) * own_scale[:, :, None]
        + prior_scaled.reshape(tok_count, head_count, HD) * prior_scale[:, :, None]
    )
    attended = (
        (numerator / denominator[:, :, None]).reshape(tok_count, feat_width).astype(jnp.bfloat16)
    )
    mixed = lax.psum_scatter(
        jnp.dot(attended, out_proj, preferred_element_type=jnp.float32).astype(jnp.bfloat16),
        "tp",
        scatter_dimension=0,
        tiled=True,
    )

    slot_ids = jnp.arange(slot_count, dtype=jnp.int32)
    left_slot_id = from_left[NEWCAP, 0].astype(jnp.int32)
    right_slot_id = from_right[NEWCAP, 0].astype(jnp.int32)

    def stored(from_left_rows, from_right_rows):
        at_left = (slot_ids == left_slot_id)[:, None, None]
        at_right = (slot_ids == right_slot_id)[:, None, None]
        return jnp.where(
            at_left,
            from_left_rows[None],
            jnp.where(at_right, from_right_rows[None], jnp.zeros((), jnp.bfloat16)),
        )

    new_keys = stored(from_left_kv[0], from_right_kv[0])
    new_values = stored(from_left_kv[1], from_right_kv[1])
    return (mixed, new_keys, new_values)


def solution(mesh):
    in_specs = (
        P("req", "tp"),
        P("req", "tp"),
        P("req", "tp"),
        P("req", None, "tp"),
        P("req", None, "tp"),
        P("tp", None),
        P("req", None),
        P("req", None),
        P("req", None),
        P("req", None),
    )
    out_specs = (P(("req", "tp"), None), P("req", None, "tp"), P("req", None, "tp"))
    return jax.shard_map(body, mesh=mesh, in_specs=in_specs, out_specs=out_specs, check_vma=False)
```

```python
import functools
import math

import jax
import jax.numpy as jnp
from jax import lax
from jax.experimental import pallas as pl
from jax.experimental.pallas import tpu as pltpu
from jax.sharding import PartitionSpec as P

HD = 224
NEWCAP = 192


floor_value = -1e30
TAG_ROWS = 8
RESULT_WIDTH = 1024


def shifted(value, axis, steps):
    count = lax.axis_size(axis)
    pairs = [(source, (source + steps) % count) for source in range(count)]
    return lax.ppermute(value, axis, pairs)


def attend_part(query_rows, key_rows, value_rows, live_mask, head_count):
    row_count = query_rows.shape[0]
    key_count = key_rows.shape[0]
    query_heads = query_rows.reshape(row_count, head_count, HD)
    key_heads = key_rows.reshape(key_count, head_count, HD)
    value_heads = value_rows.reshape(key_count, head_count, HD)
    scores = jnp.einsum(
        "thd,shd->hts", query_heads, key_heads, preferred_element_type=jnp.float32
    ) * (1.0 / math.sqrt(HD))
    scores = jnp.where(live_mask[None], scores, floor_value)
    row_top = jnp.max(scores, axis=2)
    weights = jnp.where(live_mask[None], jnp.exp(scores - row_top[:, :, None]), 0.0)
    row_total = jnp.sum(weights, axis=2)
    numerator = jnp.einsum(
        "hts,shd->thd",
        weights.astype(jnp.bfloat16),
        value_heads,
        preferred_element_type=jnp.float32,
    )
    return (numerator.reshape(row_count, head_count * HD), row_top.T, row_total.T)


def read_tag(bundle_ref):
    tag = bundle_ref[NEWCAP : NEWCAP + 1, :].astype(jnp.float32)
    lanes = lax.broadcasted_iota(jnp.int32, tag.shape, 1)

    def entry(i):
        return jnp.sum(jnp.where(lanes == i, tag, 0.0), axis=1, keepdims=True)

    return entry(0), entry(1) * 32 + entry(2)


def prior_kernel(head_count, left_ref, right_ref, key_ref, value_ref, to_left_ref, to_right_ref, numer_ref):
    slot = pl.program_id(0)
    left_slot, left_prior = read_tag(left_ref)
    right_prior = read_tag(right_ref)[1]
    from_left = left_slot == slot.astype(jnp.float32)
    prior = jnp.where(from_left, left_prior, right_prior)
    row_count = NEWCAP
    feat_width = left_ref.shape[1]
    key_count = key_ref.shape[0]
    query_rows = jnp.where(from_left, left_ref[:NEWCAP, :], right_ref[:NEWCAP, :])
    live = lax.broadcasted_iota(jnp.int32, (1, key_count), 1).astype(jnp.float32) < prior
    result_width = to_left_ref.shape[1]
    tail_lanes = lax.broadcasted_iota(jnp.int32, (row_count, result_width - feat_width), 1)
    tail = jnp.zeros((row_count, result_width - feat_width), jnp.float32)
    numer_ref[...] = jnp.zeros((row_count, feat_width), jnp.float32)
    for h in range(head_count):
        low = (h * HD) // 128 * 128
        high = min(feat_width, -(-((h + 1) * HD) // 128) * 128)
        lanes = low + lax.broadcasted_iota(jnp.int32, (1, high - low), 1)
        in_head = (lanes >= h * HD) & (lanes < (h + 1) * HD)
        head_query = jnp.where(in_head, query_rows[:, low:high], jnp.zeros((), query_rows.dtype))
        scores = lax.dot_general(
            head_query, key_ref[:, low:high], (((1,), (1,)), ((), ())),
            preferred_element_type=jnp.float32,
        ) * (1.0 / math.sqrt(HD))
        scores = jnp.where(live, scores, floor_value)
        row_top = jnp.max(scores, axis=1, keepdims=True)
        weights = jnp.where(live, jnp.exp(scores - row_top), 0.0)
        row_total = jnp.sum(weights, axis=1, keepdims=True)
        head_out = jnp.dot(
            weights.astype(jnp.bfloat16), value_ref[:, low:high], preferred_element_type=jnp.float32
        )
        numer_ref[:, low:high] = numer_ref[:, low:high] + jnp.where(in_head, head_out / row_total, 0.0)
        log_total = row_top + jnp.log(row_total)
        for part in range(3):
            piece = log_total.astype(jnp.bfloat16).astype(jnp.float32)
            tail = jnp.where(tail_lanes == part * head_count + h, piece, tail)
            log_total = log_total - piece
    for side_ref, mine in ((to_left_ref, from_left), (to_right_ref, jnp.logical_not(from_left))):
        side_ref[:, :feat_width] = jnp.where(
            mine, numer_ref[...].astype(side_ref.dtype), side_ref[:, :feat_width]
        )
        side_ref[:, feat_width:] = jnp.where(
            mine, tail.astype(side_ref.dtype), side_ref[:, feat_width:]
        )


def serve_slots(from_left, from_right, cache_keys, cache_values, head_count):
    slot_count, key_count, feat_width = cache_keys.shape
    row_count = NEWCAP
    window_lanes = sum(
        min(feat_width, -(-((h + 1) * HD) // 128) * 128) - (h * HD) // 128 * 128
        for h in range(head_count)
    )
    flops = slot_count * 4 * row_count * key_count * window_lanes
    moved = (
        2 * (from_left.size + from_right.size + cache_keys.size + cache_values.size)
        + 2 * slot_count * row_count * RESULT_WIDTH
    )
    bundle_rows = from_left.shape[0]
    return pl.pallas_call(
        functools.partial(prior_kernel, head_count),
        out_shape=(
            jax.ShapeDtypeStruct((row_count, RESULT_WIDTH), jnp.bfloat16),
            jax.ShapeDtypeStruct((row_count, RESULT_WIDTH), jnp.bfloat16),
        ),
        grid=(slot_count,),
        in_specs=[
            pl.BlockSpec((bundle_rows, feat_width), lambda s: (0, 0)),
            pl.BlockSpec((bundle_rows, feat_width), lambda s: (0, 0)),
            pl.BlockSpec((None, key_count, feat_width), lambda s: (s, 0, 0)),
            pl.BlockSpec((None, key_count, feat_width), lambda s: (s, 0, 0)),
        ],
        out_specs=(
            pl.BlockSpec((row_count, RESULT_WIDTH), lambda s: (0, 0)),
            pl.BlockSpec((row_count, RESULT_WIDTH), lambda s: (0, 0)),
        ),
        scratch_shapes=[pltpu.VMEM((row_count, feat_width), jnp.float32)],
        cost_estimate=pl.CostEstimate(
            flops=flops,
            transcendentals=slot_count * head_count * row_count * key_count,
            bytes_accessed=moved,
        ),
    )(from_left, from_right, cache_keys, cache_values)

def body(
    queries,
    keys_new,
    values_new,
    cache_keys,
    cache_values,
    out_proj,
    req_lengths,
    cache_owner,
    cache_slot,
    prior_len,
):
    tok_count = queries.shape[0]
    feat_width = queries.shape[1]
    head_count = feat_width // HD
    slot_count = cache_keys.shape[0]
    prior_rows = cache_keys.shape[1]
    req_lens = req_lengths[0]
    req_ends = jnp.cumsum(req_lens)
    positions = jnp.arange(tok_count, dtype=jnp.int32)
    row_marks = jnp.arange(NEWCAP, dtype=jnp.int32)
    prior_marks = jnp.arange(prior_rows, dtype=jnp.int32)
    req_count = lax.axis_size("req")
    req_index = lax.axis_index("req")

    first_right = cache_owner[0, 0] == (req_index + 1) % req_count

    def request_at(distance):
        pick = first_right if distance == 1 else jnp.logical_not(first_right)
        start = jnp.where(pick, 0, req_lens[0])
        length = jnp.where(pick, req_lens[0], req_lens[1])
        slot = jnp.where(pick, cache_slot[0, 0], cache_slot[0, 1])
        prior = jnp.where(pick, prior_len[0, 0], prior_len[0, 1])
        return start, length, slot, prior

    def rows_of(source, start):
        return lax.dynamic_slice_in_dim(source, start, NEWCAP, 0)

    def query_bundle(start, length, slot, prior):
        tag = jnp.stack([slot, prior // 32, prior % 32, length]).astype(jnp.bfloat16)
        tag_rows = jnp.zeros((TAG_ROWS, feat_width), jnp.bfloat16).at[0, :4].set(tag)
        return jnp.concatenate([rows_of(queries, start), tag_rows], axis=0)

    right_start, right_len, right_slot, right_prior = request_at(1)
    left_start, left_len, left_slot, left_prior = request_at(-1)

    from_left = shifted(query_bundle(right_start, right_len, right_slot, right_prior), "req", 1)
    from_right = shifted(query_bundle(left_start, left_len, left_slot, left_prior), "req", -1)

    served = serve_slots(from_left, from_right, cache_keys, cache_values, head_count)
    held_ends, served = lax.optimization_barrier((req_ends, served))
    segment = jnp.sum((positions[:, None] >= held_ends[None, :]).astype(jnp.int32), axis=1)
    own_live = (segment[:, None] == segment[None, :]) & (positions[None, :] <= positions[:, None])
    own_numer, own_top, own_total = attend_part(queries, keys_new, values_new, own_live, head_count)

    back_left, back_right = served
    got_right = shifted(back_left, "req", -1)
    got_left = shifted(back_right, "req", 1)

    def masked_rows(source, start, length):
        keep = (row_marks < length)[:, None]
        return jnp.where(keep, rows_of(source, start), jnp.zeros((), jnp.bfloat16))

    right_kv = jnp.stack(
        [masked_rows(keys_new, right_start, right_len), masked_rows(values_new, right_start, right_len)]
    )
    left_kv = jnp.stack(
        [masked_rows(keys_new, left_start, left_len), masked_rows(values_new, left_start, left_len)]
    )
    right_kv, left_kv, got_right, got_left = lax.optimization_barrier(
        (right_kv, left_kv, got_right, got_left)
    )
    from_left_kv = shifted(right_kv, "req", 1)
    from_right_kv = shifted(left_kv, "req", -1)

    def split_result(result):
        scaled = result[:, :feat_width]
        parts = result[:, feat_width : feat_width + 3 * head_count].astype(jnp.float32)
        log_total = (
            parts[:, :head_count]
            + parts[:, head_count : 2 * head_count]
            + parts[:, 2 * head_count : 3 * head_count]
        )
        return scaled, log_total

    got_right = split_result(got_right)
    got_left = split_result(got_left)

    def place(result, start, length):
        scaled, log_total = result
        shift = tok_count - start
        keep = ((positions - start >= 0) & (positions - start < length))[:, None]

        def moved(x):
            padded = jnp.pad(x, ((tok_count, tok_count - NEWCAP), (0, 0)))
            return lax.dynamic_slice_in_dim(padded, shift, tok_count, 0)

        return keep, moved(scaled), moved(log_total)

    keep_r, scaled_r, log_r = place(got_right, right_start, right_len)
    keep_l, scaled_l, log_l = place(got_left, left_start, left_len)
    prior_scaled = jnp.where(
        keep_r, scaled_r, jnp.where(keep_l, scaled_l, jnp.zeros((), jnp.bfloat16))
    ).astype(jnp.float32)
    prior_top = jnp.where(keep_r, log_r, jnp.where(keep_l, log_l, floor_value))
    prior_total = jnp.where(keep_r | keep_l, 1.0, 0.0)

    both_top = jnp.maximum(own_top, prior_top)
    own_scale = jnp.exp(own_top - both_top)
    prior_scale = jnp.exp(prior_top - both_top)
    denominator = own_total * own_scale + prior_total * prior_scale
    numerator = (
        own_numer.reshape(tok_count, head_count, HD) * own_scale[:, :, None]
        + prior_scaled.reshape(tok_count, head_count, HD) * prior_scale[:, :, None]
    )
    attended = (
        (numerator / denominator[:, :, None]).reshape(tok_count, feat_width).astype(jnp.bfloat16)
    )
    mixed = lax.psum_scatter(
        jnp.dot(attended, out_proj, preferred_element_type=jnp.float32).astype(jnp.bfloat16),
        "tp",
        scatter_dimension=0,
        tiled=True,
    )

    slot_ids = jnp.arange(slot_count, dtype=jnp.int32)
    left_slot_id = from_left[NEWCAP, 0].astype(jnp.int32)
    right_slot_id = from_right[NEWCAP, 0].astype(jnp.int32)

    def stored(from_left_rows, from_right_rows):
        at_left = (slot_ids == left_slot_id)[:, None, None]
        at_right = (slot_ids == right_slot_id)[:, None, None]
        return jnp.where(
            at_left,
            from_left_rows[None],
            jnp.where(at_right, from_right_rows[None], jnp.zeros((), jnp.bfloat16)),
        )

    new_keys = stored(from_left_kv[0], from_right_kv[0])
    new_values = stored(from_left_kv[1], from_right_kv[1])
    return (mixed, new_keys, new_values)


def solution(mesh):
    in_specs = (
        P("req", "tp"),
        P("req", "tp"),
        P("req", "tp"),
        P("req", None, "tp"),
        P("req", None, "tp"),
        P("tp", None),
        P("req", None),
        P("req", None),
        P("req", None),
        P("req", None),
    )
    out_specs = (P(("req", "tp"), None), P("req", None, "tp"), P("req", None, "tp"))
    return jax.shard_map(body, mesh=mesh, in_specs=in_specs, out_specs=out_specs, check_vma=False)
```

```python
import functools
import math

import jax
import jax.numpy as jnp
from jax import lax
from jax.experimental import pallas as pl
from jax.experimental.pallas import tpu as pltpu
from jax.sharding import PartitionSpec as P

HD = 224
NEWCAP = 192


floor_value = -1e30
TAG_ROWS = 8
RESULT_WIDTH = 1024


def shifted(value, axis, steps):
    count = lax.axis_size(axis)
    pairs = [(source, (source + steps) % count) for source in range(count)]
    return lax.ppermute(value, axis, pairs)


def attend_part(query_rows, key_rows, value_rows, live_mask, head_count):
    row_count = query_rows.shape[0]
    key_count = key_rows.shape[0]
    query_heads = query_rows.reshape(row_count, head_count, HD)
    key_heads = key_rows.reshape(key_count, head_count, HD)
    value_heads = value_rows.reshape(key_count, head_count, HD)
    scores = jnp.einsum(
        "thd,shd->hts", query_heads, key_heads, preferred_element_type=jnp.float32
    ) * (1.0 / math.sqrt(HD))
    scores = jnp.where(live_mask[None], scores, floor_value)
    row_top = jnp.max(scores, axis=2)
    weights = jnp.where(live_mask[None], jnp.exp(scores - row_top[:, :, None]), 0.0)
    row_total = jnp.sum(weights, axis=2)
    numerator = jnp.einsum(
        "hts,shd->thd",
        weights.astype(jnp.bfloat16),
        value_heads,
        preferred_element_type=jnp.float32,
    )
    return (numerator.reshape(row_count, head_count * HD), row_top.T, row_total.T)


def read_tag(bundle_ref):
    tag = bundle_ref[NEWCAP : NEWCAP + 1, :].astype(jnp.float32)
    lanes = lax.broadcasted_iota(jnp.int32, tag.shape, 1)

    def entry(i):
        return jnp.sum(jnp.where(lanes == i, tag, 0.0), axis=1, keepdims=True)

    return entry(0), entry(1) * 32 + entry(2)


def prior_kernel(head_count, left_ref, right_ref, key_ref, value_ref, to_left_ref, to_right_ref, numer_ref):
    slot = pl.program_id(0)
    left_slot, left_prior = read_tag(left_ref)
    right_prior = read_tag(right_ref)[1]
    from_left = left_slot == slot.astype(jnp.float32)
    prior = jnp.where(from_left, left_prior, right_prior)
    row_count = NEWCAP
    feat_width = left_ref.shape[1]
    key_count = key_ref.shape[0]
    query_rows = jnp.where(from_left, left_ref[:NEWCAP, :], right_ref[:NEWCAP, :])
    live = lax.broadcasted_iota(jnp.int32, (1, key_count), 1).astype(jnp.float32) < prior
    result_width = to_left_ref.shape[1]
    tail_lanes = lax.broadcasted_iota(jnp.int32, (row_count, result_width - feat_width), 1)
    tail = jnp.zeros((row_count, result_width - feat_width), jnp.float32)
    numer_ref[...] = jnp.zeros((row_count, feat_width), jnp.float32)
    for h in range(head_count):
        low = (h * HD) // 128 * 128
        high = min(feat_width, -(-((h + 1) * HD) // 128) * 128)
        lanes = low + lax.broadcasted_iota(jnp.int32, (1, high - low), 1)
        in_head = (lanes >= h * HD) & (lanes < (h + 1) * HD)
        head_query = jnp.where(in_head, query_rows[:, low:high], jnp.zeros((), query_rows.dtype))
        scores = lax.dot_general(
            head_query, key_ref[:, low:high], (((1,), (1,)), ((), ())),
            preferred_element_type=jnp.float32,
        ) * (1.0 / math.sqrt(HD))
        scores = jnp.where(live, scores, floor_value)
        row_top = jnp.max(scores, axis=1, keepdims=True)
        weights = jnp.where(live, jnp.exp(scores - row_top), 0.0)
        row_total = jnp.sum(weights, axis=1, keepdims=True)
        head_out = jnp.dot(
            weights.astype(jnp.bfloat16), value_ref[:, low:high], preferred_element_type=jnp.float32
        )
        numer_ref[:, low:high] = numer_ref[:, low:high] + jnp.where(in_head, head_out / row_total, 0.0)
        log_total = row_top + jnp.log(row_total)
        for part in range(3):
            piece = log_total.astype(jnp.bfloat16).astype(jnp.float32)
            tail = jnp.where(tail_lanes == part * head_count + h, piece, tail)
            log_total = log_total - piece
    for side_ref, mine in ((to_left_ref, from_left), (to_right_ref, jnp.logical_not(from_left))):
        side_ref[:, :feat_width] = jnp.where(
            mine, numer_ref[...].astype(side_ref.dtype), side_ref[:, :feat_width]
        )
        side_ref[:, feat_width:] = jnp.where(
            mine, tail.astype(side_ref.dtype), side_ref[:, feat_width:]
        )


def serve_slots(from_left, from_right, cache_keys, cache_values, head_count):
    slot_count, key_count, feat_width = cache_keys.shape
    row_count = NEWCAP
    window_lanes = sum(
        min(feat_width, -(-((h + 1) * HD) // 128) * 128) - (h * HD) // 128 * 128
        for h in range(head_count)
    )
    flops = slot_count * 4 * row_count * key_count * window_lanes
    moved = (
        2 * (from_left.size + from_right.size + cache_keys.size + cache_values.size)
        + 2 * slot_count * row_count * RESULT_WIDTH
    )
    bundle_rows = from_left.shape[0]
    return pl.pallas_call(
        functools.partial(prior_kernel, head_count),
        out_shape=(
            jax.ShapeDtypeStruct((row_count, RESULT_WIDTH), jnp.bfloat16),
            jax.ShapeDtypeStruct((row_count, RESULT_WIDTH), jnp.bfloat16),
        ),
        grid=(slot_count,),
        in_specs=[
            pl.BlockSpec((bundle_rows, feat_width), lambda s: (0, 0)),
            pl.BlockSpec((bundle_rows, feat_width), lambda s: (0, 0)),
            pl.BlockSpec((None, key_count, feat_width), lambda s: (s, 0, 0)),
            pl.BlockSpec((None, key_count, feat_width), lambda s: (s, 0, 0)),
        ],
        out_specs=(
            pl.BlockSpec((row_count, RESULT_WIDTH), lambda s: (0, 0)),
            pl.BlockSpec((row_count, RESULT_WIDTH), lambda s: (0, 0)),
        ),
        scratch_shapes=[pltpu.VMEM((row_count, feat_width), jnp.float32)],
        cost_estimate=pl.CostEstimate(
            flops=flops,
            transcendentals=slot_count * head_count * row_count * key_count,
            bytes_accessed=moved,
        ),
    )(from_left, from_right, cache_keys, cache_values)

def body(
    queries,
    keys_new,
    values_new,
    cache_keys,
    cache_values,
    out_proj,
    req_lengths,
    cache_owner,
    cache_slot,
    prior_len,
):
    tok_count = queries.shape[0]
    feat_width = queries.shape[1]
    head_count = feat_width // HD
    slot_count = cache_keys.shape[0]
    prior_rows = cache_keys.shape[1]
    req_lens = req_lengths[0]
    req_ends = jnp.cumsum(req_lens)
    positions = jnp.arange(tok_count, dtype=jnp.int32)
    row_marks = jnp.arange(NEWCAP, dtype=jnp.int32)
    prior_marks = jnp.arange(prior_rows, dtype=jnp.int32)
    req_count = lax.axis_size("req")
    req_index = lax.axis_index("req")

    first_right = cache_owner[0, 0] == (req_index + 1) % req_count

    def request_at(distance):
        pick = first_right if distance == 1 else jnp.logical_not(first_right)
        start = jnp.where(pick, 0, req_lens[0])
        length = jnp.where(pick, req_lens[0], req_lens[1])
        slot = jnp.where(pick, cache_slot[0, 0], cache_slot[0, 1])
        prior = jnp.where(pick, prior_len[0, 0], prior_len[0, 1])
        return start, length, slot, prior

    def rows_of(source, start):
        return lax.dynamic_slice_in_dim(source, start, NEWCAP, 0)

    def query_bundle(start, length, slot, prior):
        tag = jnp.stack([slot, prior // 32, prior % 32, length]).astype(jnp.bfloat16)
        tag_rows = jnp.zeros((TAG_ROWS, feat_width), jnp.bfloat16).at[0, :4].set(tag)
        return jnp.concatenate([rows_of(queries, start), tag_rows], axis=0)

    right_start, right_len, right_slot, right_prior = request_at(1)
    left_start, left_len, left_slot, left_prior = request_at(-1)

    from_left = shifted(query_bundle(right_start, right_len, right_slot, right_prior), "req", 1)
    from_right = shifted(query_bundle(left_start, left_len, left_slot, left_prior), "req", -1)

    served = serve_slots(from_left, from_right, cache_keys, cache_values, head_count)
    held_ends, served = lax.optimization_barrier((req_ends, served))
    segment = jnp.sum((positions[:, None] >= held_ends[None, :]).astype(jnp.int32), axis=1)
    own_live = (segment[:, None] == segment[None, :]) & (positions[None, :] <= positions[:, None])
    own_numer, own_top, own_total = attend_part(queries, keys_new, values_new, own_live, head_count)

    back_left, back_right = served
    got_right = shifted(back_left, "req", -1)
    got_left = shifted(back_right, "req", 1)

    def masked_rows(source, start, length):
        keep = (row_marks < length)[:, None]
        return jnp.where(keep, rows_of(source, start), jnp.zeros((), jnp.bfloat16))

    right_kv = jnp.stack(
        [masked_rows(keys_new, right_start, right_len), masked_rows(values_new, right_start, right_len)]
    )
    left_kv = jnp.stack(
        [masked_rows(keys_new, left_start, left_len), masked_rows(values_new, left_start, left_len)]
    )
    right_kv, left_kv, got_right, got_left = lax.optimization_barrier(
        (right_kv, left_kv, got_right, got_left)
    )
    from_left_kv = shifted(right_kv, "req", 1)
    from_right_kv = shifted(left_kv, "req", -1)

    (own_numer, own_top, own_total), got_right, got_left = lax.optimization_barrier(
        ((own_numer, own_top, own_total), got_right, got_left)
    )

    def place(result, start, length):
        shift = tok_count - start
        keep = ((positions - start >= 0) & (positions - start < length))[:, None]
        padded = jnp.pad(result, ((tok_count, tok_count - NEWCAP), (0, 0)))
        moved = lax.dynamic_slice_in_dim(padded, shift, tok_count, 0)
        return keep, moved

    keep_r, moved_r = place(got_right, right_start, right_len)
    keep_l, moved_l = place(got_left, left_start, left_len)
    prior = jnp.where(keep_r, moved_r, jnp.where(keep_l, moved_l, jnp.zeros((), moved_r.dtype)))
    prior_scaled = prior[:, :feat_width].astype(jnp.float32)
    parts = prior[:, feat_width : feat_width + 3 * head_count].astype(jnp.float32)
    log_total = (
        parts[:, :head_count] + parts[:, head_count : 2 * head_count] + parts[:, 2 * head_count :]
    )
    has_prior = keep_r | keep_l
    prior_top = jnp.where(has_prior, log_total, floor_value)
    prior_total = jnp.where(has_prior, 1.0, 0.0)

    both_top = jnp.maximum(own_top, prior_top)
    own_scale = jnp.exp(own_top - both_top)
    prior_scale = jnp.exp(prior_top - both_top)
    denominator = own_total * own_scale + prior_total * prior_scale
    numerator = (
        own_numer.reshape(tok_count, head_count, HD) * own_scale[:, :, None]
        + prior_scaled.reshape(tok_count, head_count, HD) * prior_scale[:, :, None]
    )
    attended = (
        (numerator / denominator[:, :, None]).reshape(tok_count, feat_width).astype(jnp.bfloat16)
    )
    mixed = lax.psum_scatter(
        jnp.dot(attended, out_proj, preferred_element_type=jnp.float32).astype(jnp.bfloat16),
        "tp",
        scatter_dimension=0,
        tiled=True,
    )

    slot_ids = jnp.arange(slot_count, dtype=jnp.int32)
    left_slot_id = from_left[NEWCAP, 0].astype(jnp.int32)
    right_slot_id = from_right[NEWCAP, 0].astype(jnp.int32)

    def stored(from_left_rows, from_right_rows):
        at_left = (slot_ids == left_slot_id)[:, None, None]
        at_right = (slot_ids == right_slot_id)[:, None, None]
        return jnp.where(
            at_left,
            from_left_rows[None],
            jnp.where(at_right, from_right_rows[None], jnp.zeros((), jnp.bfloat16)),
        )

    new_keys = stored(from_left_kv[0], from_right_kv[0])
    new_values = stored(from_left_kv[1], from_right_kv[1])
    return (mixed, new_keys, new_values)


def solution(mesh):
    in_specs = (
        P("req", "tp"),
        P("req", "tp"),
        P("req", "tp"),
        P("req", None, "tp"),
        P("req", None, "tp"),
        P("tp", None),
        P("req", None),
        P("req", None),
        P("req", None),
        P("req", None),
    )
    out_specs = (P(("req", "tp"), None), P("req", None, "tp"), P("req", None, "tp"))
    return jax.shard_map(body, mesh=mesh, in_specs=in_specs, out_specs=out_specs, check_vma=False)
```

```python
import functools
import math

import jax
import jax.numpy as jnp
from jax import lax
from jax.experimental import pallas as pl
from jax.experimental.pallas import tpu as pltpu
from jax.sharding import PartitionSpec as P

HD = 224
NEWCAP = 192


floor_value = -1e30
TAG_ROWS = 8
RESULT_WIDTH = 1024


def shifted(value, axis, steps):
    count = lax.axis_size(axis)
    pairs = [(source, (source + steps) % count) for source in range(count)]
    return lax.ppermute(value, axis, pairs)


def attend_part(query_rows, key_rows, value_rows, live_mask, head_count):
    row_count = query_rows.shape[0]
    key_count = key_rows.shape[0]
    query_heads = query_rows.reshape(row_count, head_count, HD)
    key_heads = key_rows.reshape(key_count, head_count, HD)
    value_heads = value_rows.reshape(key_count, head_count, HD)
    scores = jnp.einsum(
        "thd,shd->hts", query_heads, key_heads, preferred_element_type=jnp.float32
    ) * (1.0 / math.sqrt(HD))
    scores = jnp.where(live_mask[None], scores, floor_value)
    row_top = jnp.max(scores, axis=2)
    weights = jnp.where(live_mask[None], jnp.exp(scores - row_top[:, :, None]), 0.0)
    row_total = jnp.sum(weights, axis=2)
    numerator = jnp.einsum(
        "hts,shd->thd",
        weights.astype(jnp.bfloat16),
        value_heads,
        preferred_element_type=jnp.float32,
    )
    return (numerator.reshape(row_count, head_count * HD), row_top.T, row_total.T)


def read_tag(bundle_ref):
    tag = bundle_ref[NEWCAP : NEWCAP + 1, :].astype(jnp.float32)
    lanes = lax.broadcasted_iota(jnp.int32, tag.shape, 1)

    def entry(i):
        return jnp.sum(jnp.where(lanes == i, tag, 0.0), axis=1, keepdims=True)

    return entry(0), entry(1) * 32 + entry(2)


def prior_kernel(head_count, left_ref, right_ref, key_ref, value_ref, to_left_ref, to_right_ref, numer_ref):
    slot = pl.program_id(0)
    left_slot, left_prior = read_tag(left_ref)
    right_prior = read_tag(right_ref)[1]
    from_left = left_slot == slot.astype(jnp.float32)
    prior = jnp.where(from_left, left_prior, right_prior)
    row_count = NEWCAP
    feat_width = left_ref.shape[1]
    key_count = key_ref.shape[0]
    query_rows = jnp.where(from_left, left_ref[:NEWCAP, :], right_ref[:NEWCAP, :])
    live = lax.broadcasted_iota(jnp.int32, (1, key_count), 1).astype(jnp.float32) < prior
    result_width = to_left_ref.shape[1]
    tail_lanes = lax.broadcasted_iota(jnp.int32, (row_count, result_width - feat_width), 1)
    tail = jnp.zeros((row_count, result_width - feat_width), jnp.float32)
    numer_ref[...] = jnp.zeros((row_count, feat_width), jnp.float32)
    for h in range(head_count):
        low = (h * HD) // 128 * 128
        high = min(feat_width, -(-((h + 1) * HD) // 128) * 128)
        lanes = low + lax.broadcasted_iota(jnp.int32, (1, high - low), 1)
        in_head = (lanes >= h * HD) & (lanes < (h + 1) * HD)
        head_query = jnp.where(in_head, query_rows[:, low:high], jnp.zeros((), query_rows.dtype))
        scores = lax.dot_general(
            head_query, key_ref[:, low:high], (((1,), (1,)), ((), ())),
            preferred_element_type=jnp.float32,
        ) * (1.0 / math.sqrt(HD))
        scores = jnp.where(live, scores, floor_value)
        row_top = jnp.max(scores, axis=1, keepdims=True)
        weights = jnp.where(live, jnp.exp(scores - row_top), 0.0)
        row_total = jnp.sum(weights, axis=1, keepdims=True)
        head_out = jnp.dot(
            weights.astype(jnp.bfloat16), value_ref[:, low:high], preferred_element_type=jnp.float32
        )
        numer_ref[:, low:high] = numer_ref[:, low:high] + jnp.where(in_head, head_out / row_total, 0.0)
        log_total = row_top + jnp.log(row_total)
        for part in range(3):
            piece = log_total.astype(jnp.bfloat16).astype(jnp.float32)
            tail = jnp.where(tail_lanes == part * head_count + h, piece, tail)
            log_total = log_total - piece
    for side_ref, mine in ((to_left_ref, from_left), (to_right_ref, jnp.logical_not(from_left))):
        side_ref[:, :feat_width] = jnp.where(
            mine, numer_ref[...].astype(side_ref.dtype), side_ref[:, :feat_width]
        )
        side_ref[:, feat_width:] = jnp.where(
            mine, tail.astype(side_ref.dtype), side_ref[:, feat_width:]
        )


def serve_slots(from_left, from_right, cache_keys, cache_values, head_count):
    slot_count, key_count, feat_width = cache_keys.shape
    row_count = NEWCAP
    window_lanes = sum(
        min(feat_width, -(-((h + 1) * HD) // 128) * 128) - (h * HD) // 128 * 128
        for h in range(head_count)
    )
    flops = slot_count * 4 * row_count * key_count * window_lanes
    moved = (
        2 * (from_left.size + from_right.size + cache_keys.size + cache_values.size)
        + 2 * slot_count * row_count * RESULT_WIDTH
    )
    bundle_rows = from_left.shape[0]
    return pl.pallas_call(
        functools.partial(prior_kernel, head_count),
        out_shape=(
            jax.ShapeDtypeStruct((row_count, RESULT_WIDTH), jnp.bfloat16),
            jax.ShapeDtypeStruct((row_count, RESULT_WIDTH), jnp.bfloat16),
        ),
        grid=(slot_count,),
        in_specs=[
            pl.BlockSpec((bundle_rows, feat_width), lambda s: (0, 0)),
            pl.BlockSpec((bundle_rows, feat_width), lambda s: (0, 0)),
            pl.BlockSpec((None, key_count, feat_width), lambda s: (s, 0, 0)),
            pl.BlockSpec((None, key_count, feat_width), lambda s: (s, 0, 0)),
        ],
        out_specs=(
            pl.BlockSpec((row_count, RESULT_WIDTH), lambda s: (0, 0)),
            pl.BlockSpec((row_count, RESULT_WIDTH), lambda s: (0, 0)),
        ),
        scratch_shapes=[pltpu.VMEM((row_count, feat_width), jnp.float32)],
        cost_estimate=pl.CostEstimate(
            flops=flops,
            transcendentals=slot_count * head_count * row_count * key_count,
            bytes_accessed=moved,
        ),
    )(from_left, from_right, cache_keys, cache_values)

def body(
    queries,
    keys_new,
    values_new,
    cache_keys,
    cache_values,
    out_proj,
    req_lengths,
    cache_owner,
    cache_slot,
    prior_len,
):
    tok_count = queries.shape[0]
    feat_width = queries.shape[1]
    head_count = feat_width // HD
    slot_count = cache_keys.shape[0]
    prior_rows = cache_keys.shape[1]
    req_lens = req_lengths[0]
    req_ends = jnp.cumsum(req_lens)
    positions = jnp.arange(tok_count, dtype=jnp.int32)
    row_marks = jnp.arange(NEWCAP, dtype=jnp.int32)
    prior_marks = jnp.arange(prior_rows, dtype=jnp.int32)
    req_count = lax.axis_size("req")
    req_index = lax.axis_index("req")

    first_right = cache_owner[0, 0] == (req_index + 1) % req_count

    def request_at(distance):
        pick = first_right if distance == 1 else jnp.logical_not(first_right)
        start = jnp.where(pick, 0, req_lens[0])
        length = jnp.where(pick, req_lens[0], req_lens[1])
        slot = jnp.where(pick, cache_slot[0, 0], cache_slot[0, 1])
        prior = jnp.where(pick, prior_len[0, 0], prior_len[0, 1])
        return start, length, slot, prior

    def rows_of(source, start):
        return lax.dynamic_slice_in_dim(source, start, NEWCAP, 0)

    def query_bundle(start, length, slot, prior):
        tag = jnp.stack([slot, prior // 32, prior % 32, length]).astype(jnp.bfloat16)
        tag_rows = jnp.zeros((TAG_ROWS, feat_width), jnp.bfloat16).at[0, :4].set(tag)
        return jnp.concatenate([rows_of(queries, start), tag_rows], axis=0)

    right_start, right_len, right_slot, right_prior = request_at(1)
    left_start, left_len, left_slot, left_prior = request_at(-1)

    from_left = shifted(query_bundle(right_start, right_len, right_slot, right_prior), "req", 1)
    from_right = shifted(query_bundle(left_start, left_len, left_slot, left_prior), "req", -1)

    served = serve_slots(from_left, from_right, cache_keys, cache_values, head_count)
    held_ends, served = lax.optimization_barrier((req_ends, served))
    segment = jnp.sum((positions[:, None] >= held_ends[None, :]).astype(jnp.int32), axis=1)
    own_live = (segment[:, None] == segment[None, :]) & (positions[None, :] <= positions[:, None])
    own_numer, own_top, own_total = attend_part(queries, keys_new, values_new, own_live, head_count)

    back_left, back_right = served
    got_right = shifted(back_left, "req", -1)
    got_left = shifted(back_right, "req", 1)

    def masked_rows(source, start, length):
        keep = (row_marks < length)[:, None]
        return jnp.where(keep, rows_of(source, start), jnp.zeros((), jnp.bfloat16))

    right_kv = jnp.stack(
        [masked_rows(keys_new, right_start, right_len), masked_rows(values_new, right_start, right_len)]
    )
    left_kv = jnp.stack(
        [masked_rows(keys_new, left_start, left_len), masked_rows(values_new, left_start, left_len)]
    )
    right_kv, left_kv, got_right, got_left = lax.optimization_barrier(
        (right_kv, left_kv, got_right, got_left)
    )
    from_left_kv = shifted(right_kv, "req", 1)
    from_right_kv = shifted(left_kv, "req", -1)

    def split_result(result):
        scaled = result[:, :feat_width]
        parts = result[:, feat_width : feat_width + 3 * head_count].astype(jnp.float32)
        log_total = (
            parts[:, :head_count]
            + parts[:, head_count : 2 * head_count]
            + parts[:, 2 * head_count : 3 * head_count]
        )
        return scaled, log_total

    got_right = split_result(got_right)
    got_left = split_result(got_left)

    def place(result, start, length):
        scaled, log_total = result
        shift = tok_count - start
        keep = ((positions - start >= 0) & (positions - start < length))[:, None]

        def moved(x):
            padded = jnp.pad(x, ((tok_count, tok_count - NEWCAP), (0, 0)))
            return lax.dynamic_slice_in_dim(padded, shift, tok_count, 0)

        return keep, moved(scaled), moved(log_total)

    keep_r, scaled_r, log_r = place(got_right, right_start, right_len)
    keep_l, scaled_l, log_l = place(got_left, left_start, left_len)
    prior_scaled = jnp.where(
        keep_r, scaled_r, jnp.where(keep_l, scaled_l, jnp.zeros((), jnp.bfloat16))
    ).astype(jnp.float32)
    prior_top = jnp.where(keep_r, log_r, jnp.where(keep_l, log_l, floor_value))
    prior_total = jnp.where(keep_r | keep_l, 1.0, 0.0)

    both_top = jnp.maximum(own_top, prior_top)
    own_scale = jnp.exp(own_top - both_top)
    prior_scale = jnp.exp(prior_top - both_top)
    denominator = own_total * own_scale + prior_total * prior_scale
    lane_head = jnp.arange(feat_width, dtype=jnp.int32)[None, :] // HD

    def widened(per_head):
        full = jnp.zeros((tok_count, feat_width), jnp.float32)
        for h in range(head_count):
            full = jnp.where(lane_head == h, per_head[:, h : h + 1], full)
        return full

    numerator = own_numer * widened(own_scale) + prior_scaled * widened(prior_scale)
    attended = (numerator / widened(denominator)).astype(jnp.bfloat16)
    mixed = lax.psum_scatter(
        jnp.dot(attended, out_proj, preferred_element_type=jnp.float32).astype(jnp.bfloat16),
        "tp",
        scatter_dimension=0,
        tiled=True,
    )

    slot_ids = jnp.arange(slot_count, dtype=jnp.int32)
    left_slot_id = from_left[NEWCAP, 0].astype(jnp.int32)
    right_slot_id = from_right[NEWCAP, 0].astype(jnp.int32)

    def stored(from_left_rows, from_right_rows):
        at_left = (slot_ids == left_slot_id)[:, None, None]
        at_right = (slot_ids == right_slot_id)[:, None, None]
        return jnp.where(
            at_left,
            from_left_rows[None],
            jnp.where(at_right, from_right_rows[None], jnp.zeros((), jnp.bfloat16)),
        )

    new_keys = stored(from_left_kv[0], from_right_kv[0])
    new_values = stored(from_left_kv[1], from_right_kv[1])
    return (mixed, new_keys, new_values)


def solution(mesh):
    in_specs = (
        P("req", "tp"),
        P("req", "tp"),
        P("req", "tp"),
        P("req", None, "tp"),
        P("req", None, "tp"),
        P("tp", None),
        P("req", None),
        P("req", None),
        P("req", None),
        P("req", None),
    )
    out_specs = (P(("req", "tp"), None), P("req", None, "tp"), P("req", None, "tp"))
    return jax.shard_map(body, mesh=mesh, in_specs=in_specs, out_specs=out_specs, check_vma=False)
```

```python
import functools
import math

import jax
import jax.numpy as jnp
from jax import lax
from jax.experimental import pallas as pl
from jax.experimental.pallas import tpu as pltpu
from jax.sharding import PartitionSpec as P

HD = 224
NEWCAP = 192


floor_value = -1e30
TAG_ROWS = 8
RESULT_WIDTH = 1024


def shifted(value, axis, steps):
    count = lax.axis_size(axis)
    pairs = [(source, (source + steps) % count) for source in range(count)]
    return lax.ppermute(value, axis, pairs)


def attend_part(query_rows, key_rows, value_rows, live_mask, head_count):
    row_count = query_rows.shape[0]
    key_count = key_rows.shape[0]
    query_heads = query_rows.reshape(row_count, head_count, HD)
    key_heads = key_rows.reshape(key_count, head_count, HD)
    value_heads = value_rows.reshape(key_count, head_count, HD)
    scores = jnp.einsum(
        "thd,shd->hts", query_heads, key_heads, preferred_element_type=jnp.float32
    ) * (1.0 / math.sqrt(HD))
    scores = jnp.where(live_mask[None], scores, floor_value)
    row_top = jnp.max(scores, axis=2)
    weights = jnp.where(live_mask[None], jnp.exp(scores - row_top[:, :, None]), 0.0)
    row_total = jnp.sum(weights, axis=2)
    numerator = jnp.einsum(
        "hts,shd->thd",
        weights.astype(jnp.bfloat16),
        value_heads,
        preferred_element_type=jnp.float32,
    )
    return (numerator.reshape(row_count, head_count * HD), row_top.T, row_total.T)


def read_tag(bundle_ref):
    tag = bundle_ref[NEWCAP : NEWCAP + 1, :].astype(jnp.float32)
    lanes = lax.broadcasted_iota(jnp.int32, tag.shape, 1)

    def entry(i):
        return jnp.sum(jnp.where(lanes == i, tag, 0.0), axis=1, keepdims=True)

    return entry(0), entry(1) * 32 + entry(2)


def prior_kernel(head_count, left_ref, right_ref, key_ref, value_ref, to_left_ref, to_right_ref, numer_ref):
    slot = pl.program_id(0)
    left_slot, left_prior = read_tag(left_ref)
    right_prior = read_tag(right_ref)[1]
    from_left = left_slot == slot.astype(jnp.float32)
    prior = jnp.where(from_left, left_prior, right_prior)
    row_count = NEWCAP
    feat_width = left_ref.shape[1]
    key_count = key_ref.shape[0]
    query_rows = jnp.where(from_left, left_ref[:NEWCAP, :], right_ref[:NEWCAP, :])
    live = lax.broadcasted_iota(jnp.int32, (1, key_count), 1).astype(jnp.float32) < prior
    result_width = to_left_ref.shape[1]
    tail_lanes = lax.broadcasted_iota(jnp.int32, (row_count, result_width - feat_width), 1)
    tail = jnp.zeros((row_count, result_width - feat_width), jnp.float32)
    numer_ref[...] = jnp.zeros((row_count, feat_width), jnp.float32)
    for h in range(head_count):
        low = (h * HD) // 128 * 128
        high = min(feat_width, -(-((h + 1) * HD) // 128) * 128)
        lanes = low + lax.broadcasted_iota(jnp.int32, (1, high - low), 1)
        in_head = (lanes >= h * HD) & (lanes < (h + 1) * HD)
        head_query = jnp.where(in_head, query_rows[:, low:high], jnp.zeros((), query_rows.dtype))
        scores = lax.dot_general(
            head_query, key_ref[:, low:high], (((1,), (1,)), ((), ())),
            preferred_element_type=jnp.float32,
        ) * (1.0 / math.sqrt(HD))
        scores = jnp.where(live, scores, floor_value)
        row_top = jnp.max(scores, axis=1, keepdims=True)
        weights = jnp.where(live, jnp.exp(scores - row_top), 0.0)
        row_total = jnp.sum(weights, axis=1, keepdims=True)
        head_out = jnp.dot(
            weights.astype(jnp.bfloat16), value_ref[:, low:high], preferred_element_type=jnp.float32
        )
        numer_ref[:, low:high] = numer_ref[:, low:high] + jnp.where(in_head, head_out / row_total, 0.0)
        log_total = row_top + jnp.log(row_total)
        for part in range(3):
            piece = log_total.astype(jnp.bfloat16).astype(jnp.float32)
            tail = jnp.where(tail_lanes == part * head_count + h, piece, tail)
            log_total = log_total - piece
    for side_ref, mine in ((to_left_ref, from_left), (to_right_ref, jnp.logical_not(from_left))):
        side_ref[:, :feat_width] = jnp.where(
            mine, numer_ref[...].astype(side_ref.dtype), side_ref[:, :feat_width]
        )
        side_ref[:, feat_width:] = jnp.where(
            mine, tail.astype(side_ref.dtype), side_ref[:, feat_width:]
        )


def serve_slots(from_left, from_right, cache_keys, cache_values, head_count):
    slot_count, key_count, feat_width = cache_keys.shape
    row_count = NEWCAP
    window_lanes = sum(
        min(feat_width, -(-((h + 1) * HD) // 128) * 128) - (h * HD) // 128 * 128
        for h in range(head_count)
    )
    flops = slot_count * 4 * row_count * key_count * window_lanes
    moved = (
        2 * (from_left.size + from_right.size + cache_keys.size + cache_values.size)
        + 2 * slot_count * row_count * RESULT_WIDTH
    )
    bundle_rows = from_left.shape[0]
    return pl.pallas_call(
        functools.partial(prior_kernel, head_count),
        out_shape=(
            jax.ShapeDtypeStruct((row_count, RESULT_WIDTH), jnp.bfloat16),
            jax.ShapeDtypeStruct((row_count, RESULT_WIDTH), jnp.bfloat16),
        ),
        grid=(slot_count,),
        in_specs=[
            pl.BlockSpec((bundle_rows, feat_width), lambda s: (0, 0)),
            pl.BlockSpec((bundle_rows, feat_width), lambda s: (0, 0)),
            pl.BlockSpec((None, key_count, feat_width), lambda s: (s, 0, 0)),
            pl.BlockSpec((None, key_count, feat_width), lambda s: (s, 0, 0)),
        ],
        out_specs=(
            pl.BlockSpec((row_count, RESULT_WIDTH), lambda s: (0, 0)),
            pl.BlockSpec((row_count, RESULT_WIDTH), lambda s: (0, 0)),
        ),
        scratch_shapes=[pltpu.VMEM((row_count, feat_width), jnp.float32)],
        cost_estimate=pl.CostEstimate(
            flops=flops,
            transcendentals=slot_count * head_count * row_count * key_count,
            bytes_accessed=moved,
        ),
    )(from_left, from_right, cache_keys, cache_values)

def body(
    queries,
    keys_new,
    values_new,
    cache_keys,
    cache_values,
    out_proj,
    req_lengths,
    cache_owner,
    cache_slot,
    prior_len,
):
    tok_count = queries.shape[0]
    feat_width = queries.shape[1]
    head_count = feat_width // HD
    slot_count = cache_keys.shape[0]
    prior_rows = cache_keys.shape[1]
    req_lens = req_lengths[0]
    req_ends = jnp.cumsum(req_lens)
    positions = jnp.arange(tok_count, dtype=jnp.int32)
    row_marks = jnp.arange(NEWCAP, dtype=jnp.int32)
    prior_marks = jnp.arange(prior_rows, dtype=jnp.int32)
    req_count = lax.axis_size("req")
    req_index = lax.axis_index("req")

    first_right = cache_owner[0, 0] == (req_index + 1) % req_count

    def request_at(distance):
        pick = first_right if distance == 1 else jnp.logical_not(first_right)
        start = jnp.where(pick, 0, req_lens[0])
        length = jnp.where(pick, req_lens[0], req_lens[1])
        slot = jnp.where(pick, cache_slot[0, 0], cache_slot[0, 1])
        prior = jnp.where(pick, prior_len[0, 0], prior_len[0, 1])
        return start, length, slot, prior

    def rows_of(source, start):
        return lax.dynamic_slice_in_dim(source, start, NEWCAP, 0)

    def query_bundle(start, length, slot, prior):
        tag = jnp.stack([slot, prior // 32, prior % 32, length]).astype(jnp.bfloat16)
        tag_rows = jnp.zeros((TAG_ROWS, feat_width), jnp.bfloat16).at[0, :4].set(tag)
        return jnp.concatenate([rows_of(queries, start), tag_rows], axis=0)

    right_start, right_len, right_slot, right_prior = request_at(1)
    left_start, left_len, left_slot, left_prior = request_at(-1)

    right_bundle, left_bundle = lax.optimization_barrier(
        (
            query_bundle(right_start, right_len, right_slot, right_prior),
            query_bundle(left_start, left_len, left_slot, left_prior),
        )
    )
    from_left = shifted(right_bundle, "req", 1)
    from_right = shifted(left_bundle, "req", -1)

    served = serve_slots(from_left, from_right, cache_keys, cache_values, head_count)
    held_ends, served = lax.optimization_barrier((req_ends, served))
    segment = jnp.sum((positions[:, None] >= held_ends[None, :]).astype(jnp.int32), axis=1)
    own_live = (segment[:, None] == segment[None, :]) & (positions[None, :] <= positions[:, None])
    own_numer, own_top, own_total = attend_part(queries, keys_new, values_new, own_live, head_count)

    back_left, back_right = served
    got_right = shifted(back_left, "req", -1)
    got_left = shifted(back_right, "req", 1)

    def masked_rows(source, start, length):
        keep = (row_marks < length)[:, None]
        return jnp.where(keep, rows_of(source, start), jnp.zeros((), jnp.bfloat16))

    right_kv = jnp.stack(
        [masked_rows(keys_new, right_start, right_len), masked_rows(values_new, right_start, right_len)]
    )
    left_kv = jnp.stack(
        [masked_rows(keys_new, left_start, left_len), masked_rows(values_new, left_start, left_len)]
    )
    right_kv, left_kv, got_right, got_left = lax.optimization_barrier(
        (right_kv, left_kv, got_right, got_left)
    )
    from_left_kv = shifted(right_kv, "req", 1)
    from_right_kv = shifted(left_kv, "req", -1)

    def split_result(result):
        scaled = result[:, :feat_width]
        parts = result[:, feat_width : feat_width + 3 * head_count].astype(jnp.float32)
        log_total = (
            parts[:, :head_count]
            + parts[:, head_count : 2 * head_count]
            + parts[:, 2 * head_count : 3 * head_count]
        )
        return scaled, log_total

    got_right = split_result(got_right)
    got_left = split_result(got_left)

    def place(result, start, length):
        scaled, log_total = result
        shift = tok_count - start
        keep = ((positions - start >= 0) & (positions - start < length))[:, None]

        def moved(x):
            padded = jnp.pad(x, ((tok_count, tok_count - NEWCAP), (0, 0)))
            return lax.dynamic_slice_in_dim(padded, shift, tok_count, 0)

        return keep, moved(scaled), moved(log_total)

    keep_r, scaled_r, log_r = place(got_right, right_start, right_len)
    keep_l, scaled_l, log_l = place(got_left, left_start, left_len)
    prior_scaled = jnp.where(
        keep_r, scaled_r, jnp.where(keep_l, scaled_l, jnp.zeros((), jnp.bfloat16))
    ).astype(jnp.float32)
    prior_top = jnp.where(keep_r, log_r, jnp.where(keep_l, log_l, floor_value))
    prior_total = jnp.where(keep_r | keep_l, 1.0, 0.0)

    both_top = jnp.maximum(own_top, prior_top)
    own_scale = jnp.exp(own_top - both_top)
    prior_scale = jnp.exp(prior_top - both_top)
    denominator = own_total * own_scale + prior_total * prior_scale
    lane_head = jnp.arange(feat_width, dtype=jnp.int32)[None, :] // HD

    def widened(per_head):
        full = jnp.zeros((tok_count, feat_width), jnp.float32)
        for h in range(head_count):
            full = jnp.where(lane_head == h, per_head[:, h : h + 1], full)
        return full

    numerator = own_numer * widened(own_scale) + prior_scaled * widened(prior_scale)
    attended = (numerator / widened(denominator)).astype(jnp.bfloat16)
    mixed = lax.psum_scatter(
        jnp.dot(attended, out_proj, preferred_element_type=jnp.float32).astype(jnp.bfloat16),
        "tp",
        scatter_dimension=0,
        tiled=True,
    )

    slot_ids = jnp.arange(slot_count, dtype=jnp.int32)
    left_slot_id = from_left[NEWCAP, 0].astype(jnp.int32)
    right_slot_id = from_right[NEWCAP, 0].astype(jnp.int32)

    def stored(from_left_rows, from_right_rows):
        at_left = (slot_ids == left_slot_id)[:, None, None]
        at_right = (slot_ids == right_slot_id)[:, None, None]
        return jnp.where(
            at_left,
            from_left_rows[None],
            jnp.where(at_right, from_right_rows[None], jnp.zeros((), jnp.bfloat16)),
        )

    new_keys = stored(from_left_kv[0], from_right_kv[0])
    new_values = stored(from_left_kv[1], from_right_kv[1])
    return (mixed, new_keys, new_values)


def solution(mesh):
    in_specs = (
        P("req", "tp"),
        P("req", "tp"),
        P("req", "tp"),
        P("req", None, "tp"),
        P("req", None, "tp"),
        P("tp", None),
        P("req", None),
        P("req", None),
        P("req", None),
        P("req", None),
    )
    out_specs = (P(("req", "tp"), None), P("req", None, "tp"), P("req", None, "tp"))
    return jax.shard_map(body, mesh=mesh, in_specs=in_specs, out_specs=out_specs, check_vma=False)
```

```python
import functools
import math

import jax
import jax.numpy as jnp
from jax import lax
from jax.experimental import pallas as pl
from jax.experimental.pallas import tpu as pltpu
from jax.sharding import PartitionSpec as P

HD = 224
NEWCAP = 192


floor_value = -1e30
TAG_ROWS = 8
RESULT_WIDTH = 1024


def shifted(value, axis, steps):
    count = lax.axis_size(axis)
    pairs = [(source, (source + steps) % count) for source in range(count)]
    return lax.ppermute(value, axis, pairs)


def attend_part(query_rows, key_rows, value_rows, live_mask, head_count):
    row_count = query_rows.shape[0]
    key_count = key_rows.shape[0]
    query_heads = query_rows.reshape(row_count, head_count, HD)
    key_heads = key_rows.reshape(key_count, head_count, HD)
    value_heads = value_rows.reshape(key_count, head_count, HD)
    scores = jnp.einsum(
        "thd,shd->hts", query_heads, key_heads, preferred_element_type=jnp.float32
    ) * (1.0 / math.sqrt(HD))
    scores = jnp.where(live_mask[None], scores, floor_value)
    row_top = jnp.max(scores, axis=2)
    weights = jnp.where(live_mask[None], jnp.exp(scores - row_top[:, :, None]), 0.0)
    row_total = jnp.sum(weights, axis=2)
    numerator = jnp.einsum(
        "hts,shd->thd",
        weights.astype(jnp.bfloat16),
        value_heads,
        preferred_element_type=jnp.float32,
    )
    return (numerator.reshape(row_count, head_count * HD), row_top.T, row_total.T)


def read_tag(bundle_ref):
    tag = bundle_ref[NEWCAP : NEWCAP + 1, :].astype(jnp.float32)
    lanes = lax.broadcasted_iota(jnp.int32, tag.shape, 1)

    def entry(i):
        return jnp.sum(jnp.where(lanes == i, tag, 0.0), axis=1, keepdims=True)

    first = entry(0) == 1.0
    slot = jnp.where(first, entry(1), entry(2))
    prior = jnp.where(first, entry(3) * 32 + entry(4), entry(5) * 32 + entry(6))
    return slot, prior


def prior_kernel(head_count, left_ref, right_ref, key_ref, value_ref, to_left_ref, to_right_ref, numer_ref):
    slot = pl.program_id(0)
    left_slot, left_prior = read_tag(left_ref)
    right_prior = read_tag(right_ref)[1]
    from_left = left_slot == slot.astype(jnp.float32)
    prior = jnp.where(from_left, left_prior, right_prior)
    row_count = NEWCAP
    feat_width = left_ref.shape[1]
    key_count = key_ref.shape[0]
    query_rows = jnp.where(from_left, left_ref[:NEWCAP, :], right_ref[:NEWCAP, :])
    live = lax.broadcasted_iota(jnp.int32, (1, key_count), 1).astype(jnp.float32) < prior
    result_width = to_left_ref.shape[1]
    tail_lanes = lax.broadcasted_iota(jnp.int32, (row_count, result_width - feat_width), 1)
    tail = jnp.zeros((row_count, result_width - feat_width), jnp.float32)
    numer_ref[...] = jnp.zeros((row_count, feat_width), jnp.float32)
    for h in range(head_count):
        low = (h * HD) // 128 * 128
        high = min(feat_width, -(-((h + 1) * HD) // 128) * 128)
        lanes = low + lax.broadcasted_iota(jnp.int32, (1, high - low), 1)
        in_head = (lanes >= h * HD) & (lanes < (h + 1) * HD)
        head_query = jnp.where(in_head, query_rows[:, low:high], jnp.zeros((), query_rows.dtype))
        scores = lax.dot_general(
            head_query, key_ref[:, low:high], (((1,), (1,)), ((), ())),
            preferred_element_type=jnp.float32,
        ) * (1.0 / math.sqrt(HD))
        scores = jnp.where(live, scores, floor_value)
        row_top = jnp.max(scores, axis=1, keepdims=True)
        weights = jnp.where(live, jnp.exp(scores - row_top), 0.0)
        row_total = jnp.sum(weights, axis=1, keepdims=True)
        head_out = jnp.dot(
            weights.astype(jnp.bfloat16), value_ref[:, low:high], preferred_element_type=jnp.float32
        )
        numer_ref[:, low:high] = numer_ref[:, low:high] + jnp.where(in_head, head_out / row_total, 0.0)
        log_total = row_top + jnp.log(row_total)
        for part in range(3):
            piece = log_total.astype(jnp.bfloat16).astype(jnp.float32)
            tail = jnp.where(tail_lanes == part * head_count + h, piece, tail)
            log_total = log_total - piece
    for side_ref, mine in ((to_left_ref, from_left), (to_right_ref, jnp.logical_not(from_left))):
        side_ref[:, :feat_width] = jnp.where(
            mine, numer_ref[...].astype(side_ref.dtype), side_ref[:, :feat_width]
        )
        side_ref[:, feat_width:] = jnp.where(
            mine, tail.astype(side_ref.dtype), side_ref[:, feat_width:]
        )


def serve_slots(from_left, from_right, cache_keys, cache_values, head_count):
    slot_count, key_count, feat_width = cache_keys.shape
    row_count = NEWCAP
    window_lanes = sum(
        min(feat_width, -(-((h + 1) * HD) // 128) * 128) - (h * HD) // 128 * 128
        for h in range(head_count)
    )
    flops = slot_count * 4 * row_count * key_count * window_lanes
    moved = (
        2 * (from_left.size + from_right.size + cache_keys.size + cache_values.size)
        + 2 * slot_count * row_count * RESULT_WIDTH
    )
    bundle_rows = from_left.shape[0]
    return pl.pallas_call(
        functools.partial(prior_kernel, head_count),
        out_shape=(
            jax.ShapeDtypeStruct((row_count, RESULT_WIDTH), jnp.bfloat16),
            jax.ShapeDtypeStruct((row_count, RESULT_WIDTH), jnp.bfloat16),
        ),
        grid=(slot_count,),
        in_specs=[
            pl.BlockSpec((bundle_rows, feat_width), lambda s: (0, 0)),
            pl.BlockSpec((bundle_rows, feat_width), lambda s: (0, 0)),
            pl.BlockSpec((None, key_count, feat_width), lambda s: (s, 0, 0)),
            pl.BlockSpec((None, key_count, feat_width), lambda s: (s, 0, 0)),
        ],
        out_specs=(
            pl.BlockSpec((row_count, RESULT_WIDTH), lambda s: (0, 0)),
            pl.BlockSpec((row_count, RESULT_WIDTH), lambda s: (0, 0)),
        ),
        scratch_shapes=[pltpu.VMEM((row_count, feat_width), jnp.float32)],
        cost_estimate=pl.CostEstimate(
            flops=flops,
            transcendentals=slot_count * head_count * row_count * key_count,
            bytes_accessed=moved,
        ),
    )(from_left, from_right, cache_keys, cache_values)

def body(
    queries,
    keys_new,
    values_new,
    cache_keys,
    cache_values,
    out_proj,
    req_lengths,
    cache_owner,
    cache_slot,
    prior_len,
):
    tok_count = queries.shape[0]
    feat_width = queries.shape[1]
    head_count = feat_width // HD
    slot_count = cache_keys.shape[0]
    prior_rows = cache_keys.shape[1]
    req_lens = req_lengths[0]
    req_ends = jnp.cumsum(req_lens)
    positions = jnp.arange(tok_count, dtype=jnp.int32)
    row_marks = jnp.arange(NEWCAP, dtype=jnp.int32)
    prior_marks = jnp.arange(prior_rows, dtype=jnp.int32)
    req_count = lax.axis_size("req")
    req_index = lax.axis_index("req")

    first_right = cache_owner[0, 0] == (req_index + 1) % req_count

    def request_at(distance):
        pick = first_right if distance == 1 else jnp.logical_not(first_right)
        start = jnp.where(pick, 0, req_lens[0])
        length = jnp.where(pick, req_lens[0], req_lens[1])
        slot = jnp.where(pick, cache_slot[0, 0], cache_slot[0, 1])
        prior = jnp.where(pick, prior_len[0, 0], prior_len[0, 1])
        return start, length, slot, prior

    def rows_of(source, start):
        return lax.dynamic_slice_in_dim(source, start, NEWCAP, 0)

    raw_tag = jnp.stack(
        [
            cache_slot[0, 0], cache_slot[0, 1],
            prior_len[0, 0] // 32, prior_len[0, 0] % 32,
            prior_len[0, 1] // 32, prior_len[0, 1] % 32,
        ]
    )

    def query_bundle(start, pick):
        tag = jnp.concatenate([pick.astype(jnp.int32)[None], raw_tag]).astype(jnp.bfloat16)
        tag_rows = jnp.zeros((TAG_ROWS, feat_width), jnp.bfloat16).at[0, : tag.shape[0]].set(tag)
        return jnp.concatenate([rows_of(queries, start), tag_rows], axis=0)

    right_start, right_len, right_slot, right_prior = request_at(1)
    left_start, left_len, left_slot, left_prior = request_at(-1)

    from_left = shifted(query_bundle(right_start, first_right), "req", 1)
    from_right = shifted(query_bundle(left_start, jnp.logical_not(first_right)), "req", -1)

    served = serve_slots(from_left, from_right, cache_keys, cache_values, head_count)
    held_ends, served = lax.optimization_barrier((req_ends, served))
    segment = jnp.sum((positions[:, None] >= held_ends[None, :]).astype(jnp.int32), axis=1)
    own_live = (segment[:, None] == segment[None, :]) & (positions[None, :] <= positions[:, None])
    own_numer, own_top, own_total = attend_part(queries, keys_new, values_new, own_live, head_count)

    back_left, back_right = served
    got_right = shifted(back_left, "req", -1)
    got_left = shifted(back_right, "req", 1)

    def masked_rows(source, start, length):
        keep = (row_marks < length)[:, None]
        return jnp.where(keep, rows_of(source, start), jnp.zeros((), jnp.bfloat16))

    right_kv = jnp.stack(
        [masked_rows(keys_new, right_start, right_len), masked_rows(values_new, right_start, right_len)]
    )
    left_kv = jnp.stack(
        [masked_rows(keys_new, left_start, left_len), masked_rows(values_new, left_start, left_len)]
    )
    right_kv, left_kv, got_right, got_left = lax.optimization_barrier(
        (right_kv, left_kv, got_right, got_left)
    )
    from_left_kv = shifted(right_kv, "req", 1)
    from_right_kv = shifted(left_kv, "req", -1)

    def split_result(result):
        scaled = result[:, :feat_width]
        parts = result[:, feat_width : feat_width + 3 * head_count].astype(jnp.float32)
        log_total = (
            parts[:, :head_count]
            + parts[:, head_count : 2 * head_count]
            + parts[:, 2 * head_count : 3 * head_count]
        )
        return scaled, log_total

    got_right = split_result(got_right)
    got_left = split_result(got_left)

    def place(result, start, length):
        scaled, log_total = result
        shift = tok_count - start
        keep = ((positions - start >= 0) & (positions - start < length))[:, None]

        def moved(x):
            padded = jnp.pad(x, ((tok_count, tok_count - NEWCAP), (0, 0)))
            return lax.dynamic_slice_in_dim(padded, shift, tok_count, 0)

        return keep, moved(scaled), moved(log_total)

    keep_r, scaled_r, log_r = place(got_right, right_start, right_len)
    keep_l, scaled_l, log_l = place(got_left, left_start, left_len)
    prior_scaled = jnp.where(
        keep_r, scaled_r, jnp.where(keep_l, scaled_l, jnp.zeros((), jnp.bfloat16))
    ).astype(jnp.float32)
    prior_top = jnp.where(keep_r, log_r, jnp.where(keep_l, log_l, floor_value))
    prior_total = jnp.where(keep_r | keep_l, 1.0, 0.0)

    both_top = jnp.maximum(own_top, prior_top)
    own_scale = jnp.exp(own_top - both_top)
    prior_scale = jnp.exp(prior_top - both_top)
    denominator = own_total * own_scale + prior_total * prior_scale
    lane_head = jnp.arange(feat_width, dtype=jnp.int32)[None, :] // HD

    def widened(per_head):
        full = jnp.zeros((tok_count, feat_width), jnp.float32)
        for h in range(head_count):
            full = jnp.where(lane_head == h, per_head[:, h : h + 1], full)
        return full

    numerator = own_numer * widened(own_scale) + prior_scaled * widened(prior_scale)
    attended = (numerator / widened(denominator)).astype(jnp.bfloat16)
    mixed = lax.psum_scatter(
        jnp.dot(attended, out_proj, preferred_element_type=jnp.float32).astype(jnp.bfloat16),
        "tp",
        scatter_dimension=0,
        tiled=True,
    )

    slot_ids = jnp.arange(slot_count, dtype=jnp.int32)
    def slot_id(bundle):
        return jnp.where(bundle[NEWCAP, 0] == 1, bundle[NEWCAP, 1], bundle[NEWCAP, 2]).astype(jnp.int32)

    left_slot_id = slot_id(from_left)
    right_slot_id = slot_id(from_right)

    def stored(from_left_rows, from_right_rows):
        at_left = (slot_ids == left_slot_id)[:, None, None]
        at_right = (slot_ids == right_slot_id)[:, None, None]
        return jnp.where(
            at_left,
            from_left_rows[None],
            jnp.where(at_right, from_right_rows[None], jnp.zeros((), jnp.bfloat16)),
        )

    new_keys = stored(from_left_kv[0], from_right_kv[0])
    new_values = stored(from_left_kv[1], from_right_kv[1])
    return (mixed, new_keys, new_values)


def solution(mesh):
    in_specs = (
        P("req", "tp"),
        P("req", "tp"),
        P("req", "tp"),
        P("req", None, "tp"),
        P("req", None, "tp"),
        P("tp", None),
        P("req", None),
        P("req", None),
        P("req", None),
        P("req", None),
    )
    out_specs = (P(("req", "tp"), None), P("req", None, "tp"), P("req", None, "tp"))
    return jax.shard_map(body, mesh=mesh, in_specs=in_specs, out_specs=out_specs, check_vma=False)
```

```python
import functools
import math

import jax
import jax.numpy as jnp
from jax import lax
from jax.experimental import pallas as pl
from jax.experimental.pallas import tpu as pltpu
from jax.sharding import PartitionSpec as P

HD = 224
NEWCAP = 192


floor_value = -1e30
TAG_ROWS = 8
RESULT_WIDTH = 1024


def shifted(value, axis, steps):
    count = lax.axis_size(axis)
    pairs = [(source, (source + steps) % count) for source in range(count)]
    return lax.ppermute(value, axis, pairs)


def attend_part(query_rows, key_rows, value_rows, live_mask, head_count):
    row_count = query_rows.shape[0]
    key_count = key_rows.shape[0]
    query_heads = query_rows.reshape(row_count, head_count, HD)
    key_heads = key_rows.reshape(key_count, head_count, HD)
    value_heads = value_rows.reshape(key_count, head_count, HD)
    scores = jnp.einsum(
        "thd,shd->hts", query_heads, key_heads, preferred_element_type=jnp.float32
    ) * (1.0 / math.sqrt(HD))
    scores = jnp.where(live_mask[None], scores, floor_value)
    row_top = jnp.max(scores, axis=2)
    weights = jnp.where(live_mask[None], jnp.exp(scores - row_top[:, :, None]), 0.0)
    row_total = jnp.sum(weights, axis=2)
    numerator = jnp.einsum(
        "hts,shd->thd",
        weights.astype(jnp.bfloat16),
        value_heads,
        preferred_element_type=jnp.float32,
    )
    return (numerator.reshape(row_count, head_count * HD), row_top.T, row_total.T)


def read_tag(bundle_ref):
    tag = bundle_ref[NEWCAP : NEWCAP + 1, :].astype(jnp.float32)
    lanes = lax.broadcasted_iota(jnp.int32, tag.shape, 1)

    def entry(i):
        return jnp.sum(jnp.where(lanes == i, tag, 0.0), axis=1, keepdims=True)

    first = entry(0) == 1.0
    slot = jnp.where(first, entry(1), entry(2))
    prior = jnp.where(first, entry(3) * 32 + entry(4), entry(5) * 32 + entry(6))
    return slot, prior


def prior_kernel(head_count, left_ref, right_ref, key_ref, value_ref, to_left_ref, to_right_ref, numer_ref):
    slot = pl.program_id(0)
    left_slot, left_prior = read_tag(left_ref)
    right_prior = read_tag(right_ref)[1]
    from_left = left_slot == slot.astype(jnp.float32)
    prior = jnp.where(from_left, left_prior, right_prior)
    row_count = NEWCAP
    feat_width = left_ref.shape[1]
    key_count = key_ref.shape[0]
    query_rows = jnp.where(from_left, left_ref[:NEWCAP, :], right_ref[:NEWCAP, :])
    live = lax.broadcasted_iota(jnp.int32, (1, key_count), 1).astype(jnp.float32) < prior
    result_width = to_left_ref.shape[1]
    tail_lanes = lax.broadcasted_iota(jnp.int32, (row_count, result_width - feat_width), 1)
    tail = jnp.zeros((row_count, result_width - feat_width), jnp.float32)
    numer_ref[...] = jnp.zeros((row_count, feat_width), jnp.float32)
    for h in range(head_count):
        low = (h * HD) // 128 * 128
        high = min(feat_width, -(-((h + 1) * HD) // 128) * 128)
        lanes = low + lax.broadcasted_iota(jnp.int32, (1, high - low), 1)
        in_head = (lanes >= h * HD) & (lanes < (h + 1) * HD)
        head_query = jnp.where(in_head, query_rows[:, low:high], jnp.zeros((), query_rows.dtype))
        scores = lax.dot_general(
            head_query, key_ref[:, low:high], (((1,), (1,)), ((), ())),
            preferred_element_type=jnp.float32,
        ) * (1.0 / math.sqrt(HD))
        scores = jnp.where(live, scores, floor_value)
        row_top = jnp.max(scores, axis=1, keepdims=True)
        weights = jnp.where(live, jnp.exp(scores - row_top), 0.0)
        row_total = jnp.sum(weights, axis=1, keepdims=True)
        head_out = jnp.dot(
            weights.astype(jnp.bfloat16), value_ref[:, low:high], preferred_element_type=jnp.float32
        )
        numer_ref[:, low:high] = numer_ref[:, low:high] + jnp.where(in_head, head_out / row_total, 0.0)
        log_total = row_top + jnp.log(row_total)
        for part in range(3):
            piece = log_total.astype(jnp.bfloat16).astype(jnp.float32)
            tail = jnp.where(tail_lanes == part * head_count + h, piece, tail)
            log_total = log_total - piece
    for side_ref, mine in ((to_left_ref, from_left), (to_right_ref, jnp.logical_not(from_left))):
        side_ref[:, :feat_width] = jnp.where(
            mine, numer_ref[...].astype(side_ref.dtype), side_ref[:, :feat_width]
        )
        side_ref[:, feat_width:] = jnp.where(
            mine, tail.astype(side_ref.dtype), side_ref[:, feat_width:]
        )


def serve_slots(from_left, from_right, cache_keys, cache_values, head_count):
    slot_count, key_count, feat_width = cache_keys.shape
    row_count = NEWCAP
    window_lanes = sum(
        min(feat_width, -(-((h + 1) * HD) // 128) * 128) - (h * HD) // 128 * 128
        for h in range(head_count)
    )
    flops = slot_count * 4 * row_count * key_count * window_lanes
    moved = (
        2 * (from_left.size + from_right.size + cache_keys.size + cache_values.size)
        + 2 * slot_count * row_count * RESULT_WIDTH
    )
    bundle_rows = from_left.shape[0]
    return pl.pallas_call(
        functools.partial(prior_kernel, head_count),
        out_shape=(
            jax.ShapeDtypeStruct((row_count, RESULT_WIDTH), jnp.bfloat16),
            jax.ShapeDtypeStruct((row_count, RESULT_WIDTH), jnp.bfloat16),
        ),
        grid=(slot_count,),
        in_specs=[
            pl.BlockSpec((bundle_rows, feat_width), lambda s: (0, 0)),
            pl.BlockSpec((bundle_rows, feat_width), lambda s: (0, 0)),
            pl.BlockSpec((None, key_count, feat_width), lambda s: (s, 0, 0)),
            pl.BlockSpec((None, key_count, feat_width), lambda s: (s, 0, 0)),
        ],
        out_specs=(
            pl.BlockSpec((row_count, RESULT_WIDTH), lambda s: (0, 0)),
            pl.BlockSpec((row_count, RESULT_WIDTH), lambda s: (0, 0)),
        ),
        scratch_shapes=[pltpu.VMEM((row_count, feat_width), jnp.float32)],
        cost_estimate=pl.CostEstimate(
            flops=flops,
            transcendentals=slot_count * head_count * row_count * key_count,
            bytes_accessed=moved,
        ),
    )(from_left, from_right, cache_keys, cache_values)


def own_kernel(head_count, query_ref, key_ref, value_ref, seg_col_ref, seg_row_ref, numer_ref, stats_ref):
    row_count, feat_width = query_ref.shape
    rows = lax.broadcasted_iota(jnp.int32, (row_count, row_count), 0)
    cols = lax.broadcasted_iota(jnp.int32, (row_count, row_count), 1)
    live = (seg_col_ref[...] == seg_row_ref[...]) & (cols <= rows)
    stat_lanes = lax.broadcasted_iota(jnp.int32, stats_ref.shape, 1)
    stats = jnp.zeros(stats_ref.shape, jnp.float32)
    numer_ref[...] = jnp.zeros((row_count, feat_width), jnp.float32)
    for h in range(head_count):
        low = (h * HD) // 128 * 128
        high = min(feat_width, -(-((h + 1) * HD) // 128) * 128)
        lanes = low + lax.broadcasted_iota(jnp.int32, (1, high - low), 1)
        in_head = (lanes >= h * HD) & (lanes < (h + 1) * HD)
        head_query = jnp.where(in_head, query_ref[:, low:high], jnp.zeros((), query_ref.dtype))
        scores = lax.dot_general(
            head_query, key_ref[:, low:high], (((1,), (1,)), ((), ())),
            preferred_element_type=jnp.float32,
        ) * (1.0 / math.sqrt(HD))
        scores = jnp.where(live, scores, floor_value)
        row_top = jnp.max(scores, axis=1, keepdims=True)
        weights = jnp.where(live, jnp.exp(scores - row_top), 0.0)
        row_total = jnp.sum(weights, axis=1, keepdims=True)
        head_out = jnp.dot(
            weights.astype(jnp.bfloat16), value_ref[:, low:high], preferred_element_type=jnp.float32
        )
        numer_ref[:, low:high] = numer_ref[:, low:high] + jnp.where(in_head, head_out, 0.0)
        stats = jnp.where(stat_lanes == h, row_top, stats)
        stats = jnp.where(stat_lanes == head_count + h, row_total, stats)
    stats_ref[...] = stats


def attend_own(queries, keys_new, values_new, segment, head_count):
    row_count, feat_width = queries.shape
    vmem = pl.BlockSpec(memory_space=pltpu.VMEM)
    numer, stats = pl.pallas_call(
        functools.partial(own_kernel, head_count),
        out_shape=(
            jax.ShapeDtypeStruct((row_count, feat_width), jnp.float32),
            jax.ShapeDtypeStruct((row_count, 128), jnp.float32),
        ),
        in_specs=[vmem] * 5,
        out_specs=(vmem, vmem),
        cost_estimate=pl.CostEstimate(
            flops=4 * row_count * row_count * 1280,
            transcendentals=head_count * row_count * row_count,
            bytes_accessed=6 * row_count * feat_width + 4 * row_count * (feat_width + 128),
        ),
    )(queries, keys_new, values_new, segment[:, None], segment[None, :])
    return numer, stats[:, :head_count], stats[:, head_count : 2 * head_count]


def body(
    queries,
    keys_new,
    values_new,
    cache_keys,
    cache_values,
    out_proj,
    req_lengths,
    cache_owner,
    cache_slot,
    prior_len,
):
    tok_count = queries.shape[0]
    feat_width = queries.shape[1]
    head_count = feat_width // HD
    slot_count = cache_keys.shape[0]
    prior_rows = cache_keys.shape[1]
    req_lens = req_lengths[0]
    req_ends = jnp.cumsum(req_lens)
    positions = jnp.arange(tok_count, dtype=jnp.int32)
    row_marks = jnp.arange(NEWCAP, dtype=jnp.int32)
    prior_marks = jnp.arange(prior_rows, dtype=jnp.int32)
    req_count = lax.axis_size("req")
    req_index = lax.axis_index("req")

    first_right = cache_owner[0, 0] == (req_index + 1) % req_count

    def request_at(distance):
        pick = first_right if distance == 1 else jnp.logical_not(first_right)
        start = jnp.where(pick, 0, req_lens[0])
        length = jnp.where(pick, req_lens[0], req_lens[1])
        slot = jnp.where(pick, cache_slot[0, 0], cache_slot[0, 1])
        prior = jnp.where(pick, prior_len[0, 0], prior_len[0, 1])
        return start, length, slot, prior

    def rows_of(source, start):
        return lax.dynamic_slice_in_dim(source, start, NEWCAP, 0)

    raw_tag = jnp.stack(
        [
            cache_slot[0, 0], cache_slot[0, 1],
            prior_len[0, 0] // 32, prior_len[0, 0] % 32,
            prior_len[0, 1] // 32, prior_len[0, 1] % 32,
        ]
    )

    def query_bundle(start, pick):
        tag = jnp.concatenate([pick.astype(jnp.int32)[None], raw_tag]).astype(jnp.bfloat16)
        tag_rows = jnp.zeros((TAG_ROWS, feat_width), jnp.bfloat16).at[0, : tag.shape[0]].set(tag)
        return jnp.concatenate([rows_of(queries, start), tag_rows], axis=0)

    right_start, right_len, right_slot, right_prior = request_at(1)
    left_start, left_len, left_slot, left_prior = request_at(-1)

    from_left = shifted(query_bundle(right_start, first_right), "req", 1)
    from_right = shifted(query_bundle(left_start, jnp.logical_not(first_right)), "req", -1)

    served = serve_slots(from_left, from_right, cache_keys, cache_values, head_count)
    held_ends, served = lax.optimization_barrier((req_ends, served))
    segment = jnp.sum((positions[:, None] >= held_ends[None, :]).astype(jnp.int32), axis=1)
    own_numer, own_top, own_total = attend_own(queries, keys_new, values_new, segment, head_count)

    back_left, back_right = served
    got_right = shifted(back_left, "req", -1)
    got_left = shifted(back_right, "req", 1)

    def masked_rows(source, start, length):
        keep = (row_marks < length)[:, None]
        return jnp.where(keep, rows_of(source, start), jnp.zeros((), jnp.bfloat16))

    right_kv = jnp.stack(
        [masked_rows(keys_new, right_start, right_len), masked_rows(values_new, right_start, right_len)]
    )
    left_kv = jnp.stack(
        [masked_rows(keys_new, left_start, left_len), masked_rows(values_new, left_start, left_len)]
    )
    right_kv, left_kv, got_right, got_left = lax.optimization_barrier(
        (right_kv, left_kv, got_right, got_left)
    )
    from_left_kv = shifted(right_kv, "req", 1)
    from_right_kv = shifted(left_kv, "req", -1)

    def split_result(result):
        scaled = result[:, :feat_width]
        parts = result[:, feat_width : feat_width + 3 * head_count].astype(jnp.float32)
        log_total = (
            parts[:, :head_count]
            + parts[:, head_count : 2 * head_count]
            + parts[:, 2 * head_count : 3 * head_count]
        )
        return scaled, log_total

    got_right = split_result(got_right)
    got_left = split_result(got_left)

    def place(result, start, length):
        scaled, log_total = result
        shift = tok_count - start
        keep = ((positions - start >= 0) & (positions - start < length))[:, None]

        def moved(x):
            padded = jnp.pad(x, ((tok_count, tok_count - NEWCAP), (0, 0)))
            return lax.dynamic_slice_in_dim(padded, shift, tok_count, 0)

        return keep, moved(scaled), moved(log_total)

    keep_r, scaled_r, log_r = place(got_right, right_start, right_len)
    keep_l, scaled_l, log_l = place(got_left, left_start, left_len)
    prior_scaled = jnp.where(
        keep_r, scaled_r, jnp.where(keep_l, scaled_l, jnp.zeros((), jnp.bfloat16))
    ).astype(jnp.float32)
    prior_top = jnp.where(keep_r, log_r, jnp.where(keep_l, log_l, floor_value))
    prior_total = jnp.where(keep_r | keep_l, 1.0, 0.0)

    both_top = jnp.maximum(own_top, prior_top)
    own_scale = jnp.exp(own_top - both_top)
    prior_scale = jnp.exp(prior_top - both_top)
    denominator = own_total * own_scale + prior_total * prior_scale
    lane_head = jnp.arange(feat_width, dtype=jnp.int32)[None, :] // HD

    def widened(per_head):
        full = jnp.zeros((tok_count, feat_width), jnp.float32)
        for h in range(head_count):
            full = jnp.where(lane_head == h, per_head[:, h : h + 1], full)
        return full

    numerator = own_numer * widened(own_scale) + prior_scaled * widened(prior_scale)
    attended = (numerator / widened(denominator)).astype(jnp.bfloat16)
    mixed = lax.psum_scatter(
        jnp.dot(attended, out_proj, preferred_element_type=jnp.float32).astype(jnp.bfloat16),
        "tp",
        scatter_dimension=0,
        tiled=True,
    )

    slot_ids = jnp.arange(slot_count, dtype=jnp.int32)
    def slot_id(bundle):
        return jnp.where(bundle[NEWCAP, 0] == 1, bundle[NEWCAP, 1], bundle[NEWCAP, 2]).astype(jnp.int32)

    left_slot_id = slot_id(from_left)
    right_slot_id = slot_id(from_right)

    def stored(from_left_rows, from_right_rows):
        at_left = (slot_ids == left_slot_id)[:, None, None]
        at_right = (slot_ids == right_slot_id)[:, None, None]
        return jnp.where(
            at_left,
            from_left_rows[None],
            jnp.where(at_right, from_right_rows[None], jnp.zeros((), jnp.bfloat16)),
        )

    new_keys = stored(from_left_kv[0], from_right_kv[0])
    new_values = stored(from_left_kv[1], from_right_kv[1])
    return (mixed, new_keys, new_values)


def solution(mesh):
    in_specs = (
        P("req", "tp"),
        P("req", "tp"),
        P("req", "tp"),
        P("req", None, "tp"),
        P("req", None, "tp"),
        P("tp", None),
        P("req", None),
        P("req", None),
        P("req", None),
        P("req", None),
    )
    out_specs = (P(("req", "tp"), None), P("req", None, "tp"), P("req", None, "tp"))
    return jax.shard_map(body, mesh=mesh, in_specs=in_specs, out_specs=out_specs, check_vma=False)
```

```python
import functools
import math

import jax
import jax.numpy as jnp
from jax import lax
from jax.experimental import pallas as pl
from jax.experimental.pallas import tpu as pltpu
from jax.sharding import PartitionSpec as P

HD = 224
NEWCAP = 192


floor_value = -1e30
TAG_ROWS = 8
RESULT_WIDTH = 1024


def shifted(value, axis, steps):
    count = lax.axis_size(axis)
    pairs = [(source, (source + steps) % count) for source in range(count)]
    return lax.ppermute(value, axis, pairs)


def attend_part(query_rows, key_rows, value_rows, live_mask, head_count):
    row_count = query_rows.shape[0]
    key_count = key_rows.shape[0]
    query_heads = query_rows.reshape(row_count, head_count, HD)
    key_heads = key_rows.reshape(key_count, head_count, HD)
    value_heads = value_rows.reshape(key_count, head_count, HD)
    scores = jnp.einsum(
        "thd,shd->hts", query_heads, key_heads, preferred_element_type=jnp.float32
    ) * (1.0 / math.sqrt(HD))
    scores = jnp.where(live_mask[None], scores, floor_value)
    row_top = jnp.max(scores, axis=2)
    weights = jnp.where(live_mask[None], jnp.exp(scores - row_top[:, :, None]), 0.0)
    row_total = jnp.sum(weights, axis=2)
    numerator = jnp.einsum(
        "hts,shd->thd",
        weights.astype(jnp.bfloat16),
        value_heads,
        preferred_element_type=jnp.float32,
    )
    return (numerator.reshape(row_count, head_count * HD), row_top.T, row_total.T)


def read_tag(bundle_ref):
    tag = bundle_ref[NEWCAP : NEWCAP + 1, :].astype(jnp.float32)
    lanes = lax.broadcasted_iota(jnp.int32, tag.shape, 1)

    def entry(i):
        return jnp.sum(jnp.where(lanes == i, tag, 0.0), axis=1, keepdims=True)

    first = entry(0) == 1.0
    slot = jnp.where(first, entry(1), entry(2))
    prior = jnp.where(first, entry(3) * 32 + entry(4), entry(5) * 32 + entry(6))
    return slot, prior


def prior_kernel(head_count, left_ref, right_ref, key_ref, value_ref, to_left_ref, to_right_ref, numer_ref):
    slot = pl.program_id(0)
    left_slot, left_prior = read_tag(left_ref)
    right_prior = read_tag(right_ref)[1]
    from_left = left_slot == slot.astype(jnp.float32)
    prior = jnp.where(from_left, left_prior, right_prior)
    row_count = NEWCAP
    feat_width = left_ref.shape[1]
    key_count = key_ref.shape[0]
    query_rows = jnp.where(from_left, left_ref[:NEWCAP, :], right_ref[:NEWCAP, :])
    live = lax.broadcasted_iota(jnp.int32, (1, key_count), 1).astype(jnp.float32) < prior
    result_width = to_left_ref.shape[1]
    tail_lanes = lax.broadcasted_iota(jnp.int32, (row_count, result_width - feat_width), 1)
    tail = jnp.zeros((row_count, result_width - feat_width), jnp.float32)
    numer_ref[...] = jnp.zeros((row_count, feat_width), jnp.float32)
    for h in range(head_count):
        low = (h * HD) // 128 * 128
        high = min(feat_width, -(-((h + 1) * HD) // 128) * 128)
        lanes = low + lax.broadcasted_iota(jnp.int32, (1, high - low), 1)
        in_head = (lanes >= h * HD) & (lanes < (h + 1) * HD)
        head_query = jnp.where(in_head, query_rows[:, low:high], jnp.zeros((), query_rows.dtype))
        scores = lax.dot_general(
            head_query, key_ref[:, low:high], (((1,), (1,)), ((), ())),
            preferred_element_type=jnp.float32,
        ) * (1.0 / math.sqrt(HD))
        scores = jnp.where(live, scores, floor_value)
        row_top = jnp.max(scores, axis=1, keepdims=True)
        weights = jnp.where(live, jnp.exp(scores - row_top), 0.0)
        row_total = jnp.sum(weights, axis=1, keepdims=True)
        head_out = jnp.dot(
            weights.astype(jnp.bfloat16), value_ref[:, low:high], preferred_element_type=jnp.float32
        )
        numer_ref[:, low:high] = numer_ref[:, low:high] + jnp.where(in_head, head_out / row_total, 0.0)
        log_total = row_top + jnp.log(row_total)
        for part in range(3):
            piece = log_total.astype(jnp.bfloat16).astype(jnp.float32)
            tail = jnp.where(tail_lanes == part * head_count + h, piece, tail)
            log_total = log_total - piece
    for side_ref, mine in ((to_left_ref, from_left), (to_right_ref, jnp.logical_not(from_left))):
        side_ref[:, :feat_width] = jnp.where(
            mine, numer_ref[...].astype(side_ref.dtype), side_ref[:, :feat_width]
        )
        side_ref[:, feat_width:] = jnp.where(
            mine, tail.astype(side_ref.dtype), side_ref[:, feat_width:]
        )


def serve_slots(from_left, from_right, cache_keys, cache_values, head_count):
    slot_count, key_count, feat_width = cache_keys.shape
    row_count = NEWCAP
    window_lanes = sum(
        min(feat_width, -(-((h + 1) * HD) // 128) * 128) - (h * HD) // 128 * 128
        for h in range(head_count)
    )
    flops = slot_count * 4 * row_count * key_count * window_lanes
    moved = (
        2 * (from_left.size + from_right.size + cache_keys.size + cache_values.size)
        + 2 * slot_count * row_count * RESULT_WIDTH
    )
    bundle_rows = from_left.shape[0]
    return pl.pallas_call(
        functools.partial(prior_kernel, head_count),
        out_shape=(
            jax.ShapeDtypeStruct((row_count, RESULT_WIDTH), jnp.bfloat16),
            jax.ShapeDtypeStruct((row_count, RESULT_WIDTH), jnp.bfloat16),
        ),
        grid=(slot_count,),
        in_specs=[
            pl.BlockSpec((bundle_rows, feat_width), lambda s: (0, 0)),
            pl.BlockSpec((bundle_rows, feat_width), lambda s: (0, 0)),
            pl.BlockSpec((None, key_count, feat_width), lambda s: (s, 0, 0)),
            pl.BlockSpec((None, key_count, feat_width), lambda s: (s, 0, 0)),
        ],
        out_specs=(
            pl.BlockSpec((row_count, RESULT_WIDTH), lambda s: (0, 0)),
            pl.BlockSpec((row_count, RESULT_WIDTH), lambda s: (0, 0)),
        ),
        scratch_shapes=[pltpu.VMEM((row_count, feat_width), jnp.float32)],
        cost_estimate=pl.CostEstimate(
            flops=flops,
            transcendentals=slot_count * head_count * row_count * key_count,
            bytes_accessed=moved,
        ),
    )(from_left, from_right, cache_keys, cache_values)


def own_kernel(head_count, query_ref, key_ref, value_ref, seg_col_ref, seg_row_ref, numer_ref, stats_ref):
    row_count, feat_width = query_ref.shape
    rows = lax.broadcasted_iota(jnp.int32, (row_count, row_count), 0)
    cols = lax.broadcasted_iota(jnp.int32, (row_count, row_count), 1)
    live = (seg_col_ref[...] == seg_row_ref[...]) & (cols <= rows)
    stat_lanes = lax.broadcasted_iota(jnp.int32, stats_ref.shape, 1)
    stats = jnp.zeros(stats_ref.shape, jnp.float32)
    numer_ref[...] = jnp.zeros((row_count, feat_width), jnp.float32)
    for h in range(head_count):
        low = (h * HD) // 128 * 128
        high = min(feat_width, -(-((h + 1) * HD) // 128) * 128)
        lanes = low + lax.broadcasted_iota(jnp.int32, (1, high - low), 1)
        in_head = (lanes >= h * HD) & (lanes < (h + 1) * HD)
        head_query = jnp.where(in_head, query_ref[:, low:high], jnp.zeros((), query_ref.dtype))
        scores = lax.dot_general(
            head_query, key_ref[:, low:high], (((1,), (1,)), ((), ())),
            preferred_element_type=jnp.float32,
        ) * (1.0 / math.sqrt(HD))
        scores = jnp.where(live, scores, floor_value)
        row_top = jnp.max(scores, axis=1, keepdims=True)
        weights = jnp.where(live, jnp.exp(scores - row_top), 0.0)
        row_total = jnp.sum(weights, axis=1, keepdims=True)
        head_out = jnp.dot(
            weights.astype(jnp.bfloat16), value_ref[:, low:high], preferred_element_type=jnp.float32
        )
        numer_ref[:, low:high] = numer_ref[:, low:high] + jnp.where(in_head, head_out, 0.0)
        stats = jnp.where(stat_lanes == h, row_top, stats)
        stats = jnp.where(stat_lanes == head_count + h, row_total, stats)
    stats_ref[...] = stats


def attend_own(queries, keys_new, values_new, segment, head_count):
    row_count, feat_width = queries.shape
    vmem = pl.BlockSpec(memory_space=pltpu.VMEM)
    numer, stats = pl.pallas_call(
        functools.partial(own_kernel, head_count),
        out_shape=(
            jax.ShapeDtypeStruct((row_count, feat_width), jnp.float32),
            jax.ShapeDtypeStruct((row_count, 128), jnp.float32),
        ),
        in_specs=[vmem] * 5,
        out_specs=(vmem, vmem),
        cost_estimate=pl.CostEstimate(
            flops=4 * row_count * row_count * 1280,
            transcendentals=head_count * row_count * row_count,
            bytes_accessed=6 * row_count * feat_width + 4 * row_count * (feat_width + 128),
        ),
    )(queries, keys_new, values_new, segment[:, None], segment[None, :])
    return numer, stats[:, :head_count], stats[:, head_count : 2 * head_count]


def body(
    queries,
    keys_new,
    values_new,
    cache_keys,
    cache_values,
    out_proj,
    req_lengths,
    cache_owner,
    cache_slot,
    prior_len,
):
    tok_count = queries.shape[0]
    feat_width = queries.shape[1]
    head_count = feat_width // HD
    slot_count = cache_keys.shape[0]
    prior_rows = cache_keys.shape[1]
    req_lens = req_lengths[0]
    req_ends = jnp.cumsum(req_lens)
    positions = jnp.arange(tok_count, dtype=jnp.int32)
    row_marks = jnp.arange(NEWCAP, dtype=jnp.int32)
    prior_marks = jnp.arange(prior_rows, dtype=jnp.int32)
    req_count = lax.axis_size("req")
    req_index = lax.axis_index("req")

    first_right = cache_owner[0, 0] == (req_index + 1) % req_count

    def request_at(distance):
        pick = first_right if distance == 1 else jnp.logical_not(first_right)
        start = jnp.where(pick, 0, req_lens[0])
        length = jnp.where(pick, req_lens[0], req_lens[1])
        slot = jnp.where(pick, cache_slot[0, 0], cache_slot[0, 1])
        prior = jnp.where(pick, prior_len[0, 0], prior_len[0, 1])
        return start, length, slot, prior

    def rows_of(source, start):
        return lax.dynamic_slice_in_dim(source, start, NEWCAP, 0)

    raw_tag = jnp.stack(
        [
            cache_slot[0, 0], cache_slot[0, 1],
            prior_len[0, 0] // 32, prior_len[0, 0] % 32,
            prior_len[0, 1] // 32, prior_len[0, 1] % 32,
        ]
    )

    def query_bundle(start, pick):
        tag = jnp.concatenate([pick.astype(jnp.int32)[None], raw_tag]).astype(jnp.bfloat16)
        tag_rows = jnp.zeros((TAG_ROWS, feat_width), jnp.bfloat16).at[0, : tag.shape[0]].set(tag)
        return jnp.concatenate([rows_of(queries, start), tag_rows], axis=0)

    right_start, right_len, right_slot, right_prior = request_at(1)
    left_start, left_len, left_slot, left_prior = request_at(-1)

    from_left = shifted(query_bundle(right_start, first_right), "req", 1)
    from_right = shifted(query_bundle(left_start, jnp.logical_not(first_right)), "req", -1)

    served = serve_slots(from_left, from_right, cache_keys, cache_values, head_count)
    segment = jnp.sum((positions[:, None] >= req_ends[None, :]).astype(jnp.int32), axis=1)
    own_numer, own_top, own_total = attend_own(queries, keys_new, values_new, segment, head_count)

    back_left, back_right = served
    got_right = shifted(back_left, "req", -1)
    got_left = shifted(back_right, "req", 1)

    def masked_rows(source, start, length):
        keep = (row_marks < length)[:, None]
        return jnp.where(keep, rows_of(source, start), jnp.zeros((), jnp.bfloat16))

    right_kv = jnp.stack(
        [masked_rows(keys_new, right_start, right_len), masked_rows(values_new, right_start, right_len)]
    )
    left_kv = jnp.stack(
        [masked_rows(keys_new, left_start, left_len), masked_rows(values_new, left_start, left_len)]
    )
    right_kv, left_kv, got_right, got_left = lax.optimization_barrier(
        (right_kv, left_kv, got_right, got_left)
    )
    from_left_kv = shifted(right_kv, "req", 1)
    from_right_kv = shifted(left_kv, "req", -1)

    def split_result(result):
        scaled = result[:, :feat_width]
        parts = result[:, feat_width : feat_width + 3 * head_count].astype(jnp.float32)
        log_total = (
            parts[:, :head_count]
            + parts[:, head_count : 2 * head_count]
            + parts[:, 2 * head_count : 3 * head_count]
        )
        return scaled, log_total

    got_right = split_result(got_right)
    got_left = split_result(got_left)

    def place(result, start, length):
        scaled, log_total = result
        shift = tok_count - start
        keep = ((positions - start >= 0) & (positions - start < length))[:, None]

        def moved(x):
            padded = jnp.pad(x, ((tok_count, tok_count - NEWCAP), (0, 0)))
            return lax.dynamic_slice_in_dim(padded, shift, tok_count, 0)

        return keep, moved(scaled), moved(log_total)

    keep_r, scaled_r, log_r = place(got_right, right_start, right_len)
    keep_l, scaled_l, log_l = place(got_left, left_start, left_len)
    prior_scaled = jnp.where(
        keep_r, scaled_r, jnp.where(keep_l, scaled_l, jnp.zeros((), jnp.bfloat16))
    ).astype(jnp.float32)
    prior_top = jnp.where(keep_r, log_r, jnp.where(keep_l, log_l, floor_value))
    prior_total = jnp.where(keep_r | keep_l, 1.0, 0.0)

    both_top = jnp.maximum(own_top, prior_top)
    own_scale = jnp.exp(own_top - both_top)
    prior_scale = jnp.exp(prior_top - both_top)
    denominator = own_total * own_scale + prior_total * prior_scale
    lane_head = jnp.arange(feat_width, dtype=jnp.int32)[None, :] // HD

    def widened(per_head):
        full = jnp.zeros((tok_count, feat_width), jnp.float32)
        for h in range(head_count):
            full = jnp.where(lane_head == h, per_head[:, h : h + 1], full)
        return full

    numerator = own_numer * widened(own_scale) + prior_scaled * widened(prior_scale)
    attended = (numerator / widened(denominator)).astype(jnp.bfloat16)
    mixed = lax.psum_scatter(
        jnp.dot(attended, out_proj, preferred_element_type=jnp.float32).astype(jnp.bfloat16),
        "tp",
        scatter_dimension=0,
        tiled=True,
    )

    slot_ids = jnp.arange(slot_count, dtype=jnp.int32)
    def slot_id(bundle):
        return jnp.where(bundle[NEWCAP, 0] == 1, bundle[NEWCAP, 1], bundle[NEWCAP, 2]).astype(jnp.int32)

    left_slot_id = slot_id(from_left)
    right_slot_id = slot_id(from_right)

    def stored(from_left_rows, from_right_rows):
        at_left = (slot_ids == left_slot_id)[:, None, None]
        at_right = (slot_ids == right_slot_id)[:, None, None]
        return jnp.where(
            at_left,
            from_left_rows[None],
            jnp.where(at_right, from_right_rows[None], jnp.zeros((), jnp.bfloat16)),
        )

    new_keys = stored(from_left_kv[0], from_right_kv[0])
    new_values = stored(from_left_kv[1], from_right_kv[1])
    return (mixed, new_keys, new_values)


def solution(mesh):
    in_specs = (
        P("req", "tp"),
        P("req", "tp"),
        P("req", "tp"),
        P("req", None, "tp"),
        P("req", None, "tp"),
        P("tp", None),
        P("req", None),
        P("req", None),
        P("req", None),
        P("req", None),
    )
    out_specs = (P(("req", "tp"), None), P("req", None, "tp"), P("req", None, "tp"))
    return jax.shard_map(body, mesh=mesh, in_specs=in_specs, out_specs=out_specs, check_vma=False)
```

```python
import functools
import math

import jax
import jax.numpy as jnp
from jax import lax
from jax.experimental import pallas as pl
from jax.experimental.pallas import tpu as pltpu
from jax.sharding import PartitionSpec as P

HD = 224
NEWCAP = 192


floor_value = -1e30
TAG_ROWS = 8
RESULT_WIDTH = 1024


def shifted(value, axis, steps):
    count = lax.axis_size(axis)
    pairs = [(source, (source + steps) % count) for source in range(count)]
    return lax.ppermute(value, axis, pairs)


def attend_part(query_rows, key_rows, value_rows, live_mask, head_count):
    row_count = query_rows.shape[0]
    key_count = key_rows.shape[0]
    query_heads = query_rows.reshape(row_count, head_count, HD)
    key_heads = key_rows.reshape(key_count, head_count, HD)
    value_heads = value_rows.reshape(key_count, head_count, HD)
    scores = jnp.einsum(
        "thd,shd->hts", query_heads, key_heads, preferred_element_type=jnp.float32
    ) * (1.0 / math.sqrt(HD))
    scores = jnp.where(live_mask[None], scores, floor_value)
    row_top = jnp.max(scores, axis=2)
    weights = jnp.where(live_mask[None], jnp.exp(scores - row_top[:, :, None]), 0.0)
    row_total = jnp.sum(weights, axis=2)
    numerator = jnp.einsum(
        "hts,shd->thd",
        weights.astype(jnp.bfloat16),
        value_heads,
        preferred_element_type=jnp.float32,
    )
    return (numerator.reshape(row_count, head_count * HD), row_top.T, row_total.T)


def read_tag(bundle_ref):
    tag = bundle_ref[NEWCAP : NEWCAP + 1, :].astype(jnp.float32)
    lanes = lax.broadcasted_iota(jnp.int32, tag.shape, 1)

    def entry(i):
        return jnp.sum(jnp.where(lanes == i, tag, 0.0), axis=1, keepdims=True)

    first = entry(0) == 1.0
    slot = jnp.where(first, entry(1), entry(2))
    prior = jnp.where(first, entry(3) * 32 + entry(4), entry(5) * 32 + entry(6))
    return slot, prior


def prior_kernel(head_count, left_ref, right_ref, key_ref, value_ref, to_left_ref, to_right_ref, numer_ref):
    slot = pl.program_id(0)
    left_slot, left_prior = read_tag(left_ref)
    right_prior = read_tag(right_ref)[1]
    from_left = left_slot == slot.astype(jnp.float32)
    prior = jnp.where(from_left, left_prior, right_prior)
    row_count = NEWCAP
    feat_width = left_ref.shape[1]
    key_count = key_ref.shape[0]
    query_rows = jnp.where(from_left, left_ref[:NEWCAP, :], right_ref[:NEWCAP, :])
    live = lax.broadcasted_iota(jnp.int32, (1, key_count), 1).astype(jnp.float32) < prior
    result_width = to_left_ref.shape[1]
    tail_lanes = lax.broadcasted_iota(jnp.int32, (row_count, result_width - feat_width), 1)
    tail = jnp.zeros((row_count, result_width - feat_width), jnp.float32)
    numer_ref[...] = jnp.zeros((row_count, feat_width), jnp.float32)
    for h in range(head_count):
        low = (h * HD) // 128 * 128
        high = min(feat_width, -(-((h + 1) * HD) // 128) * 128)
        lanes = low + lax.broadcasted_iota(jnp.int32, (1, high - low), 1)
        in_head = (lanes >= h * HD) & (lanes < (h + 1) * HD)
        head_query = jnp.where(in_head, query_rows[:, low:high], jnp.zeros((), query_rows.dtype))
        scores = lax.dot_general(
            head_query, key_ref[:, low:high], (((1,), (1,)), ((), ())),
            preferred_element_type=jnp.float32,
        ) * (1.0 / math.sqrt(HD))
        scores = jnp.where(live, scores, floor_value)
        row_top = jnp.max(scores, axis=1, keepdims=True)
        weights = jnp.where(live, jnp.exp(scores - row_top), 0.0)
        row_total = jnp.sum(weights, axis=1, keepdims=True)
        head_out = jnp.dot(
            weights.astype(jnp.bfloat16), value_ref[:, low:high], preferred_element_type=jnp.float32
        )
        numer_ref[:, low:high] = numer_ref[:, low:high] + jnp.where(in_head, head_out / row_total, 0.0)
        log_total = row_top + jnp.log(row_total)
        for part in range(3):
            piece = log_total.astype(jnp.bfloat16).astype(jnp.float32)
            tail = jnp.where(tail_lanes == part * head_count + h, piece, tail)
            log_total = log_total - piece
    for side_ref, mine in ((to_left_ref, from_left), (to_right_ref, jnp.logical_not(from_left))):
        side_ref[:, :feat_width] = jnp.where(
            mine, numer_ref[...].astype(side_ref.dtype), side_ref[:, :feat_width]
        )
        side_ref[:, feat_width:] = jnp.where(
            mine, tail.astype(side_ref.dtype), side_ref[:, feat_width:]
        )


def serve_slots(from_left, from_right, cache_keys, cache_values, head_count):
    slot_count, key_count, feat_width = cache_keys.shape
    row_count = NEWCAP
    window_lanes = sum(
        min(feat_width, -(-((h + 1) * HD) // 128) * 128) - (h * HD) // 128 * 128
        for h in range(head_count)
    )
    flops = slot_count * 4 * row_count * key_count * window_lanes
    moved = (
        2 * (from_left.size + from_right.size + cache_keys.size + cache_values.size)
        + 2 * slot_count * row_count * RESULT_WIDTH
    )
    bundle_rows = from_left.shape[0]
    return pl.pallas_call(
        functools.partial(prior_kernel, head_count),
        out_shape=(
            jax.ShapeDtypeStruct((row_count, RESULT_WIDTH), jnp.bfloat16),
            jax.ShapeDtypeStruct((row_count, RESULT_WIDTH), jnp.bfloat16),
        ),
        grid=(slot_count,),
        in_specs=[
            pl.BlockSpec((bundle_rows, feat_width), lambda s: (0, 0)),
            pl.BlockSpec((bundle_rows, feat_width), lambda s: (0, 0)),
            pl.BlockSpec((None, key_count, feat_width), lambda s: (s, 0, 0)),
            pl.BlockSpec((None, key_count, feat_width), lambda s: (s, 0, 0)),
        ],
        out_specs=(
            pl.BlockSpec((row_count, RESULT_WIDTH), lambda s: (0, 0)),
            pl.BlockSpec((row_count, RESULT_WIDTH), lambda s: (0, 0)),
        ),
        scratch_shapes=[pltpu.VMEM((row_count, feat_width), jnp.float32)],
        cost_estimate=pl.CostEstimate(
            flops=flops,
            transcendentals=slot_count * head_count * row_count * key_count,
            bytes_accessed=moved,
        ),
    )(from_left, from_right, cache_keys, cache_values)


def own_kernel(head_count, query_ref, key_ref, value_ref, seg_col_ref, seg_row_ref, numer_ref, stats_ref):
    row_count, feat_width = query_ref.shape
    rows = lax.broadcasted_iota(jnp.int32, (row_count, row_count), 0)
    cols = lax.broadcasted_iota(jnp.int32, (row_count, row_count), 1)
    live = (seg_col_ref[...] == seg_row_ref[...]) & (cols <= rows)
    stat_lanes = lax.broadcasted_iota(jnp.int32, stats_ref.shape, 1)
    stats = jnp.zeros(stats_ref.shape, jnp.float32)
    numer_ref[...] = jnp.zeros((row_count, feat_width), jnp.float32)
    for h in range(head_count):
        low = (h * HD) // 128 * 128
        high = min(feat_width, -(-((h + 1) * HD) // 128) * 128)
        lanes = low + lax.broadcasted_iota(jnp.int32, (1, high - low), 1)
        in_head = (lanes >= h * HD) & (lanes < (h + 1) * HD)
        head_query = jnp.where(in_head, query_ref[:, low:high], jnp.zeros((), query_ref.dtype))
        scores = lax.dot_general(
            head_query, key_ref[:, low:high], (((1,), (1,)), ((), ())),
            preferred_element_type=jnp.float32,
        ) * (1.0 / math.sqrt(HD))
        scores = jnp.where(live, scores, floor_value)
        row_top = jnp.max(scores, axis=1, keepdims=True)
        weights = jnp.where(live, jnp.exp(scores - row_top), 0.0)
        row_total = jnp.sum(weights, axis=1, keepdims=True)
        head_out = jnp.dot(
            weights.astype(jnp.bfloat16), value_ref[:, low:high], preferred_element_type=jnp.float32
        )
        numer_ref[:, low:high] = numer_ref[:, low:high] + jnp.where(in_head, head_out, 0.0)
        stats = jnp.where(stat_lanes == h, row_top, stats)
        stats = jnp.where(stat_lanes == head_count + h, row_total, stats)
    stats_ref[...] = stats


def attend_own(queries, keys_new, values_new, segment, head_count):
    row_count, feat_width = queries.shape
    vmem = pl.BlockSpec(memory_space=pltpu.VMEM)
    numer, stats = pl.pallas_call(
        functools.partial(own_kernel, head_count),
        out_shape=(
            jax.ShapeDtypeStruct((row_count, feat_width), jnp.float32),
            jax.ShapeDtypeStruct((row_count, 128), jnp.float32),
        ),
        in_specs=[vmem] * 5,
        out_specs=(vmem, vmem),
        cost_estimate=pl.CostEstimate(
            flops=4 * row_count * row_count * 1280,
            transcendentals=head_count * row_count * row_count,
            bytes_accessed=6 * row_count * feat_width + 4 * row_count * (feat_width + 128),
        ),
    )(queries, keys_new, values_new, segment[:, None], segment[None, :])
    return numer, stats[:, :head_count], stats[:, head_count : 2 * head_count]


def body(
    queries,
    keys_new,
    values_new,
    cache_keys,
    cache_values,
    out_proj,
    req_lengths,
    cache_owner,
    cache_slot,
    prior_len,
):
    tok_count = queries.shape[0]
    feat_width = queries.shape[1]
    head_count = feat_width // HD
    slot_count = cache_keys.shape[0]
    prior_rows = cache_keys.shape[1]
    req_lens = req_lengths[0]
    req_ends = jnp.cumsum(req_lens)
    positions = jnp.arange(tok_count, dtype=jnp.int32)
    row_marks = jnp.arange(NEWCAP, dtype=jnp.int32)
    prior_marks = jnp.arange(prior_rows, dtype=jnp.int32)
    req_count = lax.axis_size("req")
    req_index = lax.axis_index("req")

    first_right = cache_owner[0, 0] == (req_index + 1) % req_count

    def request_at(distance):
        pick = first_right if distance == 1 else jnp.logical_not(first_right)
        start = jnp.where(pick, 0, req_lens[0])
        length = jnp.where(pick, req_lens[0], req_lens[1])
        slot = jnp.where(pick, cache_slot[0, 0], cache_slot[0, 1])
        prior = jnp.where(pick, prior_len[0, 0], prior_len[0, 1])
        return start, length, slot, prior

    def rows_of(source, start):
        return lax.dynamic_slice_in_dim(source, start, NEWCAP, 0)

    raw_tag = jnp.stack(
        [
            cache_slot[0, 0], cache_slot[0, 1],
            prior_len[0, 0] // 32, prior_len[0, 0] % 32,
            prior_len[0, 1] // 32, prior_len[0, 1] % 32,
        ]
    )

    def query_bundle(start, pick):
        tag = jnp.concatenate([pick.astype(jnp.int32)[None], raw_tag]).astype(jnp.bfloat16)
        tag_rows = jnp.zeros((TAG_ROWS, feat_width), jnp.bfloat16).at[0, : tag.shape[0]].set(tag)
        return jnp.concatenate([rows_of(queries, start), tag_rows], axis=0)

    right_start, right_len, right_slot, right_prior = request_at(1)
    left_start, left_len, left_slot, left_prior = request_at(-1)

    from_left = shifted(query_bundle(right_start, first_right), "req", 1)
    from_right = shifted(query_bundle(left_start, jnp.logical_not(first_right)), "req", -1)

    served = serve_slots(from_left, from_right, cache_keys, cache_values, head_count)
    segment = jnp.sum((positions[:, None] >= req_ends[None, :]).astype(jnp.int32), axis=1)
    own_numer, own_top, own_total = attend_own(queries, keys_new, values_new, segment, head_count)

    back_left, back_right = served
    got_right = shifted(back_left, "req", -1)
    got_left = shifted(back_right, "req", 1)

    def masked_rows(source, start, length):
        keep = (row_marks < length)[:, None]
        return jnp.where(keep, rows_of(source, start), jnp.zeros((), jnp.bfloat16))

    right_kv = jnp.stack(
        [masked_rows(keys_new, right_start, right_len), masked_rows(values_new, right_start, right_len)]
    )
    left_kv = jnp.stack(
        [masked_rows(keys_new, left_start, left_len), masked_rows(values_new, left_start, left_len)]
    )
    right_kv, left_kv, got_right, got_left = lax.optimization_barrier(
        (right_kv, left_kv, got_right, got_left)
    )
    from_left_kv = shifted(right_kv, "req", 1)
    from_right_kv = shifted(left_kv, "req", -1)

    def split_result(result):
        scaled = result[:, :feat_width]
        parts = result[:, feat_width : feat_width + 3 * head_count].astype(jnp.float32)
        log_total = (
            parts[:, :head_count]
            + parts[:, head_count : 2 * head_count]
            + parts[:, 2 * head_count : 3 * head_count]
        )
        return scaled, log_total

    got_right = split_result(got_right)
    got_left = split_result(got_left)

    def place(result, start, length):
        scaled, log_total = result
        shift = tok_count - start
        keep = ((positions - start >= 0) & (positions - start < length))[:, None]

        def moved(x):
            padded = jnp.pad(x, ((tok_count, tok_count - NEWCAP), (0, 0)))
            return lax.dynamic_slice_in_dim(padded, shift, tok_count, 0)

        return keep, moved(scaled), moved(log_total)

    keep_r, scaled_r, log_r = place(got_right, right_start, right_len)
    keep_l, scaled_l, log_l = place(got_left, left_start, left_len)
    prior_scaled = jnp.where(
        keep_r, scaled_r, jnp.where(keep_l, scaled_l, jnp.zeros((), jnp.bfloat16))
    ).astype(jnp.float32)
    prior_top = jnp.where(keep_r, log_r, jnp.where(keep_l, log_l, floor_value))
    prior_total = jnp.where(keep_r | keep_l, 1.0, 0.0)

    both_top = jnp.maximum(own_top, prior_top)
    own_scale = jnp.exp(own_top - both_top)
    prior_scale = jnp.exp(prior_top - both_top)
    denominator = own_total * own_scale + prior_total * prior_scale
    lane_head = jnp.arange(feat_width, dtype=jnp.int32)[None, :] // HD

    def widened(per_head):
        full = jnp.zeros((tok_count, feat_width), jnp.float32)
        for h in range(head_count):
            full = jnp.where(lane_head == h, per_head[:, h : h + 1], full)
        return full

    numerator = own_numer * widened(own_scale) + prior_scaled * widened(prior_scale)
    attended = (numerator / widened(denominator)).astype(jnp.bfloat16)
    head_rows = 2 * NEWCAP
    late_attended = (
        own_numer[head_rows:] / widened(own_total)[head_rows:]
    ).astype(jnp.bfloat16)
    mixed = lax.psum_scatter(
        jnp.concatenate(
            [
                jnp.dot(attended[:head_rows], out_proj, preferred_element_type=jnp.float32),
                jnp.dot(late_attended, out_proj, preferred_element_type=jnp.float32),
            ],
            axis=0,
        ).astype(jnp.bfloat16),
        "tp",
        scatter_dimension=0,
        tiled=True,
    )

    slot_ids = jnp.arange(slot_count, dtype=jnp.int32)
    def slot_id(bundle):
        return jnp.where(bundle[NEWCAP, 0] == 1, bundle[NEWCAP, 1], bundle[NEWCAP, 2]).astype(jnp.int32)

    left_slot_id = slot_id(from_left)
    right_slot_id = slot_id(from_right)

    def stored(from_left_rows, from_right_rows):
        at_left = (slot_ids == left_slot_id)[:, None, None]
        at_right = (slot_ids == right_slot_id)[:, None, None]
        return jnp.where(
            at_left,
            from_left_rows[None],
            jnp.where(at_right, from_right_rows[None], jnp.zeros((), jnp.bfloat16)),
        )

    new_keys = stored(from_left_kv[0], from_right_kv[0])
    new_values = stored(from_left_kv[1], from_right_kv[1])
    return (mixed, new_keys, new_values)


def solution(mesh):
    in_specs = (
        P("req", "tp"),
        P("req", "tp"),
        P("req", "tp"),
        P("req", None, "tp"),
        P("req", None, "tp"),
        P("tp", None),
        P("req", None),
        P("req", None),
        P("req", None),
        P("req", None),
    )
    out_specs = (P(("req", "tp"), None), P("req", None, "tp"), P("req", None, "tp"))
    return jax.shard_map(body, mesh=mesh, in_specs=in_specs, out_specs=out_specs, check_vma=False)
```
